32 devices in a mesh: dp: 4 (over y, core), mp: 8 (over z, x).
Axes of the slice: x: 2, y: 2, z: 4, core: 2. Of those that a mesh axis runs over, the one named last changes fastest.
Arguments:
- tokens: bfloat16 [512, 6144], P('dp', 'mp'), may hold values from -6 to 6
- norm_gain: bfloat16 [6144], P('mp'), may hold values from 0.5 to 1.5
- qkv_weight: bfloat16 [3, 128, 24, 6144], P(None, 'mp', None, 'dp'), may hold values from -0.078125 to 0.078125
- head_weight: bfloat16 [128, 24, 6144], P('mp', None, 'dp'), may hold values from -0.109375 to 0.109375
- up_weight: bfloat16 [12288, 6144], P('mp', 'dp'), may hold values from -0.078125 to 0.078125
- down_weight: bfloat16 [12288, 6144], P('mp', 'dp'), may hold values from -0.0546875 to 0.0546875
- cotangent: bfloat16 [512, 6144], P('dp', 'mp'), may hold values from -6 to 6
Outputs:
- mixed: bfloat16 [512, 6144], P('dp', 'mp')
- tokens_grad: float32 [512, 6144], P('dp', 'mp')
- qkv_grad: bfloat16 [3, 128, 24, 6144], P(None, 'mp', None, 'dp')
- head_grad: bfloat16 [128, 24, 6144], P('mp', None, 'dp')
- up_grad: bfloat16 [12288, 6144], P('mp', 'dp')
- down_grad: bfloat16 [12288, 6144], P('mp', 'dp')
- gain_grad: float32 [6144], P('mp')
The draws below stay inside these ranges and needn't reach their ends.
All inputs are finite; a program needn't handle non-finite values.
Results may differ from the reference program's by a relative error of at most 0.013.
Values may be sent and summed in bfloat16 or wider, within the bound.
No kernel may reach another device: no remote copies, remote signals or barrier semaphores. Data moves between devices by JAX's collectives and lax.ppermute only.
A program may use at most 256 MiB of HBM per device.

```python
import math
import jax
import jax.numpy as jnp
from jax import lax

D = 6144
FF = 12288
HEADS = 24
HS = 128
PATCHES = 128
QB = 8
IMG_DP = 1
ROWS = 128
TQ = 16
ITEMS = 192
TOKENS = 512
N_DP = 4


def levels(own_key, extent, pieces, smallest, high):
    def one(axis_at, blocks):
        steps = jax.random.uniform(jax.random.fold_in(jax.random.fold_in(own_key, 6), axis_at), (blocks,), jnp.float32, smallest / len(pieces), high / len(pieces))
        return jnp.repeat(jnp.exp(steps), extent[axis_at] // blocks).reshape((-1,) + (1,) * (len(extent) - axis_at - 1))

    level = one(*pieces[0])
    for cut in pieces[1:]:
        level = level * one(*cut)
    return level


def scatter_about(own_key, extent, deviation, most, cuts=(), kind=jnp.bfloat16):
    array = jax.random.normal(own_key, extent, jnp.float32) * deviation
    if len(cuts) > 0:
        array = levels(own_key, extent, cuts, -0.22, 0.18) * array
    return jnp.clip(array, min=-most, max=most).astype(kind)


def setup_inputs(seed: int = 0) -> dict:
    streams_of = jax.random.split(jax.random.key(seed), 8)
    return {
        "tokens": scatter_about(streams_of[0], (TOKENS, D), 1.0, 6.0, ((0, 4), (1, 8))),
        "norm_gain": jnp.clip(1.0 + 0.1 * jax.random.normal(streams_of[1], (D,), jnp.float32), 0.5, 1.5).astype(jnp.bfloat16),
        "qkv_weight": scatter_about(streams_of[2], (3, HS, HEADS, D), D ** -0.5, 0.078125, ((1, 8), (3, 4))),
        "head_weight": scatter_about(streams_of[3], (HS, HEADS, D), (HS * HEADS) ** -0.5, 0.109375, ((0, 8), (2, 4))),
        "up_weight": scatter_about(streams_of[4], (FF, D), D ** -0.5, 0.078125, ((0, 8), (1, 4))),
        "down_weight": scatter_about(streams_of[5], (FF, D), FF ** -0.5, 0.0546875, ((0, 8), (1, 4))),
        "cotangent": scatter_about(streams_of[6], (TOKENS, D), 1.0, 6.0, ((0, 4), (1, 8))),
    }


epsilon = 1e-06

def gelu_pair(inputs):
    normal_cdf = 0.5 * (1.0 + jax.scipy.special.erf(inputs * 0.7071067811865476))
    density = jnp.exp(-0.5 * inputs * inputs) * 0.3989422804014327
    return (inputs * normal_cdf, normal_cdf + inputs * density)

def head_norm(values):
    center = values - lax.optimization_barrier(jnp.mean(values, axis=0, keepdims=True))
    inverse = lax.rsqrt(lax.optimization_barrier(jnp.mean(center * center, axis=0, keepdims=True)) + epsilon)
    return (center * inverse, inverse)

def norm_back(upstream, normed, inverse):
    return inverse * (upstream - lax.optimization_barrier(jnp.mean(upstream, axis=0, keepdims=True)) - normed * lax.optimization_barrier(jnp.mean(upstream * normed, axis=0, keepdims=True)))

def to_items(pair_rows):
    depth = pair_rows.shape[1]
    shaped = pair_rows.reshape(2, depth, HEADS, IMG_DP, 1, PATCHES)
    spread = jnp.broadcast_to(shaped, (2, depth, HEADS, IMG_DP, QB, PATCHES))
    return jnp.transpose(spread, (1, 2, 3, 4, 0, 5)).reshape(depth, HEADS * IMG_DP * QB, 2, PATCHES)

def from_items(pair_items):
    depth = pair_items.shape[0]
    shaped = pair_items.reshape(depth, HEADS, IMG_DP, QB, 2, PATCHES)
    summed = lax.optimization_barrier(jnp.sum(shaped.astype(jnp.float32), axis=3)).astype(jnp.bfloat16)
    return jnp.transpose(summed, (3, 0, 1, 2, 4)).reshape(2, depth, HEADS, IMG_DP * PATCHES)

def attend(queries, keyvals):
    query_hat, query_scale = head_norm(queries.astype(jnp.float32))
    key_hat, key_scale = head_norm(keyvals[:, :, 0].astype(jnp.float32))
    query_norm = query_hat.astype(jnp.bfloat16)
    key_norm = key_hat.astype(jnp.bfloat16)
    factor = 1.0 / math.sqrt(queries.shape[0])
    scores = jnp.einsum('cia,cib->iab', query_norm.astype(jnp.float32), key_norm.astype(jnp.float32)) * factor
    raised = jnp.exp(scores)
    shares = raised / lax.optimization_barrier(jnp.sum(raised, axis=2, keepdims=True))
    rounded = shares.astype(jnp.bfloat16)
    values = keyvals[:, :, 1]
    attended = jnp.einsum('iab,cib->cia', rounded.astype(jnp.float32), values.astype(jnp.float32)).astype(jnp.bfloat16)
    stored = (query_hat, query_scale, key_hat, key_scale, query_norm, key_norm, shares, rounded, values)
    return (attended, stored)

def attend_back(upstream, stored):
    query_hat, query_scale, key_hat, key_scale, query_norm, key_norm, shares, rounded, values = stored
    factor = 1.0 / math.sqrt(upstream.shape[0])
    wide_up = upstream.astype(jnp.float32)
    share_grad = jnp.einsum('cia,cib->iab', wide_up, values.astype(jnp.float32))
    value_grad = jnp.einsum('iab,cia->cib', rounded.astype(jnp.float32), wide_up)
    score_grad = (shares * (share_grad - lax.optimization_barrier(jnp.sum(shares * share_grad, axis=2, keepdims=True))) * factor).astype(jnp.bfloat16)
    query_back = jnp.einsum('iab,cib->cia', score_grad.astype(jnp.float32), key_norm.astype(jnp.float32))
    key_back = jnp.einsum('iab,cia->cib', score_grad.astype(jnp.float32), query_norm.astype(jnp.float32))
    query_grad = norm_back(query_back, query_hat, query_scale).astype(jnp.bfloat16)
    key_grad = norm_back(key_back, key_hat, key_scale).astype(jnp.bfloat16)
    pair_grad = jnp.stack([key_grad, value_grad.astype(jnp.bfloat16)], axis=2)
    return (query_grad, pair_grad)

def reference(tokens, norm_gain, qkv_weight, head_weight, up_weight, down_weight, cotangent):
    qkv_flat = qkv_weight.reshape(3 * HS * HEADS, D)
    head_flat = head_weight.reshape(HS * HEADS, D)
    gain_wide = norm_gain.astype(jnp.float32)
    qkv_total = jnp.zeros((3 * HS * HEADS, D), jnp.float32)
    head_total = jnp.zeros((HS * HEADS, D), jnp.float32)
    up_total = jnp.zeros((FF, D), jnp.float32)
    down_total = jnp.zeros((FF, D), jnp.float32)
    gain_total = jnp.zeros((D,), jnp.float32)
    mixed_parts = []
    grad_parts = []
    for which_group in range(N_DP):
        rows_in = tokens[which_group * ROWS:(which_group + 1) * ROWS]
        cotangent_rows = cotangent[which_group * ROWS:(which_group + 1) * ROWS]
        widened = rows_in.astype(jnp.float32)
        center = widened - lax.optimization_barrier(jnp.mean(widened, axis=1, keepdims=True))
        row_scale = lax.rsqrt(lax.optimization_barrier(jnp.mean(center * center, axis=1, keepdims=True)) + epsilon)
        normed = center * row_scale
        hidden_in = (normed * gain_wide).astype(jnp.bfloat16)
        projected = jnp.dot(qkv_flat, hidden_in.T, preferred_element_type=jnp.float32).astype(jnp.bfloat16)
        projected = projected.reshape(3, HS, HEADS, ROWS)
        queries = projected[0].reshape(HS, ITEMS, TQ)
        keyvals = to_items(projected[1:])
        attended, stored = attend(queries, keyvals)
        head_rows = attended.reshape(HS * HEADS, ROWS)
        up_input = jnp.dot(up_weight, hidden_in.T, preferred_element_type=jnp.float32)
        activated, gelu_slope = gelu_pair(up_input)
        up_output = activated.astype(jnp.bfloat16)
        branch = jnp.dot(head_rows.T, head_flat, preferred_element_type=jnp.float32) + jnp.dot(up_output.T, down_weight, preferred_element_type=jnp.float32)
        mixed_parts.append((widened + branch).astype(jnp.bfloat16))
        down_total = down_total + jnp.dot(up_output, cotangent_rows, preferred_element_type=jnp.float32).astype(jnp.bfloat16).astype(jnp.float32)
        head_total = head_total + jnp.dot(head_rows, cotangent_rows, preferred_element_type=jnp.float32).astype(jnp.bfloat16).astype(jnp.float32)
        up_upstream = (jnp.dot(down_weight, cotangent_rows.T, preferred_element_type=jnp.float32) * gelu_slope).astype(jnp.bfloat16)
        head_upstream = jnp.dot(head_flat, cotangent_rows.T, preferred_element_type=jnp.float32).astype(jnp.bfloat16)
        query_grad, pair_grad = attend_back(head_upstream.reshape(HS, ITEMS, TQ), stored)
        proj_grad = jnp.concatenate([query_grad.reshape(1, HS, HEADS, ROWS), from_items(pair_grad)], axis=0)
        proj_grad = proj_grad.reshape(3 * HS * HEADS, ROWS)
        qkv_total = qkv_total + jnp.dot(proj_grad, hidden_in, preferred_element_type=jnp.float32).astype(jnp.bfloat16).astype(jnp.float32)
        up_total = up_total + jnp.dot(up_upstream, hidden_in, preferred_element_type=jnp.float32).astype(jnp.bfloat16).astype(jnp.float32)
        input_grad = jnp.dot(proj_grad.T, qkv_flat, preferred_element_type=jnp.float32) + jnp.dot(up_upstream.T, up_weight, preferred_element_type=jnp.float32)
        scaled = input_grad * gain_wide
        grad_rows = row_scale * (scaled - lax.optimization_barrier(jnp.mean(scaled, axis=1, keepdims=True)) - normed * lax.optimization_barrier(jnp.mean(scaled * normed, axis=1, keepdims=True)))
        grad_parts.append(grad_rows + cotangent_rows.astype(jnp.float32))
        gain_total = gain_total + lax.optimization_barrier(jnp.sum(input_grad * normed, axis=0))
    mixed = jnp.concatenate(mixed_parts, axis=0)
    tokens_grad = jnp.concatenate(grad_parts, axis=0)
    qkv_grad = qkv_total.astype(jnp.bfloat16).reshape(3, HS, HEADS, D)
    head_grad = head_total.astype(jnp.bfloat16).reshape(HS, HEADS, D)
    return (mixed, tokens_grad, qkv_grad, head_grad, up_total.astype(jnp.bfloat16), down_total.astype(jnp.bfloat16), gain_total)
```

```python
import math

import jax
import jax.numpy as jnp
from jax import lax
from jax.sharding import PartitionSpec as P

D = 6144
HEADS = 24
HS = 128
PATCHES = 128
QB = 8
IMG_DP = 1
ROWS = 128
TQ = 16
ITEMS = 192


epsilon = 1e-06
contract_rows = (((0,), (0,)), ((), ()))
contract_cols = (((1,), (1,)), ((), ()))


def gelu_pair(inputs):
    normal_cdf = 0.5 * (1.0 + jax.scipy.special.erf(inputs * 0.7071067811865476))
    density = jnp.exp(-0.5 * inputs * inputs) * 0.3989422804014327
    return (inputs * normal_cdf, normal_cdf + inputs * density)


def head_norm(values):
    center = values - jnp.mean(values, axis=0, keepdims=True)
    inverse = lax.rsqrt(jnp.mean(center * center, axis=0, keepdims=True) + epsilon)
    return (center * inverse, inverse)


def norm_back(upstream, normed, inverse):
    return inverse * (
        upstream
        - jnp.mean(upstream, axis=0, keepdims=True)
        - normed * jnp.mean(upstream * normed, axis=0, keepdims=True)
    )


def to_items(pair_rows):
    depth = pair_rows.shape[1]
    shaped = pair_rows.reshape(2, depth, HEADS, IMG_DP, 1, PATCHES)
    spread = jnp.broadcast_to(shaped, (2, depth, HEADS, IMG_DP, QB, PATCHES))
    return jnp.transpose(spread, (1, 2, 3, 4, 0, 5)).reshape(depth, HEADS * IMG_DP * QB, 2, PATCHES)


def from_items(pair_items):
    depth = pair_items.shape[0]
    shaped = pair_items.reshape(depth, HEADS, IMG_DP, QB, 2, PATCHES)
    summed = jnp.sum(shaped.astype(jnp.float32), axis=3).astype(jnp.bfloat16)
    return jnp.transpose(summed, (3, 0, 1, 2, 4)).reshape(2, depth, HEADS, IMG_DP * PATCHES)


def attend(queries, keyvals):
    query_hat, query_scale = head_norm(queries.astype(jnp.float32))
    key_hat, key_scale = head_norm(keyvals[:, :, 0].astype(jnp.float32))
    query_norm = query_hat.astype(jnp.bfloat16)
    key_norm = key_hat.astype(jnp.bfloat16)
    factor = 1.0 / math.sqrt(queries.shape[0])
    scores = (
        jnp.einsum("cia,cib->iab", query_norm, key_norm, preferred_element_type=jnp.float32)
        * factor
    )
    raised = jnp.exp(scores)
    shares = raised / jnp.sum(raised, axis=2, keepdims=True)
    rounded = shares.astype(jnp.bfloat16)
    values = keyvals[:, :, 1]
    attended = jnp.einsum(
        "iab,cib->cia", rounded, values, preferred_element_type=jnp.float32
    ).astype(jnp.bfloat16)
    stored = (
        query_hat,
        query_scale,
        key_hat,
        key_scale,
        query_norm,
        key_norm,
        shares,
        rounded,
        values,
    )
    return (attended, stored)


def attend_back(upstream, stored):
    query_hat, query_scale, key_hat, key_scale, query_norm, key_norm, shares, rounded, values = (
        stored
    )
    factor = 1.0 / math.sqrt(upstream.shape[0])
    share_grad = jnp.einsum("cia,cib->iab", upstream, values, preferred_element_type=jnp.float32)
    value_grad = jnp.einsum("iab,cia->cib", rounded, upstream, preferred_element_type=jnp.float32)
    score_grad = (
        shares * (share_grad - jnp.sum(shares * share_grad, axis=2, keepdims=True)) * factor
    ).astype(jnp.bfloat16)
    query_back = jnp.einsum(
        "iab,cib->cia", score_grad, key_norm, preferred_element_type=jnp.float32
    )
    key_back = jnp.einsum(
        "iab,cia->cib", score_grad, query_norm, preferred_element_type=jnp.float32
    )
    query_grad = norm_back(query_back, query_hat, query_scale).astype(jnp.bfloat16)
    key_grad = norm_back(key_back, key_hat, key_scale).astype(jnp.bfloat16)
    pair_grad = jnp.stack([key_grad, value_grad.astype(jnp.bfloat16)], axis=2)
    return (query_grad, pair_grad)


def swap_pairs(n_dp, n_mp):
    ratio = n_mp // n_dp
    pairs = []
    for row in range(n_dp):
        for col in range(n_mp):
            owner, part = divmod(col, ratio)
            pairs.append((row * n_mp + col, owner * n_mp + row * ratio + part))
    return pairs


def swap(block):
    n_dp, n_mp = lax.axis_size("dp"), lax.axis_size("mp")
    return lax.ppermute(block, ("dp", "mp"), swap_pairs(n_dp, n_mp))


def spread_quarter(block):
    n_dp, n_mp = lax.axis_size("dp"), lax.axis_size("mp")
    ratio = n_mp // n_dp
    rows, width = block.shape
    pieces = lax.all_gather(swap(block), "mp", axis=0, tiled=False)
    pieces = pieces.reshape(n_dp, ratio, rows, width)
    return jnp.transpose(pieces, (0, 2, 1, 3)).reshape(n_dp * rows, ratio * width)


def gather_quarter(partial, rows):
    n_dp, n_mp = lax.axis_size("dp"), lax.axis_size("mp")
    ratio = n_mp // n_dp
    width = partial.shape[1] // ratio
    pieces = partial.reshape(n_dp, rows, ratio, width)
    pieces = jnp.transpose(pieces, (0, 2, 1, 3)).reshape(n_mp, rows, width)
    summed = lax.psum_scatter(pieces, "mp", scatter_dimension=0, tiled=True)
    return swap(summed.reshape(rows, width))


def blockwise_grad(left, right, n_blocks):
    rows = left.shape[1] // n_blocks
    total = None
    for block in range(n_blocks):
        piece = jnp.dot(
            left[:, block * rows:(block + 1) * rows],
            right[block * rows:(block + 1) * rows],
            preferred_element_type=jnp.float32,
        ).astype(jnp.bfloat16).astype(jnp.float32)
        total = piece if total is None else total + piece
    return total.astype(jnp.bfloat16)


def shards(tokens, norm_gain, qkv_weight, head_weight, up_weight, down_weight, cotangent):
    n_dp, n_mp = lax.axis_size("dp"), lax.axis_size("mp")
    head_slice = HS // n_mp
    quarter = qkv_weight.shape[-1]
    rows, width = tokens.shape
    qkv_flat = qkv_weight.reshape(-1, quarter)
    head_flat = head_weight.reshape(-1, quarter)

    widened = tokens.astype(jnp.float32)
    block_mean = jnp.mean(widened, axis=1)
    block_center = widened - block_mean[:, None]
    block_m2 = jnp.sum(block_center * block_center, axis=1)
    stats = lax.all_gather(jnp.stack([block_mean, block_m2]), "mp", axis=0, tiled=False)
    row_mean = jnp.mean(stats[:, 0], axis=0)
    spread = stats[:, 0] - row_mean[None, :]
    row_m2 = jnp.sum(stats[:, 1], axis=0) + width * jnp.sum(spread * spread, axis=0)
    row_scale = lax.rsqrt(row_m2 / D + epsilon)[:, None]
    normed = (widened - row_mean[:, None]) * row_scale
    gain_wide = norm_gain.astype(jnp.float32)
    hidden_local = (normed * gain_wide).astype(jnp.bfloat16)
    hidden_all = spread_quarter(hidden_local)
    cot_all = spread_quarter(cotangent)

    projected = lax.dot_general(
        qkv_flat, hidden_all, contract_cols, preferred_element_type=jnp.float32
    )
    projected = lax.psum_scatter(projected, "dp", scatter_dimension=1, tiled=True)
    projected = projected.astype(jnp.bfloat16).reshape(3, head_slice, HEADS, ROWS)
    up_input = lax.dot_general(
        up_weight, hidden_all, contract_cols, preferred_element_type=jnp.float32
    )
    up_input = lax.psum_scatter(up_input, "dp", scatter_dimension=1, tiled=True)
    activated, gelu_slope = gelu_pair(up_input)
    up_output = activated.astype(jnp.bfloat16)

    queries = projected[0].reshape(head_slice, ITEMS, TQ)
    keyvals = to_items(projected[1:])
    query_heads, pair_heads = (
        lax.all_to_all(queries, "mp", split_axis=1, concat_axis=0, tiled=True),
        lax.all_to_all(keyvals, "mp", split_axis=1, concat_axis=0, tiled=True),
    )
    attended, stored = attend(query_heads, pair_heads)
    head_rows = lax.all_to_all(attended, "mp", split_axis=0, concat_axis=1, tiled=True).reshape(
        head_slice * HEADS, ROWS
    )
    head_rows_all = lax.all_gather(head_rows, "dp", axis=1, tiled=True)
    up_output_all = lax.all_gather(up_output, "dp", axis=1, tiled=True)
    branch = lax.dot_general(
        head_rows_all, head_flat, contract_rows, preferred_element_type=jnp.float32
    ) + lax.dot_general(up_output_all, down_weight, contract_rows, preferred_element_type=jnp.float32)
    branch_local = gather_quarter(branch, rows)
    mixed = (widened + branch_local).astype(jnp.bfloat16)

    down_grad = blockwise_grad(up_output_all, cot_all, n_dp)
    head_grad = blockwise_grad(head_rows_all, cot_all, n_dp)
    up_back = lax.dot_general(
        down_weight, cot_all, contract_cols, preferred_element_type=jnp.float32
    )
    up_back = lax.psum_scatter(up_back, "dp", scatter_dimension=1, tiled=True)
    up_upstream = (up_back * gelu_slope).astype(jnp.bfloat16)
    head_upstream = lax.dot_general(
        head_flat, cot_all, contract_cols, preferred_element_type=jnp.float32
    )
    head_upstream = lax.psum_scatter(head_upstream, "dp", scatter_dimension=1, tiled=True)
    head_upstream = head_upstream.astype(jnp.bfloat16).reshape(head_slice, ITEMS, TQ)
    upstream = lax.all_to_all(head_upstream, "mp", split_axis=1, concat_axis=0, tiled=True)
    query_grad, pair_grad = attend_back(upstream, stored)
    query_local, pair_local = (
        lax.all_to_all(query_grad, "mp", split_axis=0, concat_axis=1, tiled=True),
        lax.all_to_all(pair_grad, "mp", split_axis=0, concat_axis=1, tiled=True),
    )
    proj_grad = jnp.concatenate(
        [query_local.reshape(1, head_slice, HEADS, ROWS), from_items(pair_local)], axis=0
    )
    proj_grad = proj_grad.reshape(3 * head_slice * HEADS, ROWS)
    proj_grad_all = lax.all_gather(proj_grad, "dp", axis=1, tiled=True)
    up_upstream_all = lax.all_gather(up_upstream, "dp", axis=1, tiled=True)
    qkv_grad = blockwise_grad(proj_grad_all, hidden_all, n_dp)
    up_grad = blockwise_grad(up_upstream_all, hidden_all, n_dp)
    input_partial = lax.dot_general(
        proj_grad_all, qkv_flat, contract_rows, preferred_element_type=jnp.float32
    ) + lax.dot_general(up_upstream_all, up_weight, contract_rows, preferred_element_type=jnp.float32)
    input_local = gather_quarter(input_partial, rows)

    scaled = input_local * gain_wide
    plain_sum, cross_sum = lax.psum(
        (jnp.sum(scaled, axis=1), jnp.sum(scaled * normed, axis=1)), "mp"
    )
    tokens_grad = row_scale * (
        scaled - plain_sum[:, None] / D - normed * (cross_sum[:, None] / D)
    )
    tokens_grad = tokens_grad + cotangent.astype(jnp.float32)
    gain_piece = jnp.sum(input_local * normed, axis=0)
    gain_grad = lax.psum(gain_piece, "dp")
    return (
        mixed,
        tokens_grad,
        qkv_grad.reshape(qkv_weight.shape),
        head_grad.reshape(head_weight.shape),
        up_grad,
        down_grad,
        gain_grad,
    )


def solution(mesh):
    in_specs = (
        P("dp", "mp"),
        P("mp"),
        P(None, "mp", None, "dp"),
        P("mp", None, "dp"),
        P("mp", "dp"),
        P("mp", "dp"),
        P("dp", "mp"),
    )
    out_specs = (
        P("dp", "mp"),
        P("dp", "mp"),
        P(None, "mp", None, "dp"),
        P("mp", None, "dp"),
        P("mp", "dp"),
        P("mp", "dp"),
        P("mp"),
    )
    return jax.shard_map(shards, mesh=mesh, in_specs=in_specs, out_specs=out_specs, check_vma=False)
```

```python
import math

import jax
import jax.numpy as jnp
from jax import lax
from jax.sharding import PartitionSpec as P

D = 6144
HEADS = 24
HS = 128
PATCHES = 128
QB = 8
IMG_DP = 1
ROWS = 128
TQ = 16
ITEMS = 192


epsilon = 1e-06
contract_rows = (((0,), (0,)), ((), ()))
contract_cols = (((1,), (1,)), ((), ()))


def gelu_pair(inputs):
    normal_cdf = 0.5 * (1.0 + jax.scipy.special.erf(inputs * 0.7071067811865476))
    density = jnp.exp(-0.5 * inputs * inputs) * 0.3989422804014327
    return (inputs * normal_cdf, normal_cdf + inputs * density)


def head_norm(values):
    center = values - jnp.mean(values, axis=0, keepdims=True)
    inverse = lax.rsqrt(jnp.mean(center * center, axis=0, keepdims=True) + epsilon)
    return (center * inverse, inverse)


def norm_back(upstream, normed, inverse):
    return inverse * (
        upstream
        - jnp.mean(upstream, axis=0, keepdims=True)
        - normed * jnp.mean(upstream * normed, axis=0, keepdims=True)
    )


def to_items(pair_rows):
    depth = pair_rows.shape[1]
    shaped = pair_rows.reshape(2, depth, HEADS, IMG_DP, 1, PATCHES)
    spread = jnp.broadcast_to(shaped, (2, depth, HEADS, IMG_DP, QB, PATCHES))
    return jnp.transpose(spread, (1, 2, 3, 4, 0, 5)).reshape(depth, HEADS * IMG_DP * QB, 2, PATCHES)


def from_items(pair_items):
    depth = pair_items.shape[0]
    shaped = pair_items.reshape(depth, HEADS, IMG_DP, QB, 2, PATCHES)
    summed = jnp.sum(shaped.astype(jnp.float32), axis=3).astype(jnp.bfloat16)
    return jnp.transpose(summed, (3, 0, 1, 2, 4)).reshape(2, depth, HEADS, IMG_DP * PATCHES)


def attend(queries, keyvals):
    query_hat, query_scale = head_norm(queries.astype(jnp.float32))
    key_hat, key_scale = head_norm(keyvals[:, :, 0].astype(jnp.float32))
    query_norm = query_hat.astype(jnp.bfloat16)
    key_norm = key_hat.astype(jnp.bfloat16)
    factor = 1.0 / math.sqrt(queries.shape[0])
    scores = (
        jnp.einsum("cia,cib->iab", query_norm, key_norm, preferred_element_type=jnp.float32)
        * factor
    )
    raised = jnp.exp(scores)
    shares = raised / jnp.sum(raised, axis=2, keepdims=True)
    rounded = shares.astype(jnp.bfloat16)
    values = keyvals[:, :, 1]
    attended = jnp.einsum(
        "iab,cib->cia", rounded, values, preferred_element_type=jnp.float32
    ).astype(jnp.bfloat16)
    stored = (
        query_hat,
        query_scale,
        key_hat,
        key_scale,
        query_norm,
        key_norm,
        shares,
        rounded,
        values,
    )
    return (attended, stored)


def attend_back(upstream, stored):
    query_hat, query_scale, key_hat, key_scale, query_norm, key_norm, shares, rounded, values = (
        stored
    )
    factor = 1.0 / math.sqrt(upstream.shape[0])
    share_grad = jnp.einsum("cia,cib->iab", upstream, values, preferred_element_type=jnp.float32)
    value_grad = jnp.einsum("iab,cia->cib", rounded, upstream, preferred_element_type=jnp.float32)
    score_grad = (
        shares * (share_grad - jnp.sum(shares * share_grad, axis=2, keepdims=True)) * factor
    ).astype(jnp.bfloat16)
    query_back = jnp.einsum(
        "iab,cib->cia", score_grad, key_norm, preferred_element_type=jnp.float32
    )
    key_back = jnp.einsum(
        "iab,cia->cib", score_grad, query_norm, preferred_element_type=jnp.float32
    )
    query_grad = norm_back(query_back, query_hat, query_scale).astype(jnp.bfloat16)
    key_grad = norm_back(key_back, key_hat, key_scale).astype(jnp.bfloat16)
    pair_grad = jnp.stack([key_grad, value_grad.astype(jnp.bfloat16)], axis=2)
    return (query_grad, pair_grad)


def swap_pairs(n_dp, n_mp):
    ratio = n_mp // n_dp
    pairs = []
    for row in range(n_dp):
        for col in range(n_mp):
            owner, part = divmod(col, ratio)
            pairs.append((row * n_mp + col, owner * n_mp + row * ratio + part))
    return pairs


def swap(block):
    n_dp, n_mp = lax.axis_size("dp"), lax.axis_size("mp")
    return lax.ppermute(block, ("dp", "mp"), swap_pairs(n_dp, n_mp))


def spread_quarter(block):
    n_dp, n_mp = lax.axis_size("dp"), lax.axis_size("mp")
    ratio = n_mp // n_dp
    rows, width = block.shape
    pieces = lax.all_gather(swap(block), "mp", axis=0, tiled=False)
    pieces = pieces.reshape(n_dp, ratio, rows, width)
    return jnp.transpose(pieces, (0, 2, 1, 3)).reshape(n_dp * rows, ratio * width)


def gather_quarter(partial, rows):
    n_dp, n_mp = lax.axis_size("dp"), lax.axis_size("mp")
    ratio = n_mp // n_dp
    width = partial.shape[1] // ratio
    pieces = partial.reshape(n_dp, rows, ratio, width)
    pieces = jnp.transpose(pieces, (0, 2, 1, 3)).reshape(n_mp, rows, width)
    summed = lax.psum_scatter(pieces, "mp", scatter_dimension=0, tiled=True)
    return swap(summed.reshape(rows, width))


def blockwise_grad(left, right, n_blocks):
    rows = left.shape[1] // n_blocks
    total = None
    for block in range(n_blocks):
        piece = jnp.dot(
            left[:, block * rows:(block + 1) * rows],
            right[block * rows:(block + 1) * rows],
            preferred_element_type=jnp.float32,
        ).astype(jnp.bfloat16).astype(jnp.float32)
        total = piece if total is None else total + piece
    return total.astype(jnp.bfloat16)


def shards(tokens, norm_gain, qkv_weight, head_weight, up_weight, down_weight, cotangent):
    n_dp, n_mp = lax.axis_size("dp"), lax.axis_size("mp")
    head_slice = HS // n_mp
    quarter = qkv_weight.shape[-1]
    rows, width = tokens.shape
    qkv_flat = qkv_weight.reshape(-1, quarter)
    head_flat = head_weight.reshape(-1, quarter)

    widened = tokens.astype(jnp.float32)
    block_mean = jnp.mean(widened, axis=1)
    block_center = widened - block_mean[:, None]
    block_m2 = jnp.sum(block_center * block_center, axis=1)
    stats = lax.all_gather(jnp.stack([block_mean, block_m2]), "mp", axis=0, tiled=False)
    row_mean = jnp.mean(stats[:, 0], axis=0)
    spread = stats[:, 0] - row_mean[None, :]
    row_m2 = jnp.sum(stats[:, 1], axis=0) + width * jnp.sum(spread * spread, axis=0)
    row_scale = lax.rsqrt(row_m2 / D + epsilon)[:, None]
    normed = (widened - row_mean[:, None]) * row_scale
    gain_wide = norm_gain.astype(jnp.float32)
    hidden_local = (normed * gain_wide).astype(jnp.bfloat16)
    hidden_all = spread_quarter(hidden_local)
    cot_all = spread_quarter(cotangent)

    n_proj = qkv_flat.shape[0]
    proj_up = jnp.concatenate(
        [
            lax.dot_general(qkv_flat, hidden_all, contract_cols, preferred_element_type=jnp.float32),
            lax.dot_general(up_weight, hidden_all, contract_cols, preferred_element_type=jnp.float32),
        ],
        axis=0,
    )
    proj_up = lax.psum_scatter(proj_up, "dp", scatter_dimension=1, tiled=True)
    projected = proj_up[:n_proj].astype(jnp.bfloat16).reshape(3, head_slice, HEADS, ROWS)
    up_input = proj_up[n_proj:]
    activated, gelu_slope = gelu_pair(up_input)
    up_output = activated.astype(jnp.bfloat16)

    by_head = HEADS % n_mp == 0
    if by_head:
        head_group = HEADS // n_mp
        qkv_heads = lax.all_to_all(projected, "mp", split_axis=2, concat_axis=1, tiled=True)
        query_heads = qkv_heads[0].reshape(HS, head_group * QB, TQ)
        pairs = jnp.stack([qkv_heads[1], qkv_heads[2]], axis=2)
        pair_heads = jnp.broadcast_to(
            pairs[:, :, None], (HS, head_group, QB, 2, PATCHES)
        ).reshape(HS, head_group * QB, 2, PATCHES)
        attended, stored = attend(query_heads, pair_heads)
        head_rows = lax.all_to_all(
            attended.reshape(HS, head_group, ROWS), "mp", split_axis=0, concat_axis=1, tiled=True
        ).reshape(head_slice * HEADS, ROWS)
    else:
        queries = projected[0].reshape(head_slice, ITEMS, TQ)
        keyvals = to_items(projected[1:])
        query_heads, pair_heads = (
            lax.all_to_all(queries, "mp", split_axis=1, concat_axis=0, tiled=True),
            lax.all_to_all(keyvals, "mp", split_axis=1, concat_axis=0, tiled=True),
        )
        attended, stored = attend(query_heads, pair_heads)
        head_rows = lax.all_to_all(attended, "mp", split_axis=0, concat_axis=1, tiled=True).reshape(
            head_slice * HEADS, ROWS
        )
    n_att = head_rows.shape[0]
    both_all = lax.all_gather(
        jnp.concatenate([head_rows, up_output], axis=0), "dp", axis=1, tiled=True
    )
    head_rows_all, up_output_all = both_all[:n_att], both_all[n_att:]
    branch = lax.dot_general(
        head_rows_all, head_flat, contract_rows, preferred_element_type=jnp.float32
    ) + lax.dot_general(up_output_all, down_weight, contract_rows, preferred_element_type=jnp.float32)
    branch_local = gather_quarter(branch, rows)
    mixed = (widened + branch_local).astype(jnp.bfloat16)

    down_grad = blockwise_grad(up_output_all, cot_all, n_dp)
    head_grad = blockwise_grad(head_rows_all, cot_all, n_dp)
    back = jnp.concatenate(
        [
            lax.dot_general(head_flat, cot_all, contract_cols, preferred_element_type=jnp.float32),
            lax.dot_general(down_weight, cot_all, contract_cols, preferred_element_type=jnp.float32),
        ],
        axis=0,
    )
    back = lax.psum_scatter(back, "dp", scatter_dimension=1, tiled=True)
    up_upstream = (back[n_att:] * gelu_slope).astype(jnp.bfloat16)
    head_upstream = back[:n_att].astype(jnp.bfloat16).reshape(head_slice, HEADS, ROWS)
    if by_head:
        upstream = lax.all_to_all(
            head_upstream, "mp", split_axis=1, concat_axis=0, tiled=True
        ).reshape(HS, head_group * QB, TQ)
        query_grad, pair_grad = attend_back(upstream, stored)
        pair_sum = jnp.sum(
            pair_grad.reshape(HS, head_group, QB, 2, PATCHES).astype(jnp.float32), axis=2
        ).astype(jnp.bfloat16)
        grads = jnp.stack(
            [query_grad.reshape(HS, head_group, ROWS), pair_sum[:, :, 0], pair_sum[:, :, 1]]
        )
        proj_grad = lax.all_to_all(grads, "mp", split_axis=1, concat_axis=2, tiled=True)
    else:
        upstream = lax.all_to_all(
            head_upstream.reshape(head_slice, ITEMS, TQ), "mp", split_axis=1, concat_axis=0, tiled=True
        )
        query_grad, pair_grad = attend_back(upstream, stored)
        query_local, pair_local = (
            lax.all_to_all(query_grad, "mp", split_axis=0, concat_axis=1, tiled=True),
            lax.all_to_all(pair_grad, "mp", split_axis=0, concat_axis=1, tiled=True),
        )
        proj_grad = jnp.concatenate(
            [query_local.reshape(1, head_slice, HEADS, ROWS), from_items(pair_local)], axis=0
        )
    proj_grad = proj_grad.reshape(3 * head_slice * HEADS, ROWS)
    grads_all = lax.all_gather(
        jnp.concatenate([proj_grad, up_upstream], axis=0), "dp", axis=1, tiled=True
    )
    proj_grad_all, up_upstream_all = grads_all[:n_proj], grads_all[n_proj:]
    qkv_grad = blockwise_grad(proj_grad_all, hidden_all, n_dp)
    up_grad = blockwise_grad(up_upstream_all, hidden_all, n_dp)
    input_partial = lax.dot_general(
        proj_grad_all, qkv_flat, contract_rows, preferred_element_type=jnp.float32
    ) + lax.dot_general(up_upstream_all, up_weight, contract_rows, preferred_element_type=jnp.float32)
    input_local = gather_quarter(input_partial, rows)

    scaled = input_local * gain_wide
    plain_sum, cross_sum = lax.psum(
        (jnp.sum(scaled, axis=1), jnp.sum(scaled * normed, axis=1)), "mp"
    )
    tokens_grad = row_scale * (
        scaled - plain_sum[:, None] / D - normed * (cross_sum[:, None] / D)
    )
    tokens_grad = tokens_grad + cotangent.astype(jnp.float32)
    gain_piece = jnp.sum(input_local * normed, axis=0)
    gain_grad = lax.psum(gain_piece, "dp")
    return (
        mixed,
        tokens_grad,
        qkv_grad.reshape(qkv_weight.shape),
        head_grad.reshape(head_weight.shape),
        up_grad,
        down_grad,
        gain_grad,
    )


def solution(mesh):
    in_specs = (
        P("dp", "mp"),
        P("mp"),
        P(None, "mp", None, "dp"),
        P("mp", None, "dp"),
        P("mp", "dp"),
        P("mp", "dp"),
        P("dp", "mp"),
    )
    out_specs = (
        P("dp", "mp"),
        P("dp", "mp"),
        P(None, "mp", None, "dp"),
        P("mp", None, "dp"),
        P("mp", "dp"),
        P("mp", "dp"),
        P("mp"),
    )
    return jax.shard_map(shards, mesh=mesh, in_specs=in_specs, out_specs=out_specs, check_vma=False)
```

```python
import math

import jax
import jax.numpy as jnp
from jax import lax
from jax.sharding import PartitionSpec as P

D = 6144
HEADS = 24
HS = 128
PATCHES = 128
QB = 8
IMG_DP = 1
ROWS = 128
TQ = 16
ITEMS = 192


epsilon = 1e-06
contract_rows = (((0,), (0,)), ((), ()))
contract_cols = (((1,), (1,)), ((), ()))


def gelu_pair(inputs):
    normal_cdf = 0.5 * (1.0 + jax.scipy.special.erf(inputs * 0.7071067811865476))
    density = jnp.exp(-0.5 * inputs * inputs) * 0.3989422804014327
    return (inputs * normal_cdf, normal_cdf + inputs * density)


def head_norm(values):
    center = values - jnp.mean(values, axis=0, keepdims=True)
    inverse = lax.rsqrt(jnp.mean(center * center, axis=0, keepdims=True) + epsilon)
    return (center * inverse, inverse)


def norm_back(upstream, normed, inverse):
    return inverse * (
        upstream
        - jnp.mean(upstream, axis=0, keepdims=True)
        - normed * jnp.mean(upstream * normed, axis=0, keepdims=True)
    )


def to_items(pair_rows):
    depth = pair_rows.shape[1]
    shaped = pair_rows.reshape(2, depth, HEADS, IMG_DP, 1, PATCHES)
    spread = jnp.broadcast_to(shaped, (2, depth, HEADS, IMG_DP, QB, PATCHES))
    return jnp.transpose(spread, (1, 2, 3, 4, 0, 5)).reshape(depth, HEADS * IMG_DP * QB, 2, PATCHES)


def from_items(pair_items):
    depth = pair_items.shape[0]
    shaped = pair_items.reshape(depth, HEADS, IMG_DP, QB, 2, PATCHES)
    summed = jnp.sum(shaped.astype(jnp.float32), axis=3).astype(jnp.bfloat16)
    return jnp.transpose(summed, (3, 0, 1, 2, 4)).reshape(2, depth, HEADS, IMG_DP * PATCHES)


def attend(queries, keyvals):
    query_hat, query_scale = head_norm(queries.astype(jnp.float32))
    key_hat, key_scale = head_norm(keyvals[:, :, 0].astype(jnp.float32))
    query_norm = query_hat.astype(jnp.bfloat16)
    key_norm = key_hat.astype(jnp.bfloat16)
    factor = 1.0 / math.sqrt(queries.shape[0])
    scores = (
        jnp.einsum("cia,cib->iab", query_norm, key_norm, preferred_element_type=jnp.float32)
        * factor
    )
    raised = jnp.exp(scores)
    shares = raised / jnp.sum(raised, axis=2, keepdims=True)
    rounded = shares.astype(jnp.bfloat16)
    values = keyvals[:, :, 1]
    attended = jnp.einsum(
        "iab,cib->cia", rounded, values, preferred_element_type=jnp.float32
    ).astype(jnp.bfloat16)
    stored = (
        query_hat,
        query_scale,
        key_hat,
        key_scale,
        query_norm,
        key_norm,
        shares,
        rounded,
        values,
    )
    return (attended, stored)


def attend_back(upstream, stored):
    query_hat, query_scale, key_hat, key_scale, query_norm, key_norm, shares, rounded, values = (
        stored
    )
    factor = 1.0 / math.sqrt(upstream.shape[0])
    share_grad = jnp.einsum("cia,cib->iab", upstream, values, preferred_element_type=jnp.float32)
    value_grad = jnp.einsum("iab,cia->cib", rounded, upstream, preferred_element_type=jnp.float32)
    score_grad = (
        shares * (share_grad - jnp.sum(shares * share_grad, axis=2, keepdims=True)) * factor
    ).astype(jnp.bfloat16)
    query_back = jnp.einsum(
        "iab,cib->cia", score_grad, key_norm, preferred_element_type=jnp.float32
    )
    key_back = jnp.einsum(
        "iab,cia->cib", score_grad, query_norm, preferred_element_type=jnp.float32
    )
    query_grad = norm_back(query_back, query_hat, query_scale).astype(jnp.bfloat16)
    key_grad = norm_back(key_back, key_hat, key_scale).astype(jnp.bfloat16)
    pair_grad = jnp.stack([key_grad, value_grad.astype(jnp.bfloat16)], axis=2)
    return (query_grad, pair_grad)


def swap_pairs(n_dp, n_mp):
    ratio = n_mp // n_dp
    pairs = []
    for row in range(n_dp):
        for col in range(n_mp):
            owner, part = divmod(col, ratio)
            pairs.append((row * n_mp + col, owner * n_mp + row * ratio + part))
    return pairs


def swap(block):
    n_dp, n_mp = lax.axis_size("dp"), lax.axis_size("mp")
    return lax.ppermute(block, ("dp", "mp"), swap_pairs(n_dp, n_mp))


def spread_quarter(block):
    n_dp, n_mp = lax.axis_size("dp"), lax.axis_size("mp")
    ratio = n_mp // n_dp
    rows, width = block.shape
    pieces = lax.all_gather(swap(block), "mp", axis=0, tiled=False)
    pieces = pieces.reshape(n_dp, ratio, rows, width)
    return jnp.transpose(pieces, (0, 2, 1, 3)).reshape(n_dp * rows, ratio * width)


def gather_quarter(partial, rows):
    n_dp, n_mp = lax.axis_size("dp"), lax.axis_size("mp")
    ratio = n_mp // n_dp
    width = partial.shape[1] // ratio
    pieces = partial.reshape(n_dp, rows, ratio, width)
    pieces = jnp.transpose(pieces, (0, 2, 1, 3)).reshape(n_mp, rows, width)
    summed = lax.psum_scatter(pieces, "mp", scatter_dimension=0, tiled=True)
    return swap(summed.reshape(rows, width))


def gather_quarter_exchange(partial, rows):
    n_dp, n_mp = lax.axis_size("dp"), lax.axis_size("mp")
    ratio = n_mp // n_dp
    width = partial.shape[1] // ratio
    pieces = partial.reshape(n_dp, rows, ratio, width)
    pieces = jnp.transpose(pieces, (0, 2, 1, 3)).reshape(n_mp, rows, width)
    received = lax.all_to_all(pieces, "mp", split_axis=0, concat_axis=0, tiled=True)
    return swap(jnp.sum(received, axis=0))


def blockwise_grad(left, right, n_blocks):
    rows = left.shape[1] // n_blocks
    total = None
    for block in range(n_blocks):
        piece = jnp.dot(
            left[:, block * rows:(block + 1) * rows],
            right[block * rows:(block + 1) * rows],
            preferred_element_type=jnp.float32,
        ).astype(jnp.bfloat16).astype(jnp.float32)
        total = piece if total is None else total + piece
    return total.astype(jnp.bfloat16)


def shards(tokens, norm_gain, qkv_weight, head_weight, up_weight, down_weight, cotangent):
    n_dp, n_mp = lax.axis_size("dp"), lax.axis_size("mp")
    head_slice = HS // n_mp
    quarter = qkv_weight.shape[-1]
    rows, width = tokens.shape
    qkv_flat = qkv_weight.reshape(-1, quarter)
    head_flat = head_weight.reshape(-1, quarter)

    widened = tokens.astype(jnp.float32)
    block_mean = jnp.mean(widened, axis=1)
    block_center = widened - block_mean[:, None]
    block_m2 = jnp.sum(block_center * block_center, axis=1)
    stats = lax.all_gather(jnp.stack([block_mean, block_m2]), "mp", axis=0, tiled=False)
    row_mean = jnp.mean(stats[:, 0], axis=0)
    spread = stats[:, 0] - row_mean[None, :]
    row_m2 = jnp.sum(stats[:, 1], axis=0) + width * jnp.sum(spread * spread, axis=0)
    row_scale = lax.rsqrt(row_m2 / D + epsilon)[:, None]
    normed = (widened - row_mean[:, None]) * row_scale
    gain_wide = norm_gain.astype(jnp.float32)
    hidden_local = (normed * gain_wide).astype(jnp.bfloat16)
    hidden_all = spread_quarter(hidden_local)

    n_proj = qkv_flat.shape[0]
    proj_up = jnp.concatenate(
        [
            lax.dot_general(qkv_flat, hidden_all, contract_cols, preferred_element_type=jnp.float32),
            lax.dot_general(up_weight, hidden_all, contract_cols, preferred_element_type=jnp.float32),
        ],
        axis=0,
    )
    proj_up = lax.psum_scatter(proj_up, "dp", scatter_dimension=1, tiled=True)
    cot_later, proj_up = lax.optimization_barrier((cotangent, proj_up))
    cot_all = spread_quarter(cot_later)
    projected = proj_up[:n_proj].astype(jnp.bfloat16).reshape(3, head_slice, HEADS, ROWS)
    up_input = proj_up[n_proj:]
    activated, gelu_slope = gelu_pair(up_input)
    up_output = activated.astype(jnp.bfloat16)

    by_head = HEADS % n_mp == 0
    if by_head:
        head_group = HEADS // n_mp
        qkv_heads = lax.all_to_all(projected, "mp", split_axis=2, concat_axis=1, tiled=True)
        query_heads = qkv_heads[0].reshape(HS, head_group * QB, TQ)
        pairs = jnp.stack([qkv_heads[1], qkv_heads[2]], axis=2)
        pair_heads = jnp.broadcast_to(
            pairs[:, :, None], (HS, head_group, QB, 2, PATCHES)
        ).reshape(HS, head_group * QB, 2, PATCHES)
        attended, stored = attend(query_heads, pair_heads)
        head_rows = lax.all_to_all(
            attended.reshape(HS, head_group, ROWS), "mp", split_axis=0, concat_axis=1, tiled=True
        ).reshape(head_slice * HEADS, ROWS)
    else:
        queries = projected[0].reshape(head_slice, ITEMS, TQ)
        keyvals = to_items(projected[1:])
        query_heads, pair_heads = (
            lax.all_to_all(queries, "mp", split_axis=1, concat_axis=0, tiled=True),
            lax.all_to_all(keyvals, "mp", split_axis=1, concat_axis=0, tiled=True),
        )
        attended, stored = attend(query_heads, pair_heads)
        head_rows = lax.all_to_all(attended, "mp", split_axis=0, concat_axis=1, tiled=True).reshape(
            head_slice * HEADS, ROWS
        )
    n_att = head_rows.shape[0]
    both_all = lax.all_gather(
        jnp.concatenate([head_rows, up_output], axis=0), "dp", axis=1, tiled=True
    )
    head_rows_all, up_output_all = both_all[:n_att], both_all[n_att:]
    branch = lax.dot_general(
        head_rows_all, head_flat, contract_rows, preferred_element_type=jnp.float32
    ) + lax.dot_general(up_output_all, down_weight, contract_rows, preferred_element_type=jnp.float32)
    branch_local = gather_quarter_exchange(branch, rows)
    mixed = (widened + branch_local).astype(jnp.bfloat16)

    down_grad = blockwise_grad(up_output_all, cot_all, n_dp)
    head_grad = blockwise_grad(head_rows_all, cot_all, n_dp)
    back = jnp.concatenate(
        [
            lax.dot_general(head_flat, cot_all, contract_cols, preferred_element_type=jnp.float32),
            lax.dot_general(down_weight, cot_all, contract_cols, preferred_element_type=jnp.float32),
        ],
        axis=0,
    )
    back = lax.psum_scatter(back, "dp", scatter_dimension=1, tiled=True)
    up_upstream = (back[n_att:] * gelu_slope).astype(jnp.bfloat16)
    head_upstream = back[:n_att].astype(jnp.bfloat16).reshape(head_slice, HEADS, ROWS)
    if by_head:
        upstream = lax.all_to_all(
            head_upstream, "mp", split_axis=1, concat_axis=0, tiled=True
        ).reshape(HS, head_group * QB, TQ)
        query_grad, pair_grad = attend_back(upstream, stored)
        pair_sum = jnp.sum(
            pair_grad.reshape(HS, head_group, QB, 2, PATCHES).astype(jnp.float32), axis=2
        ).astype(jnp.bfloat16)
        grads = jnp.stack(
            [query_grad.reshape(HS, head_group, ROWS), pair_sum[:, :, 0], pair_sum[:, :, 1]]
        )
        proj_grad = lax.all_to_all(grads, "mp", split_axis=1, concat_axis=2, tiled=True)
    else:
        upstream = lax.all_to_all(
            head_upstream.reshape(head_slice, ITEMS, TQ), "mp", split_axis=1, concat_axis=0, tiled=True
        )
        query_grad, pair_grad = attend_back(upstream, stored)
        query_local, pair_local = (
            lax.all_to_all(query_grad, "mp", split_axis=0, concat_axis=1, tiled=True),
            lax.all_to_all(pair_grad, "mp", split_axis=0, concat_axis=1, tiled=True),
        )
        proj_grad = jnp.concatenate(
            [query_local.reshape(1, head_slice, HEADS, ROWS), from_items(pair_local)], axis=0
        )
    proj_grad = proj_grad.reshape(3 * head_slice * HEADS, ROWS)
    grads_all = lax.all_gather(
        jnp.concatenate([proj_grad, up_upstream], axis=0), "dp", axis=1, tiled=True
    )
    proj_grad_all, up_upstream_all = grads_all[:n_proj], grads_all[n_proj:]
    qkv_grad = blockwise_grad(proj_grad_all, hidden_all, n_dp)
    up_grad = blockwise_grad(up_upstream_all, hidden_all, n_dp)
    input_partial = lax.dot_general(
        proj_grad_all, qkv_flat, contract_rows, preferred_element_type=jnp.float32
    ) + lax.dot_general(up_upstream_all, up_weight, contract_rows, preferred_element_type=jnp.float32)
    input_local = gather_quarter(input_partial, rows)

    scaled = input_local * gain_wide
    plain_sum, cross_sum = lax.psum(
        (jnp.sum(scaled, axis=1), jnp.sum(scaled * normed, axis=1)), "mp"
    )
    tokens_grad = row_scale * (
        scaled - plain_sum[:, None] / D - normed * (cross_sum[:, None] / D)
    )
    tokens_grad = tokens_grad + cotangent.astype(jnp.float32)
    gain_piece = jnp.sum(input_local * normed, axis=0)
    gain_grad = lax.psum(gain_piece, "dp")
    return (
        mixed,
        tokens_grad,
        qkv_grad.reshape(qkv_weight.shape),
        head_grad.reshape(head_weight.shape),
        up_grad,
        down_grad,
        gain_grad,
    )


def solution(mesh):
    in_specs = (
        P("dp", "mp"),
        P("mp"),
        P(None, "mp", None, "dp"),
        P("mp", None, "dp"),
        P("mp", "dp"),
        P("mp", "dp"),
        P("dp", "mp"),
    )
    out_specs = (
        P("dp", "mp"),
        P("dp", "mp"),
        P(None, "mp", None, "dp"),
        P("mp", None, "dp"),
        P("mp", "dp"),
        P("mp", "dp"),
        P("mp"),
    )
    return jax.shard_map(shards, mesh=mesh, in_specs=in_specs, out_specs=out_specs, check_vma=False)
```

```python
import math

import jax
import jax.numpy as jnp
from jax import lax
from jax.sharding import PartitionSpec as P

D = 6144
HEADS = 24
HS = 128
PATCHES = 128
QB = 8
IMG_DP = 1
ROWS = 128
TQ = 16
ITEMS = 192


epsilon = 1e-06
contract_rows = (((0,), (0,)), ((), ()))
contract_cols = (((1,), (1,)), ((), ()))


def gelu_pair(inputs):
    normal_cdf = 0.5 * (1.0 + jax.scipy.special.erf(inputs * 0.7071067811865476))
    density = jnp.exp(-0.5 * inputs * inputs) * 0.3989422804014327
    return (inputs * normal_cdf, normal_cdf + inputs * density)


def head_norm(values):
    center = values - jnp.mean(values, axis=0, keepdims=True)
    inverse = lax.rsqrt(jnp.mean(center * center, axis=0, keepdims=True) + epsilon)
    return (center * inverse, inverse)


def norm_back(upstream, normed, inverse):
    return inverse * (
        upstream
        - jnp.mean(upstream, axis=0, keepdims=True)
        - normed * jnp.mean(upstream * normed, axis=0, keepdims=True)
    )


def to_items(pair_rows):
    depth = pair_rows.shape[1]
    shaped = pair_rows.reshape(2, depth, HEADS, IMG_DP, 1, PATCHES)
    spread = jnp.broadcast_to(shaped, (2, depth, HEADS, IMG_DP, QB, PATCHES))
    return jnp.transpose(spread, (1, 2, 3, 4, 0, 5)).reshape(depth, HEADS * IMG_DP * QB, 2, PATCHES)


def from_items(pair_items):
    depth = pair_items.shape[0]
    shaped = pair_items.reshape(depth, HEADS, IMG_DP, QB, 2, PATCHES)
    summed = jnp.sum(shaped.astype(jnp.float32), axis=3).astype(jnp.bfloat16)
    return jnp.transpose(summed, (3, 0, 1, 2, 4)).reshape(2, depth, HEADS, IMG_DP * PATCHES)


def attend(queries, keyvals):
    query_hat, query_scale = head_norm(queries.astype(jnp.float32))
    key_hat, key_scale = head_norm(keyvals[:, :, 0].astype(jnp.float32))
    query_norm = query_hat.astype(jnp.bfloat16)
    key_norm = key_hat.astype(jnp.bfloat16)
    factor = 1.0 / math.sqrt(queries.shape[0])
    scores = (
        jnp.einsum("cia,cib->iab", query_norm, key_norm, preferred_element_type=jnp.float32)
        * factor
    )
    raised = jnp.exp(scores)
    shares = raised / jnp.sum(raised, axis=2, keepdims=True)
    rounded = shares.astype(jnp.bfloat16)
    values = keyvals[:, :, 1]
    attended = jnp.einsum(
        "iab,cib->cia", rounded, values, preferred_element_type=jnp.float32
    ).astype(jnp.bfloat16)
    stored = (
        query_hat,
        query_scale,
        key_hat,
        key_scale,
        query_norm,
        key_norm,
        shares,
        rounded,
        values,
    )
    return (attended, stored)


def attend_back(upstream, stored):
    query_hat, query_scale, key_hat, key_scale, query_norm, key_norm, shares, rounded, values = (
        stored
    )
    factor = 1.0 / math.sqrt(upstream.shape[0])
    share_grad = jnp.einsum("cia,cib->iab", upstream, values, preferred_element_type=jnp.float32)
    value_grad = jnp.einsum("iab,cia->cib", rounded, upstream, preferred_element_type=jnp.float32)
    score_grad = (
        shares * (share_grad - jnp.sum(shares * share_grad, axis=2, keepdims=True)) * factor
    ).astype(jnp.bfloat16)
    query_back = jnp.einsum(
        "iab,cib->cia", score_grad, key_norm, preferred_element_type=jnp.float32
    )
    key_back = jnp.einsum(
        "iab,cia->cib", score_grad, query_norm, preferred_element_type=jnp.float32
    )
    query_grad = norm_back(query_back, query_hat, query_scale).astype(jnp.bfloat16)
    key_grad = norm_back(key_back, key_hat, key_scale).astype(jnp.bfloat16)
    pair_grad = jnp.stack([key_grad, value_grad.astype(jnp.bfloat16)], axis=2)
    return (query_grad, pair_grad)


def swap_pairs(n_dp, n_mp):
    ratio = n_mp // n_dp
    pairs = []
    for row in range(n_dp):
        for col in range(n_mp):
            owner, part = divmod(col, ratio)
            pairs.append((row * n_mp + col, owner * n_mp + row * ratio + part))
    return pairs


def swap(block):
    n_dp, n_mp = lax.axis_size("dp"), lax.axis_size("mp")
    return lax.ppermute(block, ("dp", "mp"), swap_pairs(n_dp, n_mp))


def spread_quarter(block):
    n_dp, n_mp = lax.axis_size("dp"), lax.axis_size("mp")
    ratio = n_mp // n_dp
    rows, width = block.shape
    pieces = lax.all_gather(swap(block), "mp", axis=0, tiled=False)
    pieces = pieces.reshape(n_dp, ratio, rows, width)
    return jnp.transpose(pieces, (0, 2, 1, 3)).reshape(n_dp * rows, ratio * width)


def gather_quarter(partial, rows):
    n_dp, n_mp = lax.axis_size("dp"), lax.axis_size("mp")
    ratio = n_mp // n_dp
    width = partial.shape[1] // ratio
    pieces = partial.reshape(n_dp, rows, ratio, width)
    pieces = jnp.transpose(pieces, (0, 2, 1, 3)).reshape(n_mp, rows, width)
    summed = lax.psum_scatter(pieces, "mp", scatter_dimension=0, tiled=True)
    return swap(summed.reshape(rows, width))


def gather_quarter_exchange(partial, rows):
    n_dp, n_mp = lax.axis_size("dp"), lax.axis_size("mp")
    ratio = n_mp // n_dp
    width = partial.shape[1] // ratio
    pieces = partial.reshape(n_dp, rows, ratio, width)
    pieces = jnp.transpose(pieces, (0, 2, 1, 3)).reshape(n_mp, rows, width)
    received = lax.all_to_all(pieces, "mp", split_axis=0, concat_axis=0, tiled=True)
    return swap(jnp.sum(received, axis=0))


def blockwise_grad(left, right, n_blocks):
    rows = left.shape[1] // n_blocks
    total = None
    for block in range(n_blocks):
        piece = jnp.dot(
            left[:, block * rows:(block + 1) * rows],
            right[block * rows:(block + 1) * rows],
            preferred_element_type=jnp.float32,
        ).astype(jnp.bfloat16).astype(jnp.float32)
        total = piece if total is None else total + piece
    return total.astype(jnp.bfloat16)


def shards(tokens, norm_gain, qkv_weight, head_weight, up_weight, down_weight, cotangent):
    n_dp, n_mp = lax.axis_size("dp"), lax.axis_size("mp")
    head_slice = HS // n_mp
    quarter = qkv_weight.shape[-1]
    rows, width = tokens.shape
    qkv_flat = qkv_weight.reshape(-1, quarter)
    head_flat = head_weight.reshape(-1, quarter)

    widened = tokens.astype(jnp.float32)
    block_mean = jnp.mean(widened, axis=1)
    block_center = widened - block_mean[:, None]
    block_m2 = jnp.sum(block_center * block_center, axis=1)
    stats = lax.all_gather(jnp.stack([block_mean, block_m2]), "mp", axis=0, tiled=False)
    row_mean = jnp.mean(stats[:, 0], axis=0)
    spread = stats[:, 0] - row_mean[None, :]
    row_m2 = jnp.sum(stats[:, 1], axis=0) + width * jnp.sum(spread * spread, axis=0)
    row_scale = lax.rsqrt(row_m2 / D + epsilon)[:, None]
    normed = (widened - row_mean[:, None]) * row_scale
    gain_wide = norm_gain.astype(jnp.float32)
    hidden_local = (normed * gain_wide).astype(jnp.bfloat16)
    hidden_all = spread_quarter(hidden_local)
    cot_all = spread_quarter(cotangent)

    n_proj = qkv_flat.shape[0]
    proj_up = jnp.concatenate(
        [
            lax.dot_general(qkv_flat, hidden_all, contract_cols, preferred_element_type=jnp.float32),
            lax.dot_general(up_weight, hidden_all, contract_cols, preferred_element_type=jnp.float32),
        ],
        axis=0,
    )
    proj_up = lax.psum_scatter(proj_up, "dp", scatter_dimension=1, tiled=True)
    cot_later, proj_up = lax.optimization_barrier((cot_all, proj_up))
    projected = proj_up[:n_proj].astype(jnp.bfloat16).reshape(3, head_slice, HEADS, ROWS)
    up_input = proj_up[n_proj:]
    activated, gelu_slope = gelu_pair(up_input)
    up_output = activated.astype(jnp.bfloat16)

    by_head = HEADS % n_mp == 0
    if by_head:
        head_group = HEADS // n_mp
        qkv_heads = lax.all_to_all(projected, "mp", split_axis=2, concat_axis=1, tiled=True)
        query_heads = qkv_heads[0].reshape(HS, head_group * QB, TQ)
        pairs = jnp.stack([qkv_heads[1], qkv_heads[2]], axis=2)
        pair_heads = jnp.broadcast_to(
            pairs[:, :, None], (HS, head_group, QB, 2, PATCHES)
        ).reshape(HS, head_group * QB, 2, PATCHES)
        attended, stored = attend(query_heads, pair_heads)
        head_rows = lax.all_to_all(
            attended.reshape(HS, head_group, ROWS), "mp", split_axis=0, concat_axis=1, tiled=True
        ).reshape(head_slice * HEADS, ROWS)
    else:
        queries = projected[0].reshape(head_slice, ITEMS, TQ)
        keyvals = to_items(projected[1:])
        query_heads, pair_heads = (
            lax.all_to_all(queries, "mp", split_axis=1, concat_axis=0, tiled=True),
            lax.all_to_all(keyvals, "mp", split_axis=1, concat_axis=0, tiled=True),
        )
        attended, stored = attend(query_heads, pair_heads)
        head_rows = lax.all_to_all(attended, "mp", split_axis=0, concat_axis=1, tiled=True).reshape(
            head_slice * HEADS, ROWS
        )
    n_att = head_rows.shape[0]
    both_all = lax.all_gather(
        jnp.concatenate([head_rows, up_output], axis=0), "dp", axis=1, tiled=True
    )
    head_rows_all, up_output_all = both_all[:n_att], both_all[n_att:]
    branch = lax.dot_general(
        head_rows_all, head_flat, contract_rows, preferred_element_type=jnp.float32
    ) + lax.dot_general(up_output_all, down_weight, contract_rows, preferred_element_type=jnp.float32)
    branch_local = gather_quarter_exchange(branch, rows)
    mixed = (widened + branch_local).astype(jnp.bfloat16)

    down_grad = blockwise_grad(up_output_all, cot_all, n_dp)
    head_grad = blockwise_grad(head_rows_all, cot_all, n_dp)
    back = jnp.concatenate(
        [
            lax.dot_general(head_flat, cot_later, contract_cols, preferred_element_type=jnp.float32),
            lax.dot_general(down_weight, cot_later, contract_cols, preferred_element_type=jnp.float32),
        ],
        axis=0,
    )
    back = lax.psum_scatter(back, "dp", scatter_dimension=1, tiled=True)
    up_upstream = (back[n_att:] * gelu_slope).astype(jnp.bfloat16)
    head_upstream = back[:n_att].astype(jnp.bfloat16).reshape(head_slice, HEADS, ROWS)
    if by_head:
        upstream = lax.all_to_all(
            head_upstream, "mp", split_axis=1, concat_axis=0, tiled=True
        ).reshape(HS, head_group * QB, TQ)
        query_grad, pair_grad = attend_back(upstream, stored)
        pair_sum = jnp.sum(
            pair_grad.reshape(HS, head_group, QB, 2, PATCHES).astype(jnp.float32), axis=2
        ).astype(jnp.bfloat16)
        grads = jnp.stack(
            [query_grad.reshape(HS, head_group, ROWS), pair_sum[:, :, 0], pair_sum[:, :, 1]]
        )
        proj_grad = lax.all_to_all(grads, "mp", split_axis=1, concat_axis=2, tiled=True)
    else:
        upstream = lax.all_to_all(
            head_upstream.reshape(head_slice, ITEMS, TQ), "mp", split_axis=1, concat_axis=0, tiled=True
        )
        query_grad, pair_grad = attend_back(upstream, stored)
        query_local, pair_local = (
            lax.all_to_all(query_grad, "mp", split_axis=0, concat_axis=1, tiled=True),
            lax.all_to_all(pair_grad, "mp", split_axis=0, concat_axis=1, tiled=True),
        )
        proj_grad = jnp.concatenate(
            [query_local.reshape(1, head_slice, HEADS, ROWS), from_items(pair_local)], axis=0
        )
    proj_grad = proj_grad.reshape(3 * head_slice * HEADS, ROWS)
    grads_all = lax.all_gather(
        jnp.concatenate([proj_grad, up_upstream], axis=0), "dp", axis=1, tiled=True
    )
    proj_grad_all, up_upstream_all = grads_all[:n_proj], grads_all[n_proj:]
    qkv_grad = blockwise_grad(proj_grad_all, hidden_all, n_dp)
    up_grad = blockwise_grad(up_upstream_all, hidden_all, n_dp)
    input_partial = lax.dot_general(
        proj_grad_all, qkv_flat, contract_rows, preferred_element_type=jnp.float32
    ) + lax.dot_general(up_upstream_all, up_weight, contract_rows, preferred_element_type=jnp.float32)
    input_local = gather_quarter(input_partial, rows)

    scaled = input_local * gain_wide
    plain_sum, cross_sum = lax.psum(
        (jnp.sum(scaled, axis=1), jnp.sum(scaled * normed, axis=1)), "mp"
    )
    tokens_grad = row_scale * (
        scaled - plain_sum[:, None] / D - normed * (cross_sum[:, None] / D)
    )
    tokens_grad = tokens_grad + cotangent.astype(jnp.float32)
    gain_piece = jnp.sum(input_local * normed, axis=0)
    gain_grad = lax.psum(gain_piece, "dp")
    return (
        mixed,
        tokens_grad,
        qkv_grad.reshape(qkv_weight.shape),
        head_grad.reshape(head_weight.shape),
        up_grad,
        down_grad,
        gain_grad,
    )


def solution(mesh):
    in_specs = (
        P("dp", "mp"),
        P("mp"),
        P(None, "mp", None, "dp"),
        P("mp", None, "dp"),
        P("mp", "dp"),
        P("mp", "dp"),
        P("dp", "mp"),
    )
    out_specs = (
        P("dp", "mp"),
        P("dp", "mp"),
        P(None, "mp", None, "dp"),
        P("mp", None, "dp"),
        P("mp", "dp"),
        P("mp", "dp"),
        P("mp"),
    )
    return jax.shard_map(shards, mesh=mesh, in_specs=in_specs, out_specs=out_specs, check_vma=False)
```

```python
import math

import jax
import jax.numpy as jnp
from jax import lax
from jax.sharding import PartitionSpec as P

D = 6144
HEADS = 24
HS = 128
PATCHES = 128
QB = 8
IMG_DP = 1
ROWS = 128
TQ = 16
ITEMS = 192


epsilon = 1e-06
contract_rows = (((0,), (0,)), ((), ()))
contract_cols = (((1,), (1,)), ((), ()))


def gelu_pair(inputs):
    normal_cdf = 0.5 * (1.0 + jax.scipy.special.erf(inputs * 0.7071067811865476))
    density = jnp.exp(-0.5 * inputs * inputs) * 0.3989422804014327
    return (inputs * normal_cdf, normal_cdf + inputs * density)


def head_norm(values):
    center = values - jnp.mean(values, axis=0, keepdims=True)
    inverse = lax.rsqrt(jnp.mean(center * center, axis=0, keepdims=True) + epsilon)
    return (center * inverse, inverse)


def norm_back(upstream, normed, inverse):
    return inverse * (
        upstream
        - jnp.mean(upstream, axis=0, keepdims=True)
        - normed * jnp.mean(upstream * normed, axis=0, keepdims=True)
    )


def to_items(pair_rows):
    depth = pair_rows.shape[1]
    shaped = pair_rows.reshape(2, depth, HEADS, IMG_DP, 1, PATCHES)
    spread = jnp.broadcast_to(shaped, (2, depth, HEADS, IMG_DP, QB, PATCHES))
    return jnp.transpose(spread, (1, 2, 3, 4, 0, 5)).reshape(depth, HEADS * IMG_DP * QB, 2, PATCHES)


def from_items(pair_items):
    depth = pair_items.shape[0]
    shaped = pair_items.reshape(depth, HEADS, IMG_DP, QB, 2, PATCHES)
    summed = jnp.sum(shaped.astype(jnp.float32), axis=3).astype(jnp.bfloat16)
    return jnp.transpose(summed, (3, 0, 1, 2, 4)).reshape(2, depth, HEADS, IMG_DP * PATCHES)


def attend(queries, keyvals):
    query_hat, query_scale = head_norm(queries.astype(jnp.float32))
    key_hat, key_scale = head_norm(keyvals[:, :, 0].astype(jnp.float32))
    query_norm = query_hat.astype(jnp.bfloat16)
    key_norm = key_hat.astype(jnp.bfloat16)
    factor = 1.0 / math.sqrt(queries.shape[0])
    scores = (
        jnp.einsum("cia,cib->iab", query_norm, key_norm, preferred_element_type=jnp.float32)
        * factor
    )
    raised = jnp.exp(scores)
    shares = raised / jnp.sum(raised, axis=2, keepdims=True)
    rounded = shares.astype(jnp.bfloat16)
    values = keyvals[:, :, 1]
    attended = jnp.einsum(
        "iab,cib->cia", rounded, values, preferred_element_type=jnp.float32
    ).astype(jnp.bfloat16)
    stored = (
        query_hat,
        query_scale,
        key_hat,
        key_scale,
        query_norm,
        key_norm,
        shares,
        rounded,
        values,
    )
    return (attended, stored)


def attend_back(upstream, stored):
    query_hat, query_scale, key_hat, key_scale, query_norm, key_norm, shares, rounded, values = (
        stored
    )
    factor = 1.0 / math.sqrt(upstream.shape[0])
    share_grad = jnp.einsum("cia,cib->iab", upstream, values, preferred_element_type=jnp.float32)
    value_grad = jnp.einsum("iab,cia->cib", rounded, upstream, preferred_element_type=jnp.float32)
    score_grad = (
        shares * (share_grad - jnp.sum(shares * share_grad, axis=2, keepdims=True)) * factor
    ).astype(jnp.bfloat16)
    query_back = jnp.einsum(
        "iab,cib->cia", score_grad, key_norm, preferred_element_type=jnp.float32
    )
    key_back = jnp.einsum(
        "iab,cia->cib", score_grad, query_norm, preferred_element_type=jnp.float32
    )
    query_grad = norm_back(query_back, query_hat, query_scale).astype(jnp.bfloat16)
    key_grad = norm_back(key_back, key_hat, key_scale).astype(jnp.bfloat16)
    pair_grad = jnp.stack([key_grad, value_grad.astype(jnp.bfloat16)], axis=2)
    return (query_grad, pair_grad)


def swap_pairs(n_dp, n_mp):
    ratio = n_mp // n_dp
    pairs = []
    for row in range(n_dp):
        for col in range(n_mp):
            owner, part = divmod(col, ratio)
            pairs.append((row * n_mp + col, owner * n_mp + row * ratio + part))
    return pairs


def swap(block):
    n_dp, n_mp = lax.axis_size("dp"), lax.axis_size("mp")
    return lax.ppermute(block, ("dp", "mp"), swap_pairs(n_dp, n_mp))


def spread_quarter(block):
    n_dp, n_mp = lax.axis_size("dp"), lax.axis_size("mp")
    ratio = n_mp // n_dp
    rows, width = block.shape
    copies = jnp.broadcast_to(swap(block)[None], (n_mp, rows, width))
    pieces = lax.all_to_all(copies, "mp", split_axis=0, concat_axis=0, tiled=True)
    pieces = pieces.reshape(n_dp, ratio, rows, width)
    return jnp.transpose(pieces, (0, 2, 1, 3)).reshape(n_dp * rows, ratio * width)


def gather_quarter(partial, rows):
    n_dp, n_mp = lax.axis_size("dp"), lax.axis_size("mp")
    ratio = n_mp // n_dp
    width = partial.shape[1] // ratio
    pieces = partial.reshape(n_dp, rows, ratio, width)
    pieces = jnp.transpose(pieces, (0, 2, 1, 3)).reshape(n_mp, rows, width)
    summed = lax.psum_scatter(pieces, "mp", scatter_dimension=0, tiled=True)
    return swap(summed.reshape(rows, width))


def gather_quarter_exchange(partial, rows):
    n_dp, n_mp = lax.axis_size("dp"), lax.axis_size("mp")
    ratio = n_mp // n_dp
    width = partial.shape[1] // ratio
    pieces = partial.reshape(n_dp, rows, ratio, width)
    pieces = jnp.transpose(pieces, (0, 2, 1, 3)).reshape(n_mp, rows, width)
    received = lax.all_to_all(pieces, "mp", split_axis=0, concat_axis=0, tiled=True)
    return swap(jnp.sum(received, axis=0))


def blockwise_grad(left, right, n_blocks):
    rows = left.shape[1] // n_blocks
    total = None
    for block in range(n_blocks):
        piece = jnp.dot(
            left[:, block * rows:(block + 1) * rows],
            right[block * rows:(block + 1) * rows],
            preferred_element_type=jnp.float32,
        ).astype(jnp.bfloat16).astype(jnp.float32)
        total = piece if total is None else total + piece
    return total.astype(jnp.bfloat16)


def shards(tokens, norm_gain, qkv_weight, head_weight, up_weight, down_weight, cotangent):
    n_dp, n_mp = lax.axis_size("dp"), lax.axis_size("mp")
    head_slice = HS // n_mp
    quarter = qkv_weight.shape[-1]
    rows, width = tokens.shape
    qkv_flat = qkv_weight.reshape(-1, quarter)
    head_flat = head_weight.reshape(-1, quarter)

    widened = tokens.astype(jnp.float32)
    block_mean = jnp.mean(widened, axis=1)
    block_center = widened - block_mean[:, None]
    block_m2 = jnp.sum(block_center * block_center, axis=1)
    stats = lax.all_gather(jnp.stack([block_mean, block_m2]), "mp", axis=0, tiled=False)
    row_mean = jnp.mean(stats[:, 0], axis=0)
    spread = stats[:, 0] - row_mean[None, :]
    row_m2 = jnp.sum(stats[:, 1], axis=0) + width * jnp.sum(spread * spread, axis=0)
    row_scale = lax.rsqrt(row_m2 / D + epsilon)[:, None]
    normed = (widened - row_mean[:, None]) * row_scale
    gain_wide = norm_gain.astype(jnp.float32)
    hidden_local = (normed * gain_wide).astype(jnp.bfloat16)
    hidden_all = spread_quarter(hidden_local)
    cot_all = spread_quarter(cotangent)

    n_proj = qkv_flat.shape[0]
    proj_up = jnp.concatenate(
        [
            lax.dot_general(qkv_flat, hidden_all, contract_cols, preferred_element_type=jnp.float32),
            lax.dot_general(up_weight, hidden_all, contract_cols, preferred_element_type=jnp.float32),
        ],
        axis=0,
    )
    proj_up = lax.psum_scatter(proj_up, "dp", scatter_dimension=1, tiled=True)
    cot_later, proj_up = lax.optimization_barrier((cot_all, proj_up))
    projected = proj_up[:n_proj].astype(jnp.bfloat16).reshape(3, head_slice, HEADS, ROWS)
    up_input = proj_up[n_proj:]
    activated, gelu_slope = gelu_pair(up_input)
    up_output = activated.astype(jnp.bfloat16)

    by_head = HEADS % n_mp == 0
    if by_head:
        head_group = HEADS // n_mp
        qkv_heads = lax.all_to_all(projected, "mp", split_axis=2, concat_axis=1, tiled=True)
        query_heads = qkv_heads[0].reshape(HS, head_group * QB, TQ)
        pairs = jnp.stack([qkv_heads[1], qkv_heads[2]], axis=2)
        pair_heads = jnp.broadcast_to(
            pairs[:, :, None], (HS, head_group, QB, 2, PATCHES)
        ).reshape(HS, head_group * QB, 2, PATCHES)
        attended, stored = attend(query_heads, pair_heads)
        head_rows = lax.all_to_all(
            attended.reshape(HS, head_group, ROWS), "mp", split_axis=0, concat_axis=1, tiled=True
        ).reshape(head_slice * HEADS, ROWS)
    else:
        queries = projected[0].reshape(head_slice, ITEMS, TQ)
        keyvals = to_items(projected[1:])
        query_heads, pair_heads = (
            lax.all_to_all(queries, "mp", split_axis=1, concat_axis=0, tiled=True),
            lax.all_to_all(keyvals, "mp", split_axis=1, concat_axis=0, tiled=True),
        )
        attended, stored = attend(query_heads, pair_heads)
        head_rows = lax.all_to_all(attended, "mp", split_axis=0, concat_axis=1, tiled=True).reshape(
            head_slice * HEADS, ROWS
        )
    n_att = head_rows.shape[0]
    both_all = lax.all_gather(
        jnp.concatenate([head_rows, up_output], axis=0), "dp", axis=1, tiled=True
    )
    head_rows_all, up_output_all = both_all[:n_att], both_all[n_att:]
    branch = lax.dot_general(
        head_rows_all, head_flat, contract_rows, preferred_element_type=jnp.float32
    ) + lax.dot_general(up_output_all, down_weight, contract_rows, preferred_element_type=jnp.float32)
    branch_local = gather_quarter_exchange(branch, rows)
    mixed = (widened + branch_local).astype(jnp.bfloat16)

    down_grad = blockwise_grad(up_output_all, cot_all, n_dp)
    head_grad = blockwise_grad(head_rows_all, cot_all, n_dp)
    back = jnp.concatenate(
        [
            lax.dot_general(head_flat, cot_later, contract_cols, preferred_element_type=jnp.float32),
            lax.dot_general(down_weight, cot_later, contract_cols, preferred_element_type=jnp.float32),
        ],
        axis=0,
    )
    back = lax.psum_scatter(back, "dp", scatter_dimension=1, tiled=True)
    up_upstream = (back[n_att:] * gelu_slope).astype(jnp.bfloat16)
    head_upstream = back[:n_att].astype(jnp.bfloat16).reshape(head_slice, HEADS, ROWS)
    if by_head:
        upstream = lax.all_to_all(
            head_upstream, "mp", split_axis=1, concat_axis=0, tiled=True
        ).reshape(HS, head_group * QB, TQ)
        query_grad, pair_grad = attend_back(upstream, stored)
        pair_sum = jnp.sum(
            pair_grad.reshape(HS, head_group, QB, 2, PATCHES).astype(jnp.float32), axis=2
        ).astype(jnp.bfloat16)
        grads = jnp.stack(
            [query_grad.reshape(HS, head_group, ROWS), pair_sum[:, :, 0], pair_sum[:, :, 1]]
        )
        proj_grad = lax.all_to_all(grads, "mp", split_axis=1, concat_axis=2, tiled=True)
    else:
        upstream = lax.all_to_all(
            head_upstream.reshape(head_slice, ITEMS, TQ), "mp", split_axis=1, concat_axis=0, tiled=True
        )
        query_grad, pair_grad = attend_back(upstream, stored)
        query_local, pair_local = (
            lax.all_to_all(query_grad, "mp", split_axis=0, concat_axis=1, tiled=True),
            lax.all_to_all(pair_grad, "mp", split_axis=0, concat_axis=1, tiled=True),
        )
        proj_grad = jnp.concatenate(
            [query_local.reshape(1, head_slice, HEADS, ROWS), from_items(pair_local)], axis=0
        )
    proj_grad = proj_grad.reshape(3 * head_slice * HEADS, ROWS)
    grads_all = lax.all_gather(
        jnp.concatenate([proj_grad, up_upstream], axis=0), "dp", axis=1, tiled=True
    )
    proj_grad_all, up_upstream_all = grads_all[:n_proj], grads_all[n_proj:]
    qkv_grad = blockwise_grad(proj_grad_all, hidden_all, n_dp)
    up_grad = blockwise_grad(up_upstream_all, hidden_all, n_dp)
    input_partial = lax.dot_general(
        proj_grad_all, qkv_flat, contract_rows, preferred_element_type=jnp.float32
    ) + lax.dot_general(up_upstream_all, up_weight, contract_rows, preferred_element_type=jnp.float32)
    input_local = gather_quarter_exchange(input_partial, rows)

    scaled = input_local * gain_wide
    plain_sum, cross_sum = lax.psum(
        (jnp.sum(scaled, axis=1), jnp.sum(scaled * normed, axis=1)), "mp"
    )
    tokens_grad = row_scale * (
        scaled - plain_sum[:, None] / D - normed * (cross_sum[:, None] / D)
    )
    tokens_grad = tokens_grad + cotangent.astype(jnp.float32)
    gain_piece = jnp.sum(input_local * normed, axis=0)
    gain_grad = lax.psum(gain_piece, "dp")
    return (
        mixed,
        tokens_grad,
        qkv_grad.reshape(qkv_weight.shape),
        head_grad.reshape(head_weight.shape),
        up_grad,
        down_grad,
        gain_grad,
    )


def solution(mesh):
    in_specs = (
        P("dp", "mp"),
        P("mp"),
        P(None, "mp", None, "dp"),
        P("mp", None, "dp"),
        P("mp", "dp"),
        P("mp", "dp"),
        P("dp", "mp"),
    )
    out_specs = (
        P("dp", "mp"),
        P("dp", "mp"),
        P(None, "mp", None, "dp"),
        P("mp", None, "dp"),
        P("mp", "dp"),
        P("mp", "dp"),
        P("mp"),
    )
    return jax.shard_map(shards, mesh=mesh, in_specs=in_specs, out_specs=out_specs, check_vma=False)
```

```python
import math

import jax
import jax.numpy as jnp
from jax import lax
from jax.sharding import PartitionSpec as P

D = 6144
HEADS = 24
HS = 128
PATCHES = 128
QB = 8
IMG_DP = 1
ROWS = 128
TQ = 16
ITEMS = 192


epsilon = 1e-06
contract_rows = (((0,), (0,)), ((), ()))
contract_cols = (((1,), (1,)), ((), ()))


def gelu_pair(inputs):
    normal_cdf = 0.5 * (1.0 + jax.scipy.special.erf(inputs * 0.7071067811865476))
    density = jnp.exp(-0.5 * inputs * inputs) * 0.3989422804014327
    return (inputs * normal_cdf, normal_cdf + inputs * density)


def head_norm(values):
    center = values - jnp.mean(values, axis=0, keepdims=True)
    inverse = lax.rsqrt(jnp.mean(center * center, axis=0, keepdims=True) + epsilon)
    return (center * inverse, inverse)


def norm_back(upstream, normed, inverse):
    return inverse * (
        upstream
        - jnp.mean(upstream, axis=0, keepdims=True)
        - normed * jnp.mean(upstream * normed, axis=0, keepdims=True)
    )


def to_items(pair_rows):
    depth = pair_rows.shape[1]
    shaped = pair_rows.reshape(2, depth, HEADS, IMG_DP, 1, PATCHES)
    spread = jnp.broadcast_to(shaped, (2, depth, HEADS, IMG_DP, QB, PATCHES))
    return jnp.transpose(spread, (1, 2, 3, 4, 0, 5)).reshape(depth, HEADS * IMG_DP * QB, 2, PATCHES)


def from_items(pair_items):
    depth = pair_items.shape[0]
    shaped = pair_items.reshape(depth, HEADS, IMG_DP, QB, 2, PATCHES)
    summed = jnp.sum(shaped.astype(jnp.float32), axis=3).astype(jnp.bfloat16)
    return jnp.transpose(summed, (3, 0, 1, 2, 4)).reshape(2, depth, HEADS, IMG_DP * PATCHES)


def attend(queries, keyvals):
    query_hat, query_scale = head_norm(queries.astype(jnp.float32))
    key_hat, key_scale = head_norm(keyvals[:, :, 0].astype(jnp.float32))
    query_norm = query_hat.astype(jnp.bfloat16)
    key_norm = key_hat.astype(jnp.bfloat16)
    factor = 1.0 / math.sqrt(queries.shape[0])
    scores = (
        jnp.einsum("cia,cib->iab", query_norm, key_norm, preferred_element_type=jnp.float32)
        * factor
    )
    raised = jnp.exp(scores)
    shares = raised / jnp.sum(raised, axis=2, keepdims=True)
    rounded = shares.astype(jnp.bfloat16)
    values = keyvals[:, :, 1]
    attended = jnp.einsum(
        "iab,cib->cia", rounded, values, preferred_element_type=jnp.float32
    ).astype(jnp.bfloat16)
    stored = (
        query_hat,
        query_scale,
        key_hat,
        key_scale,
        query_norm,
        key_norm,
        shares,
        rounded,
        values,
    )
    return (attended, stored)


def attend_back(upstream, stored):
    query_hat, query_scale, key_hat, key_scale, query_norm, key_norm, shares, rounded, values = (
        stored
    )
    factor = 1.0 / math.sqrt(upstream.shape[0])
    share_grad = jnp.einsum("cia,cib->iab", upstream, values, preferred_element_type=jnp.float32)
    value_grad = jnp.einsum("iab,cia->cib", rounded, upstream, preferred_element_type=jnp.float32)
    score_grad = (
        shares * (share_grad - jnp.sum(shares * share_grad, axis=2, keepdims=True)) * factor
    ).astype(jnp.bfloat16)
    query_back = jnp.einsum(
        "iab,cib->cia", score_grad, key_norm, preferred_element_type=jnp.float32
    )
    key_back = jnp.einsum(
        "iab,cia->cib", score_grad, query_norm, preferred_element_type=jnp.float32
    )
    query_grad = norm_back(query_back, query_hat, query_scale).astype(jnp.bfloat16)
    key_grad = norm_back(key_back, key_hat, key_scale).astype(jnp.bfloat16)
    pair_grad = jnp.stack([key_grad, value_grad.astype(jnp.bfloat16)], axis=2)
    return (query_grad, pair_grad)


def swap_pairs(n_dp, n_mp):
    ratio = n_mp // n_dp
    pairs = []
    for row in range(n_dp):
        for col in range(n_mp):
            owner, part = divmod(col, ratio)
            pairs.append((row * n_mp + col, owner * n_mp + row * ratio + part))
    return pairs


def swap(block):
    n_dp, n_mp = lax.axis_size("dp"), lax.axis_size("mp")
    return lax.ppermute(block, ("dp", "mp"), swap_pairs(n_dp, n_mp))


def spread_quarter(block):
    n_dp, n_mp = lax.axis_size("dp"), lax.axis_size("mp")
    ratio = n_mp // n_dp
    rows, width = block.shape
    copies = jnp.broadcast_to(swap(block)[None], (n_mp, rows, width))
    pieces = lax.all_to_all(copies, "mp", split_axis=0, concat_axis=0, tiled=True)
    pieces = pieces.reshape(n_dp, ratio, rows, width)
    return jnp.transpose(pieces, (0, 2, 1, 3)).reshape(n_dp * rows, ratio * width)


def gather_quarter(partial, rows):
    n_dp, n_mp = lax.axis_size("dp"), lax.axis_size("mp")
    ratio = n_mp // n_dp
    width = partial.shape[1] // ratio
    pieces = partial.reshape(n_dp, rows, ratio, width)
    pieces = jnp.transpose(pieces, (0, 2, 1, 3)).reshape(n_mp, rows, width)
    summed = lax.psum_scatter(pieces, "mp", scatter_dimension=0, tiled=True)
    return swap(summed.reshape(rows, width))


def gather_quarter_exchange(partial, rows):
    n_dp, n_mp = lax.axis_size("dp"), lax.axis_size("mp")
    ratio = n_mp // n_dp
    width = partial.shape[1] // ratio
    pieces = partial.reshape(n_dp, rows, ratio, width)
    pieces = jnp.transpose(pieces, (0, 2, 1, 3)).reshape(n_mp, rows, width)
    received = lax.all_to_all(pieces, "mp", split_axis=0, concat_axis=0, tiled=True)
    return swap(jnp.sum(received, axis=0))


def blockwise_grad(left, right, n_blocks):
    rows = left.shape[1] // n_blocks
    total = None
    for block in range(n_blocks):
        piece = jnp.dot(
            left[:, block * rows:(block + 1) * rows],
            right[block * rows:(block + 1) * rows],
            preferred_element_type=jnp.float32,
        ).astype(jnp.bfloat16).astype(jnp.float32)
        total = piece if total is None else total + piece
    return total.astype(jnp.bfloat16)


def shards(tokens, norm_gain, qkv_weight, head_weight, up_weight, down_weight, cotangent):
    n_dp, n_mp = lax.axis_size("dp"), lax.axis_size("mp")
    head_slice = HS // n_mp
    quarter = qkv_weight.shape[-1]
    rows, width = tokens.shape
    qkv_flat = qkv_weight.reshape(-1, quarter)
    head_flat = head_weight.reshape(-1, quarter)

    widened = tokens.astype(jnp.float32)
    block_mean = jnp.mean(widened, axis=1)
    block_center = widened - block_mean[:, None]
    block_m2 = jnp.sum(block_center * block_center, axis=1)
    stats = lax.all_gather(jnp.stack([block_mean, block_m2]), "mp", axis=0, tiled=False)
    row_mean = jnp.mean(stats[:, 0], axis=0)
    spread = stats[:, 0] - row_mean[None, :]
    row_m2 = jnp.sum(stats[:, 1], axis=0) + width * jnp.sum(spread * spread, axis=0)
    row_scale = lax.rsqrt(row_m2 / D + epsilon)[:, None]
    normed = (widened - row_mean[:, None]) * row_scale
    gain_wide = norm_gain.astype(jnp.float32)
    hidden_local = (normed * gain_wide).astype(jnp.bfloat16)
    hidden_all = spread_quarter(hidden_local)
    cot_all = spread_quarter(cotangent)

    n_proj = qkv_flat.shape[0]
    proj_up = jnp.concatenate(
        [
            lax.dot_general(qkv_flat, hidden_all, contract_cols, preferred_element_type=jnp.float32),
            lax.dot_general(up_weight, hidden_all, contract_cols, preferred_element_type=jnp.float32),
        ],
        axis=0,
    )
    proj_up = lax.psum_scatter(proj_up, "dp", scatter_dimension=1, tiled=True)
    cot_later, proj_up = lax.optimization_barrier((cot_all, proj_up))
    projected = proj_up[:n_proj].astype(jnp.bfloat16).reshape(3, head_slice, HEADS, ROWS)
    up_input = proj_up[n_proj:]
    activated, gelu_slope = gelu_pair(up_input)
    up_output = activated.astype(jnp.bfloat16)

    by_head = HEADS % n_mp == 0
    if by_head:
        head_group = HEADS // n_mp
        qkv_heads = lax.all_to_all(projected, "mp", split_axis=2, concat_axis=1, tiled=True)
        query_heads = qkv_heads[0].reshape(HS, head_group * QB, TQ)
        pairs = jnp.stack([qkv_heads[1], qkv_heads[2]], axis=2)
        pair_heads = jnp.broadcast_to(
            pairs[:, :, None], (HS, head_group, QB, 2, PATCHES)
        ).reshape(HS, head_group * QB, 2, PATCHES)
        attended, stored = attend(query_heads, pair_heads)
        head_rows = lax.all_to_all(
            attended.reshape(HS, head_group, ROWS), "mp", split_axis=0, concat_axis=1, tiled=True
        ).reshape(head_slice * HEADS, ROWS)
    else:
        queries = projected[0].reshape(head_slice, ITEMS, TQ)
        keyvals = to_items(projected[1:])
        query_heads, pair_heads = (
            lax.all_to_all(queries, "mp", split_axis=1, concat_axis=0, tiled=True),
            lax.all_to_all(keyvals, "mp", split_axis=1, concat_axis=0, tiled=True),
        )
        attended, stored = attend(query_heads, pair_heads)
        head_rows = lax.all_to_all(attended, "mp", split_axis=0, concat_axis=1, tiled=True).reshape(
            head_slice * HEADS, ROWS
        )
    n_att = head_rows.shape[0]
    both_all = lax.all_gather(
        jnp.concatenate([head_rows, up_output], axis=0), "dp", axis=1, tiled=True
    )
    head_rows_all, up_output_all = both_all[:n_att], both_all[n_att:]
    branch = lax.dot_general(
        head_rows_all, head_flat, contract_rows, preferred_element_type=jnp.float32
    ) + lax.dot_general(up_output_all, down_weight, contract_rows, preferred_element_type=jnp.float32)
    branch_local = gather_quarter(branch, rows)
    mixed = (widened + branch_local).astype(jnp.bfloat16)

    down_grad = blockwise_grad(up_output_all, cot_all, n_dp)
    head_grad = blockwise_grad(head_rows_all, cot_all, n_dp)
    back = jnp.concatenate(
        [
            lax.dot_general(head_flat, cot_later, contract_cols, preferred_element_type=jnp.float32),
            lax.dot_general(down_weight, cot_later, contract_cols, preferred_element_type=jnp.float32),
        ],
        axis=0,
    )
    back = lax.psum_scatter(back, "dp", scatter_dimension=1, tiled=True)
    up_upstream = (back[n_att:] * gelu_slope).astype(jnp.bfloat16)
    head_upstream = back[:n_att].astype(jnp.bfloat16).reshape(head_slice, HEADS, ROWS)
    if by_head:
        upstream = lax.all_to_all(
            head_upstream, "mp", split_axis=1, concat_axis=0, tiled=True
        ).reshape(HS, head_group * QB, TQ)
        query_grad, pair_grad = attend_back(upstream, stored)
        pair_sum = jnp.sum(
            pair_grad.reshape(HS, head_group, QB, 2, PATCHES).astype(jnp.float32), axis=2
        ).astype(jnp.bfloat16)
        grads = jnp.stack(
            [query_grad.reshape(HS, head_group, ROWS), pair_sum[:, :, 0], pair_sum[:, :, 1]]
        )
        proj_grad = lax.all_to_all(grads, "mp", split_axis=1, concat_axis=2, tiled=True)
    else:
        upstream = lax.all_to_all(
            head_upstream.reshape(head_slice, ITEMS, TQ), "mp", split_axis=1, concat_axis=0, tiled=True
        )
        query_grad, pair_grad = attend_back(upstream, stored)
        query_local, pair_local = (
            lax.all_to_all(query_grad, "mp", split_axis=0, concat_axis=1, tiled=True),
            lax.all_to_all(pair_grad, "mp", split_axis=0, concat_axis=1, tiled=True),
        )
        proj_grad = jnp.concatenate(
            [query_local.reshape(1, head_slice, HEADS, ROWS), from_items(pair_local)], axis=0
        )
    proj_grad = proj_grad.reshape(3 * head_slice * HEADS, ROWS)
    grads_all = lax.all_gather(
        jnp.concatenate([proj_grad, up_upstream], axis=0), "dp", axis=1, tiled=True
    )
    proj_grad_all, up_upstream_all = grads_all[:n_proj], grads_all[n_proj:]
    qkv_grad = blockwise_grad(proj_grad_all, hidden_all, n_dp)
    up_grad = blockwise_grad(up_upstream_all, hidden_all, n_dp)
    input_partial = lax.dot_general(
        proj_grad_all, qkv_flat, contract_rows, preferred_element_type=jnp.float32
    ) + lax.dot_general(up_upstream_all, up_weight, contract_rows, preferred_element_type=jnp.float32)
    input_local = gather_quarter_exchange(input_partial, rows)

    scaled = input_local * gain_wide
    plain_sum, cross_sum = lax.psum(
        (jnp.sum(scaled, axis=1), jnp.sum(scaled * normed, axis=1)), "mp"
    )
    tokens_grad = row_scale * (
        scaled - plain_sum[:, None] / D - normed * (cross_sum[:, None] / D)
    )
    tokens_grad = tokens_grad + cotangent.astype(jnp.float32)
    gain_piece = jnp.sum(input_local * normed, axis=0)
    gain_grad = lax.psum(gain_piece, "dp")
    return (
        mixed,
        tokens_grad,
        qkv_grad.reshape(qkv_weight.shape),
        head_grad.reshape(head_weight.shape),
        up_grad,
        down_grad,
        gain_grad,
    )


def solution(mesh):
    in_specs = (
        P("dp", "mp"),
        P("mp"),
        P(None, "mp", None, "dp"),
        P("mp", None, "dp"),
        P("mp", "dp"),
        P("mp", "dp"),
        P("dp", "mp"),
    )
    out_specs = (
        P("dp", "mp"),
        P("dp", "mp"),
        P(None, "mp", None, "dp"),
        P("mp", None, "dp"),
        P("mp", "dp"),
        P("mp", "dp"),
        P("mp"),
    )
    return jax.shard_map(shards, mesh=mesh, in_specs=in_specs, out_specs=out_specs, check_vma=False)
```

```python
import math

import jax
import jax.numpy as jnp
from jax import lax
from jax.sharding import PartitionSpec as P

D = 6144
HEADS = 24
HS = 128
PATCHES = 128
QB = 8
IMG_DP = 1
ROWS = 128
TQ = 16
ITEMS = 192


epsilon = 1e-06
contract_rows = (((0,), (0,)), ((), ()))
contract_cols = (((1,), (1,)), ((), ()))


def gelu_pair(inputs):
    normal_cdf = 0.5 * (1.0 + jax.scipy.special.erf(inputs * 0.7071067811865476))
    density = jnp.exp(-0.5 * inputs * inputs) * 0.3989422804014327
    return (inputs * normal_cdf, normal_cdf + inputs * density)


def head_norm(values):
    center = values - jnp.mean(values, axis=0, keepdims=True)
    inverse = lax.rsqrt(jnp.mean(center * center, axis=0, keepdims=True) + epsilon)
    return (center * inverse, inverse)


def norm_back(upstream, normed, inverse):
    return inverse * (
        upstream
        - jnp.mean(upstream, axis=0, keepdims=True)
        - normed * jnp.mean(upstream * normed, axis=0, keepdims=True)
    )


def to_items(pair_rows):
    depth = pair_rows.shape[1]
    shaped = pair_rows.reshape(2, depth, HEADS, IMG_DP, 1, PATCHES)
    spread = jnp.broadcast_to(shaped, (2, depth, HEADS, IMG_DP, QB, PATCHES))
    return jnp.transpose(spread, (1, 2, 3, 4, 0, 5)).reshape(depth, HEADS * IMG_DP * QB, 2, PATCHES)


def from_items(pair_items):
    depth = pair_items.shape[0]
    shaped = pair_items.reshape(depth, HEADS, IMG_DP, QB, 2, PATCHES)
    summed = jnp.sum(shaped.astype(jnp.float32), axis=3).astype(jnp.bfloat16)
    return jnp.transpose(summed, (3, 0, 1, 2, 4)).reshape(2, depth, HEADS, IMG_DP * PATCHES)


def attend(queries, keyvals):
    query_hat, query_scale = head_norm(queries.astype(jnp.float32))
    key_hat, key_scale = head_norm(keyvals[:, :, 0].astype(jnp.float32))
    query_norm = query_hat.astype(jnp.bfloat16)
    key_norm = key_hat.astype(jnp.bfloat16)
    factor = 1.0 / math.sqrt(queries.shape[0])
    scores = (
        jnp.einsum("cia,cib->iab", query_norm, key_norm, preferred_element_type=jnp.float32)
        * factor
    )
    raised = jnp.exp(scores)
    shares = raised / jnp.sum(raised, axis=2, keepdims=True)
    rounded = shares.astype(jnp.bfloat16)
    values = keyvals[:, :, 1]
    attended = jnp.einsum(
        "iab,cib->cia", rounded, values, preferred_element_type=jnp.float32
    ).astype(jnp.bfloat16)
    stored = (
        query_hat,
        query_scale,
        key_hat,
        key_scale,
        query_norm,
        key_norm,
        shares,
        rounded,
        values,
    )
    return (attended, stored)


def attend_back(upstream, stored):
    query_hat, query_scale, key_hat, key_scale, query_norm, key_norm, shares, rounded, values = (
        stored
    )
    factor = 1.0 / math.sqrt(upstream.shape[0])
    share_grad = jnp.einsum("cia,cib->iab", upstream, values, preferred_element_type=jnp.float32)
    value_grad = jnp.einsum("iab,cia->cib", rounded, upstream, preferred_element_type=jnp.float32)
    score_grad = (
        shares * (share_grad - jnp.sum(shares * share_grad, axis=2, keepdims=True)) * factor
    ).astype(jnp.bfloat16)
    query_back = jnp.einsum(
        "iab,cib->cia", score_grad, key_norm, preferred_element_type=jnp.float32
    )
    key_back = jnp.einsum(
        "iab,cia->cib", score_grad, query_norm, preferred_element_type=jnp.float32
    )
    query_grad = norm_back(query_back, query_hat, query_scale).astype(jnp.bfloat16)
    key_grad = norm_back(key_back, key_hat, key_scale).astype(jnp.bfloat16)
    pair_grad = jnp.stack([key_grad, value_grad.astype(jnp.bfloat16)], axis=2)
    return (query_grad, pair_grad)


def swap_pairs(n_dp, n_mp):
    ratio = n_mp // n_dp
    pairs = []
    for row in range(n_dp):
        for col in range(n_mp):
            owner, part = divmod(col, ratio)
            pairs.append((row * n_mp + col, owner * n_mp + row * ratio + part))
    return pairs


def swap(block):
    n_dp, n_mp = lax.axis_size("dp"), lax.axis_size("mp")
    return lax.ppermute(block, ("dp", "mp"), swap_pairs(n_dp, n_mp))


def spread_quarter(block):
    n_dp, n_mp = lax.axis_size("dp"), lax.axis_size("mp")
    ratio = n_mp // n_dp
    rows, width = block.shape
    copies = jnp.broadcast_to(swap(block)[None], (n_mp, rows, width))
    pieces = lax.all_to_all(copies, "mp", split_axis=0, concat_axis=0, tiled=True)
    pieces = pieces.reshape(n_dp, ratio, rows, width)
    return jnp.transpose(pieces, (0, 2, 1, 3)).reshape(n_dp * rows, ratio * width)


def gather_quarter(partial, rows):
    n_dp, n_mp = lax.axis_size("dp"), lax.axis_size("mp")
    ratio = n_mp // n_dp
    width = partial.shape[1] // ratio
    pieces = partial.reshape(n_dp, rows, ratio, width)
    pieces = jnp.transpose(pieces, (0, 2, 1, 3)).reshape(n_mp, rows, width)
    summed = lax.psum_scatter(pieces, "mp", scatter_dimension=0, tiled=True)
    return swap(summed.reshape(rows, width))


def gather_quarter_exchange(partial, rows):
    n_dp, n_mp = lax.axis_size("dp"), lax.axis_size("mp")
    ratio = n_mp // n_dp
    width = partial.shape[1] // ratio
    pieces = partial.reshape(n_dp, rows, ratio, width)
    pieces = jnp.transpose(pieces, (0, 2, 1, 3)).reshape(n_mp, rows, width)
    received = lax.all_to_all(pieces, "mp", split_axis=0, concat_axis=0, tiled=True)
    return swap(jnp.sum(received, axis=0))


def blockwise_grad(left, right, n_blocks):
    rows = left.shape[1] // n_blocks
    total = None
    for block in range(n_blocks):
        piece = jnp.dot(
            left[:, block * rows:(block + 1) * rows],
            right[block * rows:(block + 1) * rows],
            preferred_element_type=jnp.float32,
        ).astype(jnp.bfloat16).astype(jnp.float32)
        total = piece if total is None else total + piece
    return total.astype(jnp.bfloat16)


def shards(tokens, norm_gain, qkv_weight, head_weight, up_weight, down_weight, cotangent):
    n_dp, n_mp = lax.axis_size("dp"), lax.axis_size("mp")
    head_slice = HS // n_mp
    quarter = qkv_weight.shape[-1]
    rows, width = tokens.shape
    qkv_flat = qkv_weight.reshape(-1, quarter)
    head_flat = head_weight.reshape(-1, quarter)

    widened = tokens.astype(jnp.float32)
    block_mean = jnp.mean(widened, axis=1)
    block_center = widened - block_mean[:, None]
    block_m2 = jnp.sum(block_center * block_center, axis=1)
    gain_wide = norm_gain.astype(jnp.float32)
    packed = jnp.concatenate([block_mean, block_m2, gain_wide])
    gathered = lax.all_gather(packed, ("dp", "mp"), axis=0, tiled=False)
    gathered = gathered.reshape(n_dp, n_mp, -1)
    means = gathered[:, :, :rows]
    mean_all = jnp.mean(means, axis=1)
    spread = means - mean_all[:, None, :]
    m2_all = jnp.sum(gathered[:, :, rows:2 * rows], axis=1) + width * jnp.sum(spread * spread, axis=1)
    scale_all = lax.rsqrt(m2_all / D + epsilon)
    me = lax.axis_index("dp")
    row_mean = lax.dynamic_index_in_dim(mean_all, me, 0, keepdims=False)[:, None]
    row_scale = lax.dynamic_index_in_dim(scale_all, me, 0, keepdims=False)[:, None]
    normed = (widened - row_mean) * row_scale
    gain_quarter = lax.dynamic_slice_in_dim(
        gathered[0, :, 2 * rows:].reshape(-1), me * quarter, quarter
    )
    tokens_all = spread_quarter(tokens).astype(jnp.float32)
    normed_all = (tokens_all - mean_all.reshape(-1, 1)) * scale_all.reshape(-1, 1)
    hidden_all = (normed_all * gain_quarter).astype(jnp.bfloat16)
    cot_all = spread_quarter(cotangent)

    n_proj = qkv_flat.shape[0]
    proj_up = jnp.concatenate(
        [
            lax.dot_general(qkv_flat, hidden_all, contract_cols, preferred_element_type=jnp.float32),
            lax.dot_general(up_weight, hidden_all, contract_cols, preferred_element_type=jnp.float32),
        ],
        axis=0,
    )
    proj_up = lax.psum_scatter(proj_up, "dp", scatter_dimension=1, tiled=True)
    cot_later, proj_up = lax.optimization_barrier((cot_all, proj_up))
    projected = proj_up[:n_proj].astype(jnp.bfloat16).reshape(3, head_slice, HEADS, ROWS)
    up_input = proj_up[n_proj:]
    activated, gelu_slope = gelu_pair(up_input)
    up_output = activated.astype(jnp.bfloat16)

    by_head = HEADS % n_mp == 0
    if by_head:
        head_group = HEADS // n_mp
        qkv_heads = lax.all_to_all(projected, "mp", split_axis=2, concat_axis=1, tiled=True)
        query_heads = qkv_heads[0].reshape(HS, head_group * QB, TQ)
        pairs = jnp.stack([qkv_heads[1], qkv_heads[2]], axis=2)
        pair_heads = jnp.broadcast_to(
            pairs[:, :, None], (HS, head_group, QB, 2, PATCHES)
        ).reshape(HS, head_group * QB, 2, PATCHES)
        attended, stored = attend(query_heads, pair_heads)
        head_rows = lax.all_to_all(
            attended.reshape(HS, head_group, ROWS), "mp", split_axis=0, concat_axis=1, tiled=True
        ).reshape(head_slice * HEADS, ROWS)
    else:
        queries = projected[0].reshape(head_slice, ITEMS, TQ)
        keyvals = to_items(projected[1:])
        query_heads, pair_heads = (
            lax.all_to_all(queries, "mp", split_axis=1, concat_axis=0, tiled=True),
            lax.all_to_all(keyvals, "mp", split_axis=1, concat_axis=0, tiled=True),
        )
        attended, stored = attend(query_heads, pair_heads)
        head_rows = lax.all_to_all(attended, "mp", split_axis=0, concat_axis=1, tiled=True).reshape(
            head_slice * HEADS, ROWS
        )
    n_att = head_rows.shape[0]
    both_all = lax.all_gather(
        jnp.concatenate([head_rows, up_output], axis=0), "dp", axis=1, tiled=True
    )
    head_rows_all, up_output_all = both_all[:n_att], both_all[n_att:]
    branch = lax.dot_general(
        head_rows_all, head_flat, contract_rows, preferred_element_type=jnp.float32
    ) + lax.dot_general(up_output_all, down_weight, contract_rows, preferred_element_type=jnp.float32)
    branch_local = gather_quarter(branch, rows)
    mixed = (widened + branch_local).astype(jnp.bfloat16)

    down_grad = blockwise_grad(up_output_all, cot_all, n_dp)
    head_grad = blockwise_grad(head_rows_all, cot_all, n_dp)
    back = jnp.concatenate(
        [
            lax.dot_general(head_flat, cot_later, contract_cols, preferred_element_type=jnp.float32),
            lax.dot_general(down_weight, cot_later, contract_cols, preferred_element_type=jnp.float32),
        ],
        axis=0,
    )
    back = lax.psum_scatter(back, "dp", scatter_dimension=1, tiled=True)
    up_upstream = (back[n_att:] * gelu_slope).astype(jnp.bfloat16)
    head_upstream = back[:n_att].astype(jnp.bfloat16).reshape(head_slice, HEADS, ROWS)
    if by_head:
        upstream = lax.all_to_all(
            head_upstream, "mp", split_axis=1, concat_axis=0, tiled=True
        ).reshape(HS, head_group * QB, TQ)
        query_grad, pair_grad = attend_back(upstream, stored)
        pair_sum = jnp.sum(
            pair_grad.reshape(HS, head_group, QB, 2, PATCHES).astype(jnp.float32), axis=2
        ).astype(jnp.bfloat16)
        grads = jnp.stack(
            [query_grad.reshape(HS, head_group, ROWS), pair_sum[:, :, 0], pair_sum[:, :, 1]]
        )
        proj_grad = lax.all_to_all(grads, "mp", split_axis=1, concat_axis=2, tiled=True)
    else:
        upstream = lax.all_to_all(
            head_upstream.reshape(head_slice, ITEMS, TQ), "mp", split_axis=1, concat_axis=0, tiled=True
        )
        query_grad, pair_grad = attend_back(upstream, stored)
        query_local, pair_local = (
            lax.all_to_all(query_grad, "mp", split_axis=0, concat_axis=1, tiled=True),
            lax.all_to_all(pair_grad, "mp", split_axis=0, concat_axis=1, tiled=True),
        )
        proj_grad = jnp.concatenate(
            [query_local.reshape(1, head_slice, HEADS, ROWS), from_items(pair_local)], axis=0
        )
    proj_grad = proj_grad.reshape(3 * head_slice * HEADS, ROWS)
    grads_all = lax.all_gather(
        jnp.concatenate([proj_grad, up_upstream], axis=0), "dp", axis=1, tiled=True
    )
    proj_grad_all, up_upstream_all = grads_all[:n_proj], grads_all[n_proj:]
    qkv_grad = blockwise_grad(proj_grad_all, hidden_all, n_dp)
    up_grad = blockwise_grad(up_upstream_all, hidden_all, n_dp)
    input_partial = lax.dot_general(
        proj_grad_all, qkv_flat, contract_rows, preferred_element_type=jnp.float32
    ) + lax.dot_general(up_upstream_all, up_weight, contract_rows, preferred_element_type=jnp.float32)
    scaled_partial = input_partial * gain_quarter
    row_sums = lax.psum(
        jnp.stack(
            [jnp.sum(scaled_partial, axis=1), jnp.sum(scaled_partial * normed_all, axis=1)]
        ),
        ("dp", "mp"),
    )
    row_sums = lax.dynamic_slice_in_dim(row_sums, me * rows, rows, 1)
    plain_sum, cross_sum = row_sums[0], row_sums[1]
    input_local = gather_quarter_exchange(input_partial, rows)

    scaled = input_local * gain_wide
    tokens_grad = row_scale * (
        scaled - plain_sum[:, None] / D - normed * (cross_sum[:, None] / D)
    )
    tokens_grad = tokens_grad + cotangent.astype(jnp.float32)
    gain_piece = jnp.sum(input_local * normed, axis=0)
    gain_grad = lax.psum(gain_piece, "dp")
    return (
        mixed,
        tokens_grad,
        qkv_grad.reshape(qkv_weight.shape),
        head_grad.reshape(head_weight.shape),
        up_grad,
        down_grad,
        gain_grad,
    )


def solution(mesh):
    in_specs = (
        P("dp", "mp"),
        P("mp"),
        P(None, "mp", None, "dp"),
        P("mp", None, "dp"),
        P("mp", "dp"),
        P("mp", "dp"),
        P("dp", "mp"),
    )
    out_specs = (
        P("dp", "mp"),
        P("dp", "mp"),
        P(None, "mp", None, "dp"),
        P("mp", None, "dp"),
        P("mp", "dp"),
        P("mp", "dp"),
        P("mp"),
    )
    return jax.shard_map(shards, mesh=mesh, in_specs=in_specs, out_specs=out_specs, check_vma=False)
```

```python
import math

import jax
import jax.numpy as jnp
from jax import lax
from jax.sharding import PartitionSpec as P

D = 6144
HEADS = 24
HS = 128
PATCHES = 128
QB = 8
IMG_DP = 1
ROWS = 128
TQ = 16
ITEMS = 192


epsilon = 1e-06
contract_rows = (((0,), (0,)), ((), ()))
contract_cols = (((1,), (1,)), ((), ()))


def gelu_pair(inputs):
    normal_cdf = 0.5 * (1.0 + jax.scipy.special.erf(inputs * 0.7071067811865476))
    density = jnp.exp(-0.5 * inputs * inputs) * 0.3989422804014327
    return (inputs * normal_cdf, normal_cdf + inputs * density)


def head_norm(values):
    center = values - jnp.mean(values, axis=0, keepdims=True)
    inverse = lax.rsqrt(jnp.mean(center * center, axis=0, keepdims=True) + epsilon)
    return (center * inverse, inverse)


def norm_back(upstream, normed, inverse):
    return inverse * (
        upstream
        - jnp.mean(upstream, axis=0, keepdims=True)
        - normed * jnp.mean(upstream * normed, axis=0, keepdims=True)
    )


def to_items(pair_rows):
    depth = pair_rows.shape[1]
    shaped = pair_rows.reshape(2, depth, HEADS, IMG_DP, 1, PATCHES)
    spread = jnp.broadcast_to(shaped, (2, depth, HEADS, IMG_DP, QB, PATCHES))
    return jnp.transpose(spread, (1, 2, 3, 4, 0, 5)).reshape(depth, HEADS * IMG_DP * QB, 2, PATCHES)


def from_items(pair_items):
    depth = pair_items.shape[0]
    shaped = pair_items.reshape(depth, HEADS, IMG_DP, QB, 2, PATCHES)
    summed = jnp.sum(shaped.astype(jnp.float32), axis=3).astype(jnp.bfloat16)
    return jnp.transpose(summed, (3, 0, 1, 2, 4)).reshape(2, depth, HEADS, IMG_DP * PATCHES)


def attend(queries, keyvals):
    query_hat, query_scale = head_norm(queries.astype(jnp.float32))
    key_hat, key_scale = head_norm(keyvals[:, :, 0].astype(jnp.float32))
    query_norm = query_hat.astype(jnp.bfloat16)
    key_norm = key_hat.astype(jnp.bfloat16)
    factor = 1.0 / math.sqrt(queries.shape[0])
    scores = (
        jnp.einsum("cia,cib->iab", query_norm, key_norm, preferred_element_type=jnp.float32)
        * factor
    )
    raised = jnp.exp(scores)
    shares = raised / jnp.sum(raised, axis=2, keepdims=True)
    rounded = shares.astype(jnp.bfloat16)
    values = keyvals[:, :, 1]
    attended = jnp.einsum(
        "iab,cib->cia", rounded, values, preferred_element_type=jnp.float32
    ).astype(jnp.bfloat16)
    stored = (
        query_hat,
        query_scale,
        key_hat,
        key_scale,
        query_norm,
        key_norm,
        shares,
        rounded,
        values,
    )
    return (attended, stored)


def attend_back(upstream, stored):
    query_hat, query_scale, key_hat, key_scale, query_norm, key_norm, shares, rounded, values = (
        stored
    )
    factor = 1.0 / math.sqrt(upstream.shape[0])
    share_grad = jnp.einsum("cia,cib->iab", upstream, values, preferred_element_type=jnp.float32)
    value_grad = jnp.einsum("iab,cia->cib", rounded, upstream, preferred_element_type=jnp.float32)
    score_grad = (
        shares * (share_grad - jnp.sum(shares * share_grad, axis=2, keepdims=True)) * factor
    ).astype(jnp.bfloat16)
    query_back = jnp.einsum(
        "iab,cib->cia", score_grad, key_norm, preferred_element_type=jnp.float32
    )
    key_back = jnp.einsum(
        "iab,cia->cib", score_grad, query_norm, preferred_element_type=jnp.float32
    )
    query_grad = norm_back(query_back, query_hat, query_scale).astype(jnp.bfloat16)
    key_grad = norm_back(key_back, key_hat, key_scale).astype(jnp.bfloat16)
    pair_grad = jnp.stack([key_grad, value_grad.astype(jnp.bfloat16)], axis=2)
    return (query_grad, pair_grad)


def swap_pairs(n_dp, n_mp):
    ratio = n_mp // n_dp
    pairs = []
    for row in range(n_dp):
        for col in range(n_mp):
            owner, part = divmod(col, ratio)
            pairs.append((row * n_mp + col, owner * n_mp + row * ratio + part))
    return pairs


def swap(block):
    n_dp, n_mp = lax.axis_size("dp"), lax.axis_size("mp")
    return lax.ppermute(block, ("dp", "mp"), swap_pairs(n_dp, n_mp))


def spread_quarter(block):
    n_dp, n_mp = lax.axis_size("dp"), lax.axis_size("mp")
    ratio = n_mp // n_dp
    rows, width = block.shape
    copies = jnp.broadcast_to(swap(block)[None], (n_mp, rows, width))
    pieces = lax.all_to_all(copies, "mp", split_axis=0, concat_axis=0, tiled=True)
    pieces = pieces.reshape(n_dp, ratio, rows, width)
    return jnp.transpose(pieces, (0, 2, 1, 3)).reshape(n_dp * rows, ratio * width)


def gather_quarter(partial, rows):
    n_dp, n_mp = lax.axis_size("dp"), lax.axis_size("mp")
    ratio = n_mp // n_dp
    width = partial.shape[1] // ratio
    pieces = partial.reshape(n_dp, rows, ratio, width)
    pieces = jnp.transpose(pieces, (0, 2, 1, 3)).reshape(n_mp, rows, width)
    summed = lax.psum_scatter(pieces, "mp", scatter_dimension=0, tiled=True)
    return swap(summed.reshape(rows, width))


def gather_quarter_exchange(partial, rows):
    n_dp, n_mp = lax.axis_size("dp"), lax.axis_size("mp")
    ratio = n_mp // n_dp
    width = partial.shape[1] // ratio
    pieces = partial.reshape(n_dp, rows, ratio, width)
    pieces = jnp.transpose(pieces, (0, 2, 1, 3)).reshape(n_mp, rows, width)
    received = lax.all_to_all(pieces, "mp", split_axis=0, concat_axis=0, tiled=True)
    return swap(jnp.sum(received, axis=0))


def blockwise_grad(left, right, n_blocks):
    rows = left.shape[1] // n_blocks
    total = None
    for block in range(n_blocks):
        piece = jnp.dot(
            left[:, block * rows:(block + 1) * rows],
            right[block * rows:(block + 1) * rows],
            preferred_element_type=jnp.float32,
        ).astype(jnp.bfloat16).astype(jnp.float32)
        total = piece if total is None else total + piece
    return total.astype(jnp.bfloat16)


def shards(tokens, norm_gain, qkv_weight, head_weight, up_weight, down_weight, cotangent):
    n_dp, n_mp = lax.axis_size("dp"), lax.axis_size("mp")
    head_slice = HS // n_mp
    quarter = qkv_weight.shape[-1]
    rows, width = tokens.shape
    qkv_flat = qkv_weight.reshape(-1, quarter)
    head_flat = head_weight.reshape(-1, quarter)

    widened = tokens.astype(jnp.float32)
    block_mean = jnp.mean(widened, axis=1)
    block_center = widened - block_mean[:, None]
    block_m2 = jnp.sum(block_center * block_center, axis=1)
    gain_wide = norm_gain.astype(jnp.float32)
    packed = jnp.concatenate([block_mean, block_m2, gain_wide])
    stats = lax.all_gather(packed, "mp", axis=0, tiled=False)
    row_mean = jnp.mean(stats[:, :rows], axis=0)
    spread = stats[:, :rows] - row_mean[None, :]
    row_m2 = jnp.sum(stats[:, rows:2 * rows], axis=0) + width * jnp.sum(spread * spread, axis=0)
    row_scale = lax.rsqrt(row_m2 / D + epsilon)
    image_stats = lax.all_gather(jnp.stack([row_mean, row_scale]), "dp", axis=0, tiled=False)
    mean_all = image_stats[:, 0].reshape(-1, 1)
    scale_all = image_stats[:, 1].reshape(-1, 1)
    row_mean, row_scale = row_mean[:, None], row_scale[:, None]
    normed = (widened - row_mean) * row_scale
    gain_quarter = lax.dynamic_slice_in_dim(
        stats[:, 2 * rows:].reshape(-1), lax.axis_index("dp") * quarter, quarter
    )
    tokens_all = spread_quarter(tokens).astype(jnp.float32)
    hidden_all = (((tokens_all - mean_all) * scale_all) * gain_quarter).astype(jnp.bfloat16)
    cot_all = spread_quarter(cotangent)

    n_proj = qkv_flat.shape[0]
    proj_up = jnp.concatenate(
        [
            lax.dot_general(qkv_flat, hidden_all, contract_cols, preferred_element_type=jnp.float32),
            lax.dot_general(up_weight, hidden_all, contract_cols, preferred_element_type=jnp.float32),
        ],
        axis=0,
    )
    proj_up = lax.psum_scatter(proj_up, "dp", scatter_dimension=1, tiled=True)
    cot_later, proj_up = lax.optimization_barrier((cot_all, proj_up))
    projected = proj_up[:n_proj].astype(jnp.bfloat16).reshape(3, head_slice, HEADS, ROWS)
    up_input = proj_up[n_proj:]
    activated, gelu_slope = gelu_pair(up_input)
    up_output = activated.astype(jnp.bfloat16)

    by_head = HEADS % n_mp == 0
    if by_head:
        head_group = HEADS // n_mp
        qkv_heads = lax.all_to_all(projected, "mp", split_axis=2, concat_axis=1, tiled=True)
        query_heads = qkv_heads[0].reshape(HS, head_group * QB, TQ)
        pairs = jnp.stack([qkv_heads[1], qkv_heads[2]], axis=2)
        pair_heads = jnp.broadcast_to(
            pairs[:, :, None], (HS, head_group, QB, 2, PATCHES)
        ).reshape(HS, head_group * QB, 2, PATCHES)
        attended, stored = attend(query_heads, pair_heads)
        head_rows = lax.all_to_all(
            attended.reshape(HS, head_group, ROWS), "mp", split_axis=0, concat_axis=1, tiled=True
        ).reshape(head_slice * HEADS, ROWS)
    else:
        queries = projected[0].reshape(head_slice, ITEMS, TQ)
        keyvals = to_items(projected[1:])
        query_heads, pair_heads = (
            lax.all_to_all(queries, "mp", split_axis=1, concat_axis=0, tiled=True),
            lax.all_to_all(keyvals, "mp", split_axis=1, concat_axis=0, tiled=True),
        )
        attended, stored = attend(query_heads, pair_heads)
        head_rows = lax.all_to_all(attended, "mp", split_axis=0, concat_axis=1, tiled=True).reshape(
            head_slice * HEADS, ROWS
        )
    n_att = head_rows.shape[0]
    both_all = lax.all_gather(
        jnp.concatenate([head_rows, up_output], axis=0), "dp", axis=1, tiled=True
    )
    head_rows_all, up_output_all = both_all[:n_att], both_all[n_att:]
    branch = lax.dot_general(
        head_rows_all, head_flat, contract_rows, preferred_element_type=jnp.float32
    ) + lax.dot_general(up_output_all, down_weight, contract_rows, preferred_element_type=jnp.float32)
    branch_local = gather_quarter(branch, rows)
    mixed = (widened + branch_local).astype(jnp.bfloat16)

    down_grad = blockwise_grad(up_output_all, cot_all, n_dp)
    head_grad = blockwise_grad(head_rows_all, cot_all, n_dp)
    back = jnp.concatenate(
        [
            lax.dot_general(head_flat, cot_later, contract_cols, preferred_element_type=jnp.float32),
            lax.dot_general(down_weight, cot_later, contract_cols, preferred_element_type=jnp.float32),
        ],
        axis=0,
    )
    back = lax.psum_scatter(back, "dp", scatter_dimension=1, tiled=True)
    up_upstream = (back[n_att:] * gelu_slope).astype(jnp.bfloat16)
    head_upstream = back[:n_att].astype(jnp.bfloat16).reshape(head_slice, HEADS, ROWS)
    if by_head:
        upstream = lax.all_to_all(
            head_upstream, "mp", split_axis=1, concat_axis=0, tiled=True
        ).reshape(HS, head_group * QB, TQ)
        query_grad, pair_grad = attend_back(upstream, stored)
        pair_sum = jnp.sum(
            pair_grad.reshape(HS, head_group, QB, 2, PATCHES).astype(jnp.float32), axis=2
        ).astype(jnp.bfloat16)
        grads = jnp.stack(
            [query_grad.reshape(HS, head_group, ROWS), pair_sum[:, :, 0], pair_sum[:, :, 1]]
        )
        proj_grad = lax.all_to_all(grads, "mp", split_axis=1, concat_axis=2, tiled=True)
    else:
        upstream = lax.all_to_all(
            head_upstream.reshape(head_slice, ITEMS, TQ), "mp", split_axis=1, concat_axis=0, tiled=True
        )
        query_grad, pair_grad = attend_back(upstream, stored)
        query_local, pair_local = (
            lax.all_to_all(query_grad, "mp", split_axis=0, concat_axis=1, tiled=True),
            lax.all_to_all(pair_grad, "mp", split_axis=0, concat_axis=1, tiled=True),
        )
        proj_grad = jnp.concatenate(
            [query_local.reshape(1, head_slice, HEADS, ROWS), from_items(pair_local)], axis=0
        )
    proj_grad = proj_grad.reshape(3 * head_slice * HEADS, ROWS)
    grads_all = lax.all_gather(
        jnp.concatenate([proj_grad, up_upstream], axis=0), "dp", axis=1, tiled=True
    )
    proj_grad_all, up_upstream_all = grads_all[:n_proj], grads_all[n_proj:]
    qkv_grad = blockwise_grad(proj_grad_all, hidden_all, n_dp)
    up_grad = blockwise_grad(up_upstream_all, hidden_all, n_dp)
    input_partial = lax.dot_general(
        proj_grad_all, qkv_flat, contract_rows, preferred_element_type=jnp.float32
    ) + lax.dot_general(up_upstream_all, up_weight, contract_rows, preferred_element_type=jnp.float32)
    input_local = gather_quarter_exchange(input_partial, rows)

    scaled = input_local * gain_wide
    plain_sum, cross_sum = lax.psum(
        (jnp.sum(scaled, axis=1), jnp.sum(scaled * normed, axis=1)), "mp"
    )
    tokens_grad = row_scale * (
        scaled - plain_sum[:, None] / D - normed * (cross_sum[:, None] / D)
    )
    tokens_grad = tokens_grad + cotangent.astype(jnp.float32)
    gain_piece = jnp.sum(input_local * normed, axis=0)
    gain_grad = lax.psum(gain_piece, "dp")
    return (
        mixed,
        tokens_grad,
        qkv_grad.reshape(qkv_weight.shape),
        head_grad.reshape(head_weight.shape),
        up_grad,
        down_grad,
        gain_grad,
    )


def solution(mesh):
    in_specs = (
        P("dp", "mp"),
        P("mp"),
        P(None, "mp", None, "dp"),
        P("mp", None, "dp"),
        P("mp", "dp"),
        P("mp", "dp"),
        P("dp", "mp"),
    )
    out_specs = (
        P("dp", "mp"),
        P("dp", "mp"),
        P(None, "mp", None, "dp"),
        P("mp", None, "dp"),
        P("mp", "dp"),
        P("mp", "dp"),
        P("mp"),
    )
    return jax.shard_map(shards, mesh=mesh, in_specs=in_specs, out_specs=out_specs, check_vma=False)
```

```python
import math

import jax
import jax.numpy as jnp
from jax import lax
from jax.sharding import PartitionSpec as P

D = 6144
HEADS = 24
HS = 128
PATCHES = 128
QB = 8
IMG_DP = 1
ROWS = 128
TQ = 16
ITEMS = 192


epsilon = 1e-06
contract_rows = (((0,), (0,)), ((), ()))
contract_cols = (((1,), (1,)), ((), ()))


def gelu_pair(inputs):
    normal_cdf = 0.5 * (1.0 + jax.scipy.special.erf(inputs * 0.7071067811865476))
    density = jnp.exp(-0.5 * inputs * inputs) * 0.3989422804014327
    return (inputs * normal_cdf, normal_cdf + inputs * density)


def head_norm(values):
    center = values - jnp.mean(values, axis=0, keepdims=True)
    inverse = lax.rsqrt(jnp.mean(center * center, axis=0, keepdims=True) + epsilon)
    return (center * inverse, inverse)


def norm_back(upstream, normed, inverse):
    return inverse * (
        upstream
        - jnp.mean(upstream, axis=0, keepdims=True)
        - normed * jnp.mean(upstream * normed, axis=0, keepdims=True)
    )


def to_items(pair_rows):
    depth = pair_rows.shape[1]
    shaped = pair_rows.reshape(2, depth, HEADS, IMG_DP, 1, PATCHES)
    spread = jnp.broadcast_to(shaped, (2, depth, HEADS, IMG_DP, QB, PATCHES))
    return jnp.transpose(spread, (1, 2, 3, 4, 0, 5)).reshape(depth, HEADS * IMG_DP * QB, 2, PATCHES)


def from_items(pair_items):
    depth = pair_items.shape[0]
    shaped = pair_items.reshape(depth, HEADS, IMG_DP, QB, 2, PATCHES)
    summed = jnp.sum(shaped.astype(jnp.float32), axis=3).astype(jnp.bfloat16)
    return jnp.transpose(summed, (3, 0, 1, 2, 4)).reshape(2, depth, HEADS, IMG_DP * PATCHES)


def attend(queries, keyvals):
    query_hat, query_scale = head_norm(queries.astype(jnp.float32))
    key_hat, key_scale = head_norm(keyvals[:, :, 0].astype(jnp.float32))
    query_norm = query_hat.astype(jnp.bfloat16)
    key_norm = key_hat.astype(jnp.bfloat16)
    factor = 1.0 / math.sqrt(queries.shape[0])
    scores = (
        jnp.einsum("cia,cib->iab", query_norm, key_norm, preferred_element_type=jnp.float32)
        * factor
    )
    raised = jnp.exp(scores)
    shares = raised / jnp.sum(raised, axis=2, keepdims=True)
    rounded = shares.astype(jnp.bfloat16)
    values = keyvals[:, :, 1]
    attended = jnp.einsum(
        "iab,cib->cia", rounded, values, preferred_element_type=jnp.float32
    ).astype(jnp.bfloat16)
    stored = (
        query_hat,
        query_scale,
        key_hat,
        key_scale,
        query_norm,
        key_norm,
        shares,
        rounded,
        values,
    )
    return (attended, stored)


def attend_back(upstream, stored):
    query_hat, query_scale, key_hat, key_scale, query_norm, key_norm, shares, rounded, values = (
        stored
    )
    factor = 1.0 / math.sqrt(upstream.shape[0])
    share_grad = jnp.einsum("cia,cib->iab", upstream, values, preferred_element_type=jnp.float32)
    value_grad = jnp.einsum("iab,cia->cib", rounded, upstream, preferred_element_type=jnp.float32)
    score_grad = (
        shares * (share_grad - jnp.sum(shares * share_grad, axis=2, keepdims=True)) * factor
    ).astype(jnp.bfloat16)
    query_back = jnp.einsum(
        "iab,cib->cia", score_grad, key_norm, preferred_element_type=jnp.float32
    )
    key_back = jnp.einsum(
        "iab,cia->cib", score_grad, query_norm, preferred_element_type=jnp.float32
    )
    query_grad = norm_back(query_back, query_hat, query_scale).astype(jnp.bfloat16)
    key_grad = norm_back(key_back, key_hat, key_scale).astype(jnp.bfloat16)
    pair_grad = jnp.stack([key_grad, value_grad.astype(jnp.bfloat16)], axis=2)
    return (query_grad, pair_grad)


def swap_pairs(n_dp, n_mp):
    ratio = n_mp // n_dp
    pairs = []
    for row in range(n_dp):
        for col in range(n_mp):
            owner, part = divmod(col, ratio)
            pairs.append((row * n_mp + col, owner * n_mp + row * ratio + part))
    return pairs


def swap(block):
    n_dp, n_mp = lax.axis_size("dp"), lax.axis_size("mp")
    return lax.ppermute(block, ("dp", "mp"), swap_pairs(n_dp, n_mp))


def spread_quarter(block):
    n_dp, n_mp = lax.axis_size("dp"), lax.axis_size("mp")
    ratio = n_mp // n_dp
    rows, width = block.shape
    copies = jnp.broadcast_to(swap(block)[None], (n_mp, rows, width))
    pieces = lax.all_to_all(copies, "mp", split_axis=0, concat_axis=0, tiled=True)
    pieces = pieces.reshape(n_dp, ratio, rows, width)
    return jnp.transpose(pieces, (0, 2, 1, 3)).reshape(n_dp * rows, ratio * width)


def spread_quarter_rows(block):
    n_dp, n_mp = lax.axis_size("dp"), lax.axis_size("mp")
    ratio = n_mp // n_dp
    rows, width = block.shape
    copies = jnp.broadcast_to(swap(block)[None], (n_mp, rows, width))
    pieces = lax.all_to_all(copies, "mp", split_axis=0, concat_axis=0, tiled=True)
    pieces = pieces.reshape(n_dp, ratio, rows, width)
    return jnp.transpose(pieces, (0, 2, 1, 3)).reshape(n_dp, rows, ratio * width)


def gather_quarter(partial, rows):
    n_dp, n_mp = lax.axis_size("dp"), lax.axis_size("mp")
    ratio = n_mp // n_dp
    width = partial.shape[1] // ratio
    pieces = partial.reshape(n_dp, rows, ratio, width)
    pieces = jnp.transpose(pieces, (0, 2, 1, 3)).reshape(n_mp, rows, width)
    summed = lax.psum_scatter(pieces, "mp", scatter_dimension=0, tiled=True)
    return swap(summed.reshape(rows, width))


def gather_quarter_exchange(partial, rows):
    n_dp, n_mp = lax.axis_size("dp"), lax.axis_size("mp")
    ratio = n_mp // n_dp
    width = partial.shape[1] // ratio
    pieces = partial.reshape(n_dp, rows, ratio, width)
    pieces = jnp.transpose(pieces, (0, 2, 1, 3)).reshape(n_mp, rows, width)
    received = lax.all_to_all(pieces, "mp", split_axis=0, concat_axis=0, tiled=True)
    return swap(jnp.sum(received, axis=0))


def blockwise_grad(left, right, n_blocks):
    rows = left.shape[1] // n_blocks
    total = None
    for block in range(n_blocks):
        piece = jnp.dot(
            left[:, block * rows:(block + 1) * rows],
            right[block * rows:(block + 1) * rows],
            preferred_element_type=jnp.float32,
        ).astype(jnp.bfloat16).astype(jnp.float32)
        total = piece if total is None else total + piece
    return total.astype(jnp.bfloat16)


def shards(tokens, norm_gain, qkv_weight, head_weight, up_weight, down_weight, cotangent):
    n_dp, n_mp = lax.axis_size("dp"), lax.axis_size("mp")
    head_slice = HS // n_mp
    quarter = qkv_weight.shape[-1]
    rows, width = tokens.shape
    qkv_flat = qkv_weight.reshape(-1, quarter)
    head_flat = head_weight.reshape(-1, quarter)

    widened = tokens.astype(jnp.float32)
    gain_wide = norm_gain.astype(jnp.float32)
    with_gain = jnp.concatenate([tokens, norm_gain.reshape(1, width)], axis=0)
    spread_in = spread_quarter_rows(with_gain)
    tokens_all = spread_in[:, :rows].reshape(-1, quarter).astype(jnp.float32)
    gain_quarter = spread_in[0, rows].astype(jnp.float32)
    part_mean = jnp.mean(tokens_all, axis=1)
    part_center = tokens_all - part_mean[:, None]
    part_m2 = jnp.sum(part_center * part_center, axis=1)
    parts = lax.all_gather(jnp.stack([part_mean, part_m2]), "dp", axis=0, tiled=False)
    mean_all = jnp.mean(parts[:, 0], axis=0)
    spread = parts[:, 0] - mean_all[None, :]
    m2_all = jnp.sum(parts[:, 1], axis=0) + quarter * jnp.sum(spread * spread, axis=0)
    scale_all = lax.rsqrt(m2_all / D + epsilon)
    hidden_all = (
        ((tokens_all - mean_all[:, None]) * scale_all[:, None]) * gain_quarter
    ).astype(jnp.bfloat16)
    me = lax.axis_index("dp")
    row_mean = lax.dynamic_slice_in_dim(mean_all, me * rows, rows)[:, None]
    row_scale = lax.dynamic_slice_in_dim(scale_all, me * rows, rows)[:, None]
    normed = (widened - row_mean) * row_scale
    cot_all = spread_quarter(cotangent)

    n_proj = qkv_flat.shape[0]
    proj_up = jnp.concatenate(
        [
            lax.dot_general(qkv_flat, hidden_all, contract_cols, preferred_element_type=jnp.float32),
            lax.dot_general(up_weight, hidden_all, contract_cols, preferred_element_type=jnp.float32),
        ],
        axis=0,
    )
    proj_up = lax.psum_scatter(proj_up, "dp", scatter_dimension=1, tiled=True)
    cot_later, proj_up = lax.optimization_barrier((cot_all, proj_up))
    projected = proj_up[:n_proj].astype(jnp.bfloat16).reshape(3, head_slice, HEADS, ROWS)
    up_input = proj_up[n_proj:]
    activated, gelu_slope = gelu_pair(up_input)
    up_output = activated.astype(jnp.bfloat16)

    by_head = HEADS % n_mp == 0
    if by_head:
        head_group = HEADS // n_mp
        qkv_heads = lax.all_to_all(projected, "mp", split_axis=2, concat_axis=1, tiled=True)
        query_heads = qkv_heads[0].reshape(HS, head_group * QB, TQ)
        pairs = jnp.stack([qkv_heads[1], qkv_heads[2]], axis=2)
        pair_heads = jnp.broadcast_to(
            pairs[:, :, None], (HS, head_group, QB, 2, PATCHES)
        ).reshape(HS, head_group * QB, 2, PATCHES)
        attended, stored = attend(query_heads, pair_heads)
        head_rows = lax.all_to_all(
            attended.reshape(HS, head_group, ROWS), "mp", split_axis=0, concat_axis=1, tiled=True
        ).reshape(head_slice * HEADS, ROWS)
    else:
        queries = projected[0].reshape(head_slice, ITEMS, TQ)
        keyvals = to_items(projected[1:])
        query_heads, pair_heads = (
            lax.all_to_all(queries, "mp", split_axis=1, concat_axis=0, tiled=True),
            lax.all_to_all(keyvals, "mp", split_axis=1, concat_axis=0, tiled=True),
        )
        attended, stored = attend(query_heads, pair_heads)
        head_rows = lax.all_to_all(attended, "mp", split_axis=0, concat_axis=1, tiled=True).reshape(
            head_slice * HEADS, ROWS
        )
    n_att = head_rows.shape[0]
    both_all = lax.all_gather(
        jnp.concatenate([head_rows, up_output], axis=0), "dp", axis=1, tiled=True
    )
    head_rows_all, up_output_all = both_all[:n_att], both_all[n_att:]
    branch = lax.dot_general(
        head_rows_all, head_flat, contract_rows, preferred_element_type=jnp.float32
    ) + lax.dot_general(up_output_all, down_weight, contract_rows, preferred_element_type=jnp.float32)
    branch_local = gather_quarter(branch, rows)
    mixed = (widened + branch_local).astype(jnp.bfloat16)

    down_grad = blockwise_grad(up_output_all, cot_all, n_dp)
    head_grad = blockwise_grad(head_rows_all, cot_all, n_dp)
    back = jnp.concatenate(
        [
            lax.dot_general(head_flat, cot_later, contract_cols, preferred_element_type=jnp.float32),
            lax.dot_general(down_weight, cot_later, contract_cols, preferred_element_type=jnp.float32),
        ],
        axis=0,
    )
    back = lax.psum_scatter(back, "dp", scatter_dimension=1, tiled=True)
    up_upstream = (back[n_att:] * gelu_slope).astype(jnp.bfloat16)
    head_upstream = back[:n_att].astype(jnp.bfloat16).reshape(head_slice, HEADS, ROWS)
    if by_head:
        upstream = lax.all_to_all(
            head_upstream, "mp", split_axis=1, concat_axis=0, tiled=True
        ).reshape(HS, head_group * QB, TQ)
        query_grad, pair_grad = attend_back(upstream, stored)
        pair_sum = jnp.sum(
            pair_grad.reshape(HS, head_group, QB, 2, PATCHES).astype(jnp.float32), axis=2
        ).astype(jnp.bfloat16)
        grads = jnp.stack(
            [query_grad.reshape(HS, head_group, ROWS), pair_sum[:, :, 0], pair_sum[:, :, 1]]
        )
        proj_grad = lax.all_to_all(grads, "mp", split_axis=1, concat_axis=2, tiled=True)
    else:
        upstream = lax.all_to_all(
            head_upstream.reshape(head_slice, ITEMS, TQ), "mp", split_axis=1, concat_axis=0, tiled=True
        )
        query_grad, pair_grad = attend_back(upstream, stored)
        query_local, pair_local = (
            lax.all_to_all(query_grad, "mp", split_axis=0, concat_axis=1, tiled=True),
            lax.all_to_all(pair_grad, "mp", split_axis=0, concat_axis=1, tiled=True),
        )
        proj_grad = jnp.concatenate(
            [query_local.reshape(1, head_slice, HEADS, ROWS), from_items(pair_local)], axis=0
        )
    proj_grad = proj_grad.reshape(3 * head_slice * HEADS, ROWS)
    grads_all = lax.all_gather(
        jnp.concatenate([proj_grad, up_upstream], axis=0), "dp", axis=1, tiled=True
    )
    proj_grad_all, up_upstream_all = grads_all[:n_proj], grads_all[n_proj:]
    qkv_grad = blockwise_grad(proj_grad_all, hidden_all, n_dp)
    up_grad = blockwise_grad(up_upstream_all, hidden_all, n_dp)
    input_partial = lax.dot_general(
        proj_grad_all, qkv_flat, contract_rows, preferred_element_type=jnp.float32
    ) + lax.dot_general(up_upstream_all, up_weight, contract_rows, preferred_element_type=jnp.float32)
    input_local = gather_quarter_exchange(input_partial, rows)

    scaled = input_local * gain_wide
    plain_sum, cross_sum = lax.psum(
        (jnp.sum(scaled, axis=1), jnp.sum(scaled * normed, axis=1)), "mp"
    )
    tokens_grad = row_scale * (
        scaled - plain_sum[:, None] / D - normed * (cross_sum[:, None] / D)
    )
    tokens_grad = tokens_grad + cotangent.astype(jnp.float32)
    gain_piece = jnp.sum(input_local * normed, axis=0)
    gain_grad = lax.psum(gain_piece, "dp")
    return (
        mixed,
        tokens_grad,
        qkv_grad.reshape(qkv_weight.shape),
        head_grad.reshape(head_weight.shape),
        up_grad,
        down_grad,
        gain_grad,
    )


def solution(mesh):
    in_specs = (
        P("dp", "mp"),
        P("mp"),
        P(None, "mp", None, "dp"),
        P("mp", None, "dp"),
        P("mp", "dp"),
        P("mp", "dp"),
        P("dp", "mp"),
    )
    out_specs = (
        P("dp", "mp"),
        P("dp", "mp"),
        P(None, "mp", None, "dp"),
        P("mp", None, "dp"),
        P("mp", "dp"),
        P("mp", "dp"),
        P("mp"),
    )
    return jax.shard_map(shards, mesh=mesh, in_specs=in_specs, out_specs=out_specs, check_vma=False)
```

```python
import math

import jax
import jax.numpy as jnp
from jax import lax
from jax.sharding import PartitionSpec as P

D = 6144
HEADS = 24
HS = 128
PATCHES = 128
QB = 8
IMG_DP = 1
ROWS = 128
TQ = 16
ITEMS = 192


epsilon = 1e-06
contract_rows = (((0,), (0,)), ((), ()))
contract_cols = (((1,), (1,)), ((), ()))


def gelu_pair(inputs):
    normal_cdf = 0.5 * (1.0 + jax.scipy.special.erf(inputs * 0.7071067811865476))
    density = jnp.exp(-0.5 * inputs * inputs) * 0.3989422804014327
    return (inputs * normal_cdf, normal_cdf + inputs * density)


def head_norm(values):
    center = values - jnp.mean(values, axis=0, keepdims=True)
    inverse = lax.rsqrt(jnp.mean(center * center, axis=0, keepdims=True) + epsilon)
    return (center * inverse, inverse)


def norm_back(upstream, normed, inverse):
    return inverse * (
        upstream
        - jnp.mean(upstream, axis=0, keepdims=True)
        - normed * jnp.mean(upstream * normed, axis=0, keepdims=True)
    )


def to_items(pair_rows):
    depth = pair_rows.shape[1]
    shaped = pair_rows.reshape(2, depth, HEADS, IMG_DP, 1, PATCHES)
    spread = jnp.broadcast_to(shaped, (2, depth, HEADS, IMG_DP, QB, PATCHES))
    return jnp.transpose(spread, (1, 2, 3, 4, 0, 5)).reshape(depth, HEADS * IMG_DP * QB, 2, PATCHES)


def from_items(pair_items):
    depth = pair_items.shape[0]
    shaped = pair_items.reshape(depth, HEADS, IMG_DP, QB, 2, PATCHES)
    summed = jnp.sum(shaped.astype(jnp.float32), axis=3).astype(jnp.bfloat16)
    return jnp.transpose(summed, (3, 0, 1, 2, 4)).reshape(2, depth, HEADS, IMG_DP * PATCHES)


def attend(queries, keyvals):
    query_hat, query_scale = head_norm(queries.astype(jnp.float32))
    key_hat, key_scale = head_norm(keyvals[:, :, 0].astype(jnp.float32))
    query_norm = query_hat.astype(jnp.bfloat16)
    key_norm = key_hat.astype(jnp.bfloat16)
    factor = 1.0 / math.sqrt(queries.shape[0])
    scores = (
        jnp.einsum("cia,cib->iab", query_norm, key_norm, preferred_element_type=jnp.float32)
        * factor
    )
    raised = jnp.exp(scores)
    shares = raised / jnp.sum(raised, axis=2, keepdims=True)
    rounded = shares.astype(jnp.bfloat16)
    values = keyvals[:, :, 1]
    attended = jnp.einsum(
        "iab,cib->cia", rounded, values, preferred_element_type=jnp.float32
    ).astype(jnp.bfloat16)
    stored = (
        query_hat,
        query_scale,
        key_hat,
        key_scale,
        query_norm,
        key_norm,
        shares,
        rounded,
        values,
    )
    return (attended, stored)


def attend_back(upstream, stored):
    query_hat, query_scale, key_hat, key_scale, query_norm, key_norm, shares, rounded, values = (
        stored
    )
    factor = 1.0 / math.sqrt(upstream.shape[0])
    share_grad = jnp.einsum("cia,cib->iab", upstream, values, preferred_element_type=jnp.float32)
    value_grad = jnp.einsum("iab,cia->cib", rounded, upstream, preferred_element_type=jnp.float32)
    score_grad = (
        shares * (share_grad - jnp.sum(shares * share_grad, axis=2, keepdims=True)) * factor
    ).astype(jnp.bfloat16)
    query_back = jnp.einsum(
        "iab,cib->cia", score_grad, key_norm, preferred_element_type=jnp.float32
    )
    key_back = jnp.einsum(
        "iab,cia->cib", score_grad, query_norm, preferred_element_type=jnp.float32
    )
    query_grad = norm_back(query_back, query_hat, query_scale).astype(jnp.bfloat16)
    key_grad = norm_back(key_back, key_hat, key_scale).astype(jnp.bfloat16)
    pair_grad = jnp.stack([key_grad, value_grad.astype(jnp.bfloat16)], axis=2)
    return (query_grad, pair_grad)


def swap_pairs(n_dp, n_mp):
    ratio = n_mp // n_dp
    pairs = []
    for row in range(n_dp):
        for col in range(n_mp):
            owner, part = divmod(col, ratio)
            pairs.append((row * n_mp + col, owner * n_mp + row * ratio + part))
    return pairs


def swap(block):
    n_dp, n_mp = lax.axis_size("dp"), lax.axis_size("mp")
    return lax.ppermute(block, ("dp", "mp"), swap_pairs(n_dp, n_mp))


def spread_quarter(block):
    n_dp, n_mp = lax.axis_size("dp"), lax.axis_size("mp")
    ratio = n_mp // n_dp
    rows, width = block.shape
    copies = jnp.broadcast_to(swap(block)[None], (n_mp, rows, width))
    pieces = lax.all_to_all(copies, "mp", split_axis=0, concat_axis=0, tiled=True)
    pieces = pieces.reshape(n_dp, ratio, rows, width)
    return jnp.transpose(pieces, (0, 2, 1, 3)).reshape(n_dp * rows, ratio * width)


def spread_quarter_rows(block):
    n_dp, n_mp = lax.axis_size("dp"), lax.axis_size("mp")
    ratio = n_mp // n_dp
    rows, width = block.shape
    copies = jnp.broadcast_to(swap(block)[None], (n_mp, rows, width))
    pieces = lax.all_to_all(copies, "mp", split_axis=0, concat_axis=0, tiled=True)
    pieces = pieces.reshape(n_dp, ratio, rows, width)
    return jnp.transpose(pieces, (0, 2, 1, 3)).reshape(n_dp, rows, ratio * width)


def gather_quarter(partial, rows):
    n_dp, n_mp = lax.axis_size("dp"), lax.axis_size("mp")
    ratio = n_mp // n_dp
    width = partial.shape[1] // ratio
    pieces = partial.reshape(n_dp, rows, ratio, width)
    pieces = jnp.transpose(pieces, (0, 2, 1, 3)).reshape(n_mp, rows, width)
    summed = lax.psum_scatter(pieces, "mp", scatter_dimension=0, tiled=True)
    return swap(summed.reshape(rows, width))


def gather_quarter_exchange(partial, rows):
    n_dp, n_mp = lax.axis_size("dp"), lax.axis_size("mp")
    ratio = n_mp // n_dp
    width = partial.shape[1] // ratio
    pieces = partial.reshape(n_dp, rows, ratio, width)
    pieces = jnp.transpose(pieces, (0, 2, 1, 3)).reshape(n_mp, rows, width)
    received = lax.all_to_all(pieces, "mp", split_axis=0, concat_axis=0, tiled=True)
    return swap(jnp.sum(received, axis=0))


def blockwise_grad(left, right, n_blocks):
    rows = left.shape[1] // n_blocks
    total = None
    for block in range(n_blocks):
        piece = jnp.dot(
            left[:, block * rows:(block + 1) * rows],
            right[block * rows:(block + 1) * rows],
            preferred_element_type=jnp.float32,
        ).astype(jnp.bfloat16).astype(jnp.float32)
        total = piece if total is None else total + piece
    return total.astype(jnp.bfloat16)


def shards(tokens, norm_gain, qkv_weight, head_weight, up_weight, down_weight, cotangent):
    n_dp, n_mp = lax.axis_size("dp"), lax.axis_size("mp")
    head_slice = HS // n_mp
    quarter = qkv_weight.shape[-1]
    rows, width = tokens.shape
    qkv_flat = qkv_weight.reshape(-1, quarter)
    head_flat = head_weight.reshape(-1, quarter)

    widened = tokens.astype(jnp.float32)
    gain_wide = norm_gain.astype(jnp.float32)
    with_gain = jnp.concatenate([tokens, norm_gain.reshape(1, width)], axis=0)
    spread_in = spread_quarter_rows(with_gain)
    tokens_all = spread_in[:, :rows].reshape(-1, quarter).astype(jnp.float32)
    gain_quarter = spread_in[0, rows].astype(jnp.float32)
    part_mean = jnp.mean(tokens_all, axis=1)
    part_center = tokens_all - part_mean[:, None]
    part_m2 = jnp.sum(part_center * part_center, axis=1)
    parts = lax.all_gather(jnp.stack([part_mean, part_m2]), "dp", axis=0, tiled=False)
    mean_all = jnp.mean(parts[:, 0], axis=0)
    spread = parts[:, 0] - mean_all[None, :]
    m2_all = jnp.sum(parts[:, 1], axis=0) + quarter * jnp.sum(spread * spread, axis=0)
    scale_all = lax.rsqrt(m2_all / D + epsilon)
    hidden_all = (
        ((tokens_all - mean_all[:, None]) * scale_all[:, None]) * gain_quarter
    ).astype(jnp.bfloat16)
    me = lax.axis_index("dp")
    row_mean = lax.dynamic_slice_in_dim(mean_all, me * rows, rows)[:, None]
    row_scale = lax.dynamic_slice_in_dim(scale_all, me * rows, rows)[:, None]
    normed = (widened - row_mean) * row_scale
    cot_all = spread_quarter(cotangent)

    n_proj = qkv_flat.shape[0]
    proj_up = jnp.concatenate(
        [
            lax.dot_general(qkv_flat, hidden_all, contract_cols, preferred_element_type=jnp.float32),
            lax.dot_general(up_weight, hidden_all, contract_cols, preferred_element_type=jnp.float32),
        ],
        axis=0,
    )
    proj_up = lax.psum_scatter(proj_up, "dp", scatter_dimension=1, tiled=True)
    cot_later, proj_up = lax.optimization_barrier((cot_all, proj_up))
    projected = proj_up[:n_proj].astype(jnp.bfloat16).reshape(3, head_slice, HEADS, ROWS)
    up_input = proj_up[n_proj:]
    activated, gelu_slope = gelu_pair(up_input)
    up_output = activated.astype(jnp.bfloat16)

    by_head = HEADS % n_mp == 0
    if by_head:
        head_group = HEADS // n_mp
        qkv_heads = lax.all_to_all(projected, "mp", split_axis=2, concat_axis=1, tiled=True)
        query_heads = qkv_heads[0].reshape(HS, head_group * QB, TQ)
        pairs = jnp.stack([qkv_heads[1], qkv_heads[2]], axis=2)
        pair_heads = jnp.broadcast_to(
            pairs[:, :, None], (HS, head_group, QB, 2, PATCHES)
        ).reshape(HS, head_group * QB, 2, PATCHES)
        attended, stored = attend(query_heads, pair_heads)
        head_rows = lax.all_to_all(
            attended.reshape(HS, head_group, ROWS), "mp", split_axis=0, concat_axis=1, tiled=True
        ).reshape(head_slice * HEADS, ROWS)
    else:
        queries = projected[0].reshape(head_slice, ITEMS, TQ)
        keyvals = to_items(projected[1:])
        query_heads, pair_heads = (
            lax.all_to_all(queries, "mp", split_axis=1, concat_axis=0, tiled=True),
            lax.all_to_all(keyvals, "mp", split_axis=1, concat_axis=0, tiled=True),
        )
        attended, stored = attend(query_heads, pair_heads)
        head_rows = lax.all_to_all(attended, "mp", split_axis=0, concat_axis=1, tiled=True).reshape(
            head_slice * HEADS, ROWS
        )
    n_att = head_rows.shape[0]
    both_all = lax.all_gather(
        jnp.concatenate([head_rows, up_output], axis=0), "dp", axis=1, tiled=True
    )
    head_rows_all, up_output_all = both_all[:n_att], both_all[n_att:]
    branch = lax.dot_general(
        head_rows_all, head_flat, contract_rows, preferred_element_type=jnp.float32
    ) + lax.dot_general(up_output_all, down_weight, contract_rows, preferred_element_type=jnp.float32)

    down_grad = blockwise_grad(up_output_all, cot_all, n_dp)
    head_grad = blockwise_grad(head_rows_all, cot_all, n_dp)
    back = jnp.concatenate(
        [
            lax.dot_general(head_flat, cot_later, contract_cols, preferred_element_type=jnp.float32),
            lax.dot_general(down_weight, cot_later, contract_cols, preferred_element_type=jnp.float32),
        ],
        axis=0,
    )
    back = lax.psum_scatter(back, "dp", scatter_dimension=1, tiled=True)
    up_upstream = (back[n_att:] * gelu_slope).astype(jnp.bfloat16)
    head_upstream = back[:n_att].astype(jnp.bfloat16).reshape(head_slice, HEADS, ROWS)
    if by_head:
        upstream = lax.all_to_all(
            head_upstream, "mp", split_axis=1, concat_axis=0, tiled=True
        ).reshape(HS, head_group * QB, TQ)
        query_grad, pair_grad = attend_back(upstream, stored)
        pair_sum = jnp.sum(
            pair_grad.reshape(HS, head_group, QB, 2, PATCHES).astype(jnp.float32), axis=2
        ).astype(jnp.bfloat16)
        grads = jnp.stack(
            [query_grad.reshape(HS, head_group, ROWS), pair_sum[:, :, 0], pair_sum[:, :, 1]]
        )
        branch, grads = lax.optimization_barrier((branch, grads))
        proj_grad = lax.all_to_all(grads, "mp", split_axis=1, concat_axis=2, tiled=True)
    else:
        upstream = lax.all_to_all(
            head_upstream.reshape(head_slice, ITEMS, TQ), "mp", split_axis=1, concat_axis=0, tiled=True
        )
        query_grad, pair_grad = attend_back(upstream, stored)
        branch, pair_grad = lax.optimization_barrier((branch, pair_grad))
        query_local, pair_local = (
            lax.all_to_all(query_grad, "mp", split_axis=0, concat_axis=1, tiled=True),
            lax.all_to_all(pair_grad, "mp", split_axis=0, concat_axis=1, tiled=True),
        )
        proj_grad = jnp.concatenate(
            [query_local.reshape(1, head_slice, HEADS, ROWS), from_items(pair_local)], axis=0
        )
    proj_grad = proj_grad.reshape(3 * head_slice * HEADS, ROWS)
    branch_local = gather_quarter_exchange(branch, rows)
    mixed = (widened + branch_local).astype(jnp.bfloat16)
    grads_all = lax.all_gather(
        jnp.concatenate([proj_grad, up_upstream], axis=0), "dp", axis=1, tiled=True
    )
    proj_grad_all, up_upstream_all = grads_all[:n_proj], grads_all[n_proj:]
    qkv_grad = blockwise_grad(proj_grad_all, hidden_all, n_dp)
    up_grad = blockwise_grad(up_upstream_all, hidden_all, n_dp)
    input_partial = lax.dot_general(
        proj_grad_all, qkv_flat, contract_rows, preferred_element_type=jnp.float32
    ) + lax.dot_general(up_upstream_all, up_weight, contract_rows, preferred_element_type=jnp.float32)
    input_local = gather_quarter(input_partial, rows)

    scaled = input_local * gain_wide
    plain_sum, cross_sum = lax.psum(
        (jnp.sum(scaled, axis=1), jnp.sum(scaled * normed, axis=1)), "mp"
    )
    tokens_grad = row_scale * (
        scaled - plain_sum[:, None] / D - normed * (cross_sum[:, None] / D)
    )
    tokens_grad = tokens_grad + cotangent.astype(jnp.float32)
    gain_piece = jnp.sum(input_local * normed, axis=0)
    gain_grad = lax.psum(gain_piece, "dp")
    return (
        mixed,
        tokens_grad,
        qkv_grad.reshape(qkv_weight.shape),
        head_grad.reshape(head_weight.shape),
        up_grad,
        down_grad,
        gain_grad,
    )


def solution(mesh):
    in_specs = (
        P("dp", "mp"),
        P("mp"),
        P(None, "mp", None, "dp"),
        P("mp", None, "dp"),
        P("mp", "dp"),
        P("mp", "dp"),
        P("dp", "mp"),
    )
    out_specs = (
        P("dp", "mp"),
        P("dp", "mp"),
        P(None, "mp", None, "dp"),
        P("mp", None, "dp"),
        P("mp", "dp"),
        P("mp", "dp"),
        P("mp"),
    )
    return jax.shard_map(shards, mesh=mesh, in_specs=in_specs, out_specs=out_specs, check_vma=False)
```

```python
import math

import jax
import jax.numpy as jnp
from jax import lax
from jax.sharding import PartitionSpec as P

D = 6144
HEADS = 24
HS = 128
PATCHES = 128
QB = 8
IMG_DP = 1
ROWS = 128
TQ = 16
ITEMS = 192


epsilon = 1e-06
contract_rows = (((0,), (0,)), ((), ()))
contract_cols = (((1,), (1,)), ((), ()))


def gelu_pair(inputs):
    normal_cdf = 0.5 * (1.0 + jax.scipy.special.erf(inputs * 0.7071067811865476))
    density = jnp.exp(-0.5 * inputs * inputs) * 0.3989422804014327
    return (inputs * normal_cdf, normal_cdf + inputs * density)


def head_norm(values):
    center = values - jnp.mean(values, axis=0, keepdims=True)
    inverse = lax.rsqrt(jnp.mean(center * center, axis=0, keepdims=True) + epsilon)
    return (center * inverse, inverse)


def norm_back(upstream, normed, inverse):
    return inverse * (
        upstream
        - jnp.mean(upstream, axis=0, keepdims=True)
        - normed * jnp.mean(upstream * normed, axis=0, keepdims=True)
    )


def to_items(pair_rows):
    depth = pair_rows.shape[1]
    shaped = pair_rows.reshape(2, depth, HEADS, IMG_DP, 1, PATCHES)
    spread = jnp.broadcast_to(shaped, (2, depth, HEADS, IMG_DP, QB, PATCHES))
    return jnp.transpose(spread, (1, 2, 3, 4, 0, 5)).reshape(depth, HEADS * IMG_DP * QB, 2, PATCHES)


def from_items(pair_items):
    depth = pair_items.shape[0]
    shaped = pair_items.reshape(depth, HEADS, IMG_DP, QB, 2, PATCHES)
    summed = jnp.sum(shaped.astype(jnp.float32), axis=3).astype(jnp.bfloat16)
    return jnp.transpose(summed, (3, 0, 1, 2, 4)).reshape(2, depth, HEADS, IMG_DP * PATCHES)


def attend(queries, keyvals):
    query_hat, query_scale = head_norm(queries.astype(jnp.float32))
    key_hat, key_scale = head_norm(keyvals[:, :, 0].astype(jnp.float32))
    query_norm = query_hat.astype(jnp.bfloat16)
    key_norm = key_hat.astype(jnp.bfloat16)
    factor = 1.0 / math.sqrt(queries.shape[0])
    scores = (
        jnp.einsum("cia,cib->iab", query_norm, key_norm, preferred_element_type=jnp.float32)
        * factor
    )
    raised = jnp.exp(scores)
    shares = raised / jnp.sum(raised, axis=2, keepdims=True)
    rounded = shares.astype(jnp.bfloat16)
    values = keyvals[:, :, 1]
    attended = jnp.einsum(
        "iab,cib->cia", rounded, values, preferred_element_type=jnp.float32
    ).astype(jnp.bfloat16)
    stored = (
        query_hat,
        query_scale,
        key_hat,
        key_scale,
        query_norm,
        key_norm,
        shares,
        rounded,
        values,
    )
    return (attended, stored)


def attend_back(upstream, stored):
    query_hat, query_scale, key_hat, key_scale, query_norm, key_norm, shares, rounded, values = (
        stored
    )
    factor = 1.0 / math.sqrt(upstream.shape[0])
    share_grad = jnp.einsum("cia,cib->iab", upstream, values, preferred_element_type=jnp.float32)
    value_grad = jnp.einsum("iab,cia->cib", rounded, upstream, preferred_element_type=jnp.float32)
    score_grad = (
        shares * (share_grad - jnp.sum(shares * share_grad, axis=2, keepdims=True)) * factor
    ).astype(jnp.bfloat16)
    query_back = jnp.einsum(
        "iab,cib->cia", score_grad, key_norm, preferred_element_type=jnp.float32
    )
    key_back = jnp.einsum(
        "iab,cia->cib", score_grad, query_norm, preferred_element_type=jnp.float32
    )
    query_grad = norm_back(query_back, query_hat, query_scale).astype(jnp.bfloat16)
    key_grad = norm_back(key_back, key_hat, key_scale).astype(jnp.bfloat16)
    pair_grad = jnp.stack([key_grad, value_grad.astype(jnp.bfloat16)], axis=2)
    return (query_grad, pair_grad)


def swap_pairs(n_dp, n_mp):
    ratio = n_mp // n_dp
    pairs = []
    for row in range(n_dp):
        for col in range(n_mp):
            owner, part = divmod(col, ratio)
            pairs.append((row * n_mp + col, owner * n_mp + row * ratio + part))
    return pairs


def swap(block):
    n_dp, n_mp = lax.axis_size("dp"), lax.axis_size("mp")
    return lax.ppermute(block, ("dp", "mp"), swap_pairs(n_dp, n_mp))


def spread_quarter(block):
    n_dp, n_mp = lax.axis_size("dp"), lax.axis_size("mp")
    ratio = n_mp // n_dp
    rows, width = block.shape
    copies = jnp.broadcast_to(swap(block)[None], (n_mp, rows, width))
    pieces = lax.all_to_all(copies, "mp", split_axis=0, concat_axis=0, tiled=True)
    pieces = pieces.reshape(n_dp, ratio, rows, width)
    return jnp.transpose(pieces, (0, 2, 1, 3)).reshape(n_dp * rows, ratio * width)


def spread_quarter_rows(block):
    n_dp, n_mp = lax.axis_size("dp"), lax.axis_size("mp")
    ratio = n_mp // n_dp
    rows, width = block.shape
    copies = jnp.broadcast_to(swap(block)[None], (n_mp, rows, width))
    pieces = lax.all_to_all(copies, "mp", split_axis=0, concat_axis=0, tiled=True)
    pieces = pieces.reshape(n_dp, ratio, rows, width)
    return jnp.transpose(pieces, (0, 2, 1, 3)).reshape(n_dp, rows, ratio * width)


def gather_quarter(partial, rows):
    n_dp, n_mp = lax.axis_size("dp"), lax.axis_size("mp")
    ratio = n_mp // n_dp
    width = partial.shape[1] // ratio
    pieces = partial.reshape(n_dp, rows, ratio, width)
    pieces = jnp.transpose(pieces, (0, 2, 1, 3)).reshape(n_mp, rows, width)
    summed = lax.psum_scatter(pieces, "mp", scatter_dimension=0, tiled=True)
    return swap(summed.reshape(rows, width))


def gather_quarter_exchange(partial, rows):
    n_dp, n_mp = lax.axis_size("dp"), lax.axis_size("mp")
    ratio = n_mp // n_dp
    width = partial.shape[1] // ratio
    pieces = partial.reshape(n_dp, rows, ratio, width)
    pieces = jnp.transpose(pieces, (0, 2, 1, 3)).reshape(n_mp, rows, width)
    received = lax.all_to_all(pieces, "mp", split_axis=0, concat_axis=0, tiled=True)
    return swap(jnp.sum(received, axis=0))


def blockwise_grad(left, right, n_blocks):
    rows = left.shape[1] // n_blocks
    total = None
    for block in range(n_blocks):
        piece = jnp.dot(
            left[:, block * rows:(block + 1) * rows],
            right[block * rows:(block + 1) * rows],
            preferred_element_type=jnp.float32,
        ).astype(jnp.bfloat16).astype(jnp.float32)
        total = piece if total is None else total + piece
    return total.astype(jnp.bfloat16)


def shards(tokens, norm_gain, qkv_weight, head_weight, up_weight, down_weight, cotangent):
    n_dp, n_mp = lax.axis_size("dp"), lax.axis_size("mp")
    head_slice = HS // n_mp
    quarter = qkv_weight.shape[-1]
    rows, width = tokens.shape
    qkv_flat = qkv_weight.reshape(-1, quarter)
    head_flat = head_weight.reshape(-1, quarter)

    widened = tokens.astype(jnp.float32)
    gain_wide = norm_gain.astype(jnp.float32)
    with_gain = jnp.concatenate([tokens, norm_gain.reshape(1, width)], axis=0)
    spread_in = spread_quarter_rows(with_gain)
    tokens_all = spread_in[:, :rows].reshape(-1, quarter).astype(jnp.float32)
    gain_quarter = spread_in[0, rows].astype(jnp.float32)
    part_mean = jnp.mean(tokens_all, axis=1)
    part_center = tokens_all - part_mean[:, None]
    part_m2 = jnp.sum(part_center * part_center, axis=1)
    parts = lax.all_gather(jnp.stack([part_mean, part_m2]), "dp", axis=0, tiled=False)
    mean_all = jnp.mean(parts[:, 0], axis=0)
    spread = parts[:, 0] - mean_all[None, :]
    m2_all = jnp.sum(parts[:, 1], axis=0) + quarter * jnp.sum(spread * spread, axis=0)
    scale_all = lax.rsqrt(m2_all / D + epsilon)
    normed_all = (tokens_all - mean_all[:, None]) * scale_all[:, None]
    hidden_all = (normed_all * gain_quarter).astype(jnp.bfloat16)
    me = lax.axis_index("dp")
    row_mean = lax.dynamic_slice_in_dim(mean_all, me * rows, rows)[:, None]
    row_scale = lax.dynamic_slice_in_dim(scale_all, me * rows, rows)[:, None]
    normed = (widened - row_mean) * row_scale
    cot_all = spread_quarter(cotangent)

    n_proj = qkv_flat.shape[0]
    proj_up = jnp.concatenate(
        [
            lax.dot_general(qkv_flat, hidden_all, contract_cols, preferred_element_type=jnp.float32),
            lax.dot_general(up_weight, hidden_all, contract_cols, preferred_element_type=jnp.float32),
        ],
        axis=0,
    )
    proj_up = lax.psum_scatter(proj_up, "dp", scatter_dimension=1, tiled=True)
    cot_later, proj_up = lax.optimization_barrier((cot_all, proj_up))
    projected = proj_up[:n_proj].astype(jnp.bfloat16).reshape(3, head_slice, HEADS, ROWS)
    up_input = proj_up[n_proj:]
    activated, gelu_slope = gelu_pair(up_input)
    up_output = activated.astype(jnp.bfloat16)

    by_head = HEADS % n_mp == 0
    if by_head:
        head_group = HEADS // n_mp
        qkv_heads = lax.all_to_all(projected, "mp", split_axis=2, concat_axis=1, tiled=True)
        query_heads = qkv_heads[0].reshape(HS, head_group * QB, TQ)
        pairs = jnp.stack([qkv_heads[1], qkv_heads[2]], axis=2)
        pair_heads = jnp.broadcast_to(
            pairs[:, :, None], (HS, head_group, QB, 2, PATCHES)
        ).reshape(HS, head_group * QB, 2, PATCHES)
        attended, stored = attend(query_heads, pair_heads)
        head_rows = lax.all_to_all(
            attended.reshape(HS, head_group, ROWS), "mp", split_axis=0, concat_axis=1, tiled=True
        ).reshape(head_slice * HEADS, ROWS)
    else:
        queries = projected[0].reshape(head_slice, ITEMS, TQ)
        keyvals = to_items(projected[1:])
        query_heads, pair_heads = (
            lax.all_to_all(queries, "mp", split_axis=1, concat_axis=0, tiled=True),
            lax.all_to_all(keyvals, "mp", split_axis=1, concat_axis=0, tiled=True),
        )
        attended, stored = attend(query_heads, pair_heads)
        head_rows = lax.all_to_all(attended, "mp", split_axis=0, concat_axis=1, tiled=True).reshape(
            head_slice * HEADS, ROWS
        )
    n_att = head_rows.shape[0]
    both_all = lax.all_gather(
        jnp.concatenate([head_rows, up_output], axis=0), "dp", axis=1, tiled=True
    )
    head_rows_all, up_output_all = both_all[:n_att], both_all[n_att:]
    branch = lax.dot_general(
        head_rows_all, head_flat, contract_rows, preferred_element_type=jnp.float32
    ) + lax.dot_general(up_output_all, down_weight, contract_rows, preferred_element_type=jnp.float32)
    branch_local = gather_quarter(branch, rows)
    mixed = (widened + branch_local).astype(jnp.bfloat16)

    down_grad = blockwise_grad(up_output_all, cot_all, n_dp)
    head_grad = blockwise_grad(head_rows_all, cot_all, n_dp)
    back = jnp.concatenate(
        [
            lax.dot_general(head_flat, cot_later, contract_cols, preferred_element_type=jnp.float32),
            lax.dot_general(down_weight, cot_later, contract_cols, preferred_element_type=jnp.float32),
        ],
        axis=0,
    )
    back = lax.psum_scatter(back, "dp", scatter_dimension=1, tiled=True)
    up_upstream = (back[n_att:] * gelu_slope).astype(jnp.bfloat16)
    head_upstream = back[:n_att].astype(jnp.bfloat16).reshape(head_slice, HEADS, ROWS)
    if by_head:
        upstream = lax.all_to_all(
            head_upstream, "mp", split_axis=1, concat_axis=0, tiled=True
        ).reshape(HS, head_group * QB, TQ)
        query_grad, pair_grad = attend_back(upstream, stored)
        pair_sum = jnp.sum(
            pair_grad.reshape(HS, head_group, QB, 2, PATCHES).astype(jnp.float32), axis=2
        ).astype(jnp.bfloat16)
        grads = jnp.stack(
            [query_grad.reshape(HS, head_group, ROWS), pair_sum[:, :, 0], pair_sum[:, :, 1]]
        )
        proj_grad = lax.all_to_all(grads, "mp", split_axis=1, concat_axis=2, tiled=True)
    else:
        upstream = lax.all_to_all(
            head_upstream.reshape(head_slice, ITEMS, TQ), "mp", split_axis=1, concat_axis=0, tiled=True
        )
        query_grad, pair_grad = attend_back(upstream, stored)
        query_local, pair_local = (
            lax.all_to_all(query_grad, "mp", split_axis=0, concat_axis=1, tiled=True),
            lax.all_to_all(pair_grad, "mp", split_axis=0, concat_axis=1, tiled=True),
        )
        proj_grad = jnp.concatenate(
            [query_local.reshape(1, head_slice, HEADS, ROWS), from_items(pair_local)], axis=0
        )
    proj_grad = proj_grad.reshape(3 * head_slice * HEADS, ROWS)
    grads_all = lax.all_gather(
        jnp.concatenate([proj_grad, up_upstream], axis=0), "dp", axis=1, tiled=True
    )
    proj_grad_all, up_upstream_all = grads_all[:n_proj], grads_all[n_proj:]
    qkv_grad = blockwise_grad(proj_grad_all, hidden_all, n_dp)
    up_grad = blockwise_grad(up_upstream_all, hidden_all, n_dp)
    input_partial = lax.dot_general(
        proj_grad_all, qkv_flat, contract_rows, preferred_element_type=jnp.float32
    ) + lax.dot_general(up_upstream_all, up_weight, contract_rows, preferred_element_type=jnp.float32)
    scaled_partial = input_partial * gain_quarter
    tokens_count = input_partial.shape[0]
    quarter_sums = lax.psum(
        jnp.concatenate(
            [
                jnp.sum(scaled_partial, axis=1),
                jnp.sum(scaled_partial * normed_all, axis=1),
                jnp.sum(input_partial * normed_all, axis=0),
            ]
        ),
        "mp",
    )
    row_sums = lax.psum(quarter_sums[:2 * tokens_count].reshape(2, tokens_count), "dp")
    row_sums = lax.dynamic_slice_in_dim(row_sums, me * rows, rows, 1)
    plain_sum, cross_sum = row_sums[0], row_sums[1]
    part = lax.axis_index("mp") % (n_mp // n_dp)
    gain_grad = swap(
        lax.dynamic_slice_in_dim(quarter_sums[2 * tokens_count:], part * width, width)
    )
    input_local = gather_quarter_exchange(input_partial, rows)

    scaled = input_local * gain_wide
    tokens_grad = row_scale * (
        scaled - plain_sum[:, None] / D - normed * (cross_sum[:, None] / D)
    )
    tokens_grad = tokens_grad + cotangent.astype(jnp.float32)
    return (
        mixed,
        tokens_grad,
        qkv_grad.reshape(qkv_weight.shape),
        head_grad.reshape(head_weight.shape),
        up_grad,
        down_grad,
        gain_grad,
    )


def solution(mesh):
    in_specs = (
        P("dp", "mp"),
        P("mp"),
        P(None, "mp", None, "dp"),
        P("mp", None, "dp"),
        P("mp", "dp"),
        P("mp", "dp"),
        P("dp", "mp"),
    )
    out_specs = (
        P("dp", "mp"),
        P("dp", "mp"),
        P(None, "mp", None, "dp"),
        P("mp", None, "dp"),
        P("mp", "dp"),
        P("mp", "dp"),
        P("mp"),
    )
    return jax.shard_map(shards, mesh=mesh, in_specs=in_specs, out_specs=out_specs, check_vma=False)
```

```python
import math

import jax
import jax.numpy as jnp
from jax import lax
from jax.sharding import PartitionSpec as P

D = 6144
HEADS = 24
HS = 128
PATCHES = 128
QB = 8
IMG_DP = 1
ROWS = 128
TQ = 16
ITEMS = 192


epsilon = 1e-06
contract_rows = (((0,), (0,)), ((), ()))
contract_cols = (((1,), (1,)), ((), ()))


def gelu_pair(inputs):
    normal_cdf = 0.5 * (1.0 + jax.scipy.special.erf(inputs * 0.7071067811865476))
    density = jnp.exp(-0.5 * inputs * inputs) * 0.3989422804014327
    return (inputs * normal_cdf, normal_cdf + inputs * density)


def head_norm(values):
    center = values - jnp.mean(values, axis=0, keepdims=True)
    inverse = lax.rsqrt(jnp.mean(center * center, axis=0, keepdims=True) + epsilon)
    return (center * inverse, inverse)


def norm_back(upstream, normed, inverse):
    return inverse * (
        upstream
        - jnp.mean(upstream, axis=0, keepdims=True)
        - normed * jnp.mean(upstream * normed, axis=0, keepdims=True)
    )


def to_items(pair_rows):
    depth = pair_rows.shape[1]
    shaped = pair_rows.reshape(2, depth, HEADS, IMG_DP, 1, PATCHES)
    spread = jnp.broadcast_to(shaped, (2, depth, HEADS, IMG_DP, QB, PATCHES))
    return jnp.transpose(spread, (1, 2, 3, 4, 0, 5)).reshape(depth, HEADS * IMG_DP * QB, 2, PATCHES)


def from_items(pair_items):
    depth = pair_items.shape[0]
    shaped = pair_items.reshape(depth, HEADS, IMG_DP, QB, 2, PATCHES)
    summed = jnp.sum(shaped.astype(jnp.float32), axis=3).astype(jnp.bfloat16)
    return jnp.transpose(summed, (3, 0, 1, 2, 4)).reshape(2, depth, HEADS, IMG_DP * PATCHES)


def attend(queries, keyvals):
    query_hat, query_scale = head_norm(queries.astype(jnp.float32))
    key_hat, key_scale = head_norm(keyvals[:, :, 0].astype(jnp.float32))
    query_norm = query_hat.astype(jnp.bfloat16)
    key_norm = key_hat.astype(jnp.bfloat16)
    factor = 1.0 / math.sqrt(queries.shape[0])
    scores = (
        jnp.einsum("cia,cib->iab", query_norm, key_norm, preferred_element_type=jnp.float32)
        * factor
    )
    raised = jnp.exp(scores)
    shares = raised / jnp.sum(raised, axis=2, keepdims=True)
    rounded = shares.astype(jnp.bfloat16)
    values = keyvals[:, :, 1]
    attended = jnp.einsum(
        "iab,cib->cia", rounded, values, preferred_element_type=jnp.float32
    ).astype(jnp.bfloat16)
    stored = (
        query_hat,
        query_scale,
        key_hat,
        key_scale,
        query_norm,
        key_norm,
        shares,
        rounded,
        values,
    )
    return (attended, stored)


def attend_back(upstream, stored):
    query_hat, query_scale, key_hat, key_scale, query_norm, key_norm, shares, rounded, values = (
        stored
    )
    factor = 1.0 / math.sqrt(upstream.shape[0])
    share_grad = jnp.einsum("cia,cib->iab", upstream, values, preferred_element_type=jnp.float32)
    value_grad = jnp.einsum("iab,cia->cib", rounded, upstream, preferred_element_type=jnp.float32)
    score_grad = (
        shares * (share_grad - jnp.sum(shares * share_grad, axis=2, keepdims=True)) * factor
    ).astype(jnp.bfloat16)
    query_back = jnp.einsum(
        "iab,cib->cia", score_grad, key_norm, preferred_element_type=jnp.float32
    )
    key_back = jnp.einsum(
        "iab,cia->cib", score_grad, query_norm, preferred_element_type=jnp.float32
    )
    query_grad = norm_back(query_back, query_hat, query_scale).astype(jnp.bfloat16)
    key_grad = norm_back(key_back, key_hat, key_scale).astype(jnp.bfloat16)
    pair_grad = jnp.stack([key_grad, value_grad.astype(jnp.bfloat16)], axis=2)
    return (query_grad, pair_grad)


def swap_pairs(n_dp, n_mp):
    ratio = n_mp // n_dp
    pairs = []
    for row in range(n_dp):
        for col in range(n_mp):
            owner, part = divmod(col, ratio)
            pairs.append((row * n_mp + col, owner * n_mp + row * ratio + part))
    return pairs


def swap(block):
    n_dp, n_mp = lax.axis_size("dp"), lax.axis_size("mp")
    return lax.ppermute(block, ("dp", "mp"), swap_pairs(n_dp, n_mp))


def spread_quarter(block):
    n_dp, n_mp = lax.axis_size("dp"), lax.axis_size("mp")
    ratio = n_mp // n_dp
    rows, width = block.shape
    copies = jnp.broadcast_to(swap(block)[None], (n_mp, rows, width))
    pieces = lax.all_to_all(copies, "mp", split_axis=0, concat_axis=0, tiled=True)
    pieces = pieces.reshape(n_dp, ratio, rows, width)
    return jnp.transpose(pieces, (0, 2, 1, 3)).reshape(n_dp * rows, ratio * width)


def spread_quarter_rows(block):
    n_dp, n_mp = lax.axis_size("dp"), lax.axis_size("mp")
    ratio = n_mp // n_dp
    rows, width = block.shape
    copies = jnp.broadcast_to(swap(block)[None], (n_mp, rows, width))
    pieces = lax.all_to_all(copies, "mp", split_axis=0, concat_axis=0, tiled=True)
    pieces = pieces.reshape(n_dp, ratio, rows, width)
    return jnp.transpose(pieces, (0, 2, 1, 3)).reshape(n_dp, rows, ratio * width)


def gather_quarter(partial, rows):
    n_dp, n_mp = lax.axis_size("dp"), lax.axis_size("mp")
    ratio = n_mp // n_dp
    width = partial.shape[1] // ratio
    pieces = partial.reshape(n_dp, rows, ratio, width)
    pieces = jnp.transpose(pieces, (0, 2, 1, 3)).reshape(n_mp, rows, width)
    summed = lax.psum_scatter(pieces, "mp", scatter_dimension=0, tiled=True)
    return swap(summed.reshape(rows, width))


def gather_quarter_exchange(partial, rows):
    n_dp, n_mp = lax.axis_size("dp"), lax.axis_size("mp")
    ratio = n_mp // n_dp
    width = partial.shape[1] // ratio
    pieces = partial.reshape(n_dp, rows, ratio, width)
    pieces = jnp.transpose(pieces, (0, 2, 1, 3)).reshape(n_mp, rows, width)
    received = lax.all_to_all(pieces, "mp", split_axis=0, concat_axis=0, tiled=True)
    return swap(jnp.sum(received, axis=0))


def blockwise_grad(left, right, n_blocks):
    rows = left.shape[1] // n_blocks
    total = None
    for block in range(n_blocks):
        piece = jnp.dot(
            left[:, block * rows:(block + 1) * rows],
            right[block * rows:(block + 1) * rows],
            preferred_element_type=jnp.float32,
        ).astype(jnp.bfloat16).astype(jnp.float32)
        total = piece if total is None else total + piece
    return total.astype(jnp.bfloat16)


def shards(tokens, norm_gain, qkv_weight, head_weight, up_weight, down_weight, cotangent):
    n_dp, n_mp = lax.axis_size("dp"), lax.axis_size("mp")
    head_slice = HS // n_mp
    quarter = qkv_weight.shape[-1]
    rows, width = tokens.shape
    qkv_flat = qkv_weight.reshape(-1, quarter)
    head_flat = head_weight.reshape(-1, quarter)

    widened = tokens.astype(jnp.float32)
    gain_wide = norm_gain.astype(jnp.float32)
    with_gain = jnp.concatenate([tokens, norm_gain.reshape(1, width)], axis=0)
    spread_in = spread_quarter_rows(with_gain)
    tokens_all = spread_in[:, :rows].reshape(-1, quarter).astype(jnp.float32)
    gain_quarter = spread_in[0, rows].astype(jnp.float32)
    part_mean = jnp.mean(tokens_all, axis=1)
    part_center = tokens_all - part_mean[:, None]
    part_m2 = jnp.sum(part_center * part_center, axis=1)
    parts = lax.all_gather(jnp.stack([part_mean, part_m2]), "dp", axis=0, tiled=False)
    mean_all = jnp.mean(parts[:, 0], axis=0)
    spread = parts[:, 0] - mean_all[None, :]
    m2_all = jnp.sum(parts[:, 1], axis=0) + quarter * jnp.sum(spread * spread, axis=0)
    scale_all = lax.rsqrt(m2_all / D + epsilon)
    hidden_all = (
        ((tokens_all - mean_all[:, None]) * scale_all[:, None]) * gain_quarter
    ).astype(jnp.bfloat16)
    me = lax.axis_index("dp")
    row_mean = lax.dynamic_slice_in_dim(mean_all, me * rows, rows)[:, None]
    row_scale = lax.dynamic_slice_in_dim(scale_all, me * rows, rows)[:, None]
    normed = (widened - row_mean) * row_scale
    cot_all = spread_quarter(cotangent)

    n_proj = qkv_flat.shape[0]
    projected = lax.psum_scatter(
        lax.dot_general(qkv_flat, hidden_all, contract_cols, preferred_element_type=jnp.float32),
        "dp",
        scatter_dimension=1,
        tiled=True,
    )
    cot_later, projected = lax.optimization_barrier((cot_all, projected))
    projected = projected.astype(jnp.bfloat16).reshape(3, head_slice, HEADS, ROWS)
    up_input = lax.psum_scatter(
        lax.dot_general(up_weight, hidden_all, contract_cols, preferred_element_type=jnp.float32),
        "dp",
        scatter_dimension=1,
        tiled=True,
    )
    activated, gelu_slope = gelu_pair(up_input)
    up_output = activated.astype(jnp.bfloat16)

    by_head = HEADS % n_mp == 0
    if by_head:
        head_group = HEADS // n_mp
        qkv_heads = lax.all_to_all(projected, "mp", split_axis=2, concat_axis=1, tiled=True)
        query_heads = qkv_heads[0].reshape(HS, head_group * QB, TQ)
        pairs = jnp.stack([qkv_heads[1], qkv_heads[2]], axis=2)
        pair_heads = jnp.broadcast_to(
            pairs[:, :, None], (HS, head_group, QB, 2, PATCHES)
        ).reshape(HS, head_group * QB, 2, PATCHES)
        attended, stored = attend(query_heads, pair_heads)
        head_rows = lax.all_to_all(
            attended.reshape(HS, head_group, ROWS), "mp", split_axis=0, concat_axis=1, tiled=True
        ).reshape(head_slice * HEADS, ROWS)
    else:
        queries = projected[0].reshape(head_slice, ITEMS, TQ)
        keyvals = to_items(projected[1:])
        query_heads, pair_heads = (
            lax.all_to_all(queries, "mp", split_axis=1, concat_axis=0, tiled=True),
            lax.all_to_all(keyvals, "mp", split_axis=1, concat_axis=0, tiled=True),
        )
        attended, stored = attend(query_heads, pair_heads)
        head_rows = lax.all_to_all(attended, "mp", split_axis=0, concat_axis=1, tiled=True).reshape(
            head_slice * HEADS, ROWS
        )
    n_att = head_rows.shape[0]
    both_all = lax.all_gather(
        jnp.concatenate([head_rows, up_output], axis=0), "dp", axis=1, tiled=True
    )
    head_rows_all, up_output_all = both_all[:n_att], both_all[n_att:]
    branch = lax.dot_general(
        head_rows_all, head_flat, contract_rows, preferred_element_type=jnp.float32
    ) + lax.dot_general(up_output_all, down_weight, contract_rows, preferred_element_type=jnp.float32)
    branch_local = gather_quarter(branch, rows)
    mixed = (widened + branch_local).astype(jnp.bfloat16)

    down_grad = blockwise_grad(up_output_all, cot_all, n_dp)
    head_grad = blockwise_grad(head_rows_all, cot_all, n_dp)
    back = jnp.concatenate(
        [
            lax.dot_general(head_flat, cot_later, contract_cols, preferred_element_type=jnp.float32),
            lax.dot_general(down_weight, cot_later, contract_cols, preferred_element_type=jnp.float32),
        ],
        axis=0,
    )
    back = lax.psum_scatter(back, "dp", scatter_dimension=1, tiled=True)
    up_upstream = (back[n_att:] * gelu_slope).astype(jnp.bfloat16)
    head_upstream = back[:n_att].astype(jnp.bfloat16).reshape(head_slice, HEADS, ROWS)
    if by_head:
        upstream = lax.all_to_all(
            head_upstream, "mp", split_axis=1, concat_axis=0, tiled=True
        ).reshape(HS, head_group * QB, TQ)
        query_grad, pair_grad = attend_back(upstream, stored)
        pair_sum = jnp.sum(
            pair_grad.reshape(HS, head_group, QB, 2, PATCHES).astype(jnp.float32), axis=2
        ).astype(jnp.bfloat16)
        grads = jnp.stack(
            [query_grad.reshape(HS, head_group, ROWS), pair_sum[:, :, 0], pair_sum[:, :, 1]]
        )
        proj_grad = lax.all_to_all(grads, "mp", split_axis=1, concat_axis=2, tiled=True)
    else:
        upstream = lax.all_to_all(
            head_upstream.reshape(head_slice, ITEMS, TQ), "mp", split_axis=1, concat_axis=0, tiled=True
        )
        query_grad, pair_grad = attend_back(upstream, stored)
        query_local, pair_local = (
            lax.all_to_all(query_grad, "mp", split_axis=0, concat_axis=1, tiled=True),
            lax.all_to_all(pair_grad, "mp", split_axis=0, concat_axis=1, tiled=True),
        )
        proj_grad = jnp.concatenate(
            [query_local.reshape(1, head_slice, HEADS, ROWS), from_items(pair_local)], axis=0
        )
    proj_grad = proj_grad.reshape(3 * head_slice * HEADS, ROWS)
    grads_all = lax.all_gather(
        jnp.concatenate([proj_grad, up_upstream], axis=0), "dp", axis=1, tiled=True
    )
    proj_grad_all, up_upstream_all = grads_all[:n_proj], grads_all[n_proj:]
    qkv_grad = blockwise_grad(proj_grad_all, hidden_all, n_dp)
    up_grad = blockwise_grad(up_upstream_all, hidden_all, n_dp)
    input_partial = lax.dot_general(
        proj_grad_all, qkv_flat, contract_rows, preferred_element_type=jnp.float32
    ) + lax.dot_general(up_upstream_all, up_weight, contract_rows, preferred_element_type=jnp.float32)
    input_local = gather_quarter_exchange(input_partial, rows)

    scaled = input_local * gain_wide
    plain_sum, cross_sum = lax.psum(
        (jnp.sum(scaled, axis=1), jnp.sum(scaled * normed, axis=1)), "mp"
    )
    tokens_grad = row_scale * (
        scaled - plain_sum[:, None] / D - normed * (cross_sum[:, None] / D)
    )
    tokens_grad = tokens_grad + cotangent.astype(jnp.float32)
    gain_piece = jnp.sum(input_local * normed, axis=0)
    gain_grad = lax.psum(gain_piece, "dp")
    return (
        mixed,
        tokens_grad,
        qkv_grad.reshape(qkv_weight.shape),
        head_grad.reshape(head_weight.shape),
        up_grad,
        down_grad,
        gain_grad,
    )


def solution(mesh):
    in_specs = (
        P("dp", "mp"),
        P("mp"),
        P(None, "mp", None, "dp"),
        P("mp", None, "dp"),
        P("mp", "dp"),
        P("mp", "dp"),
        P("dp", "mp"),
    )
    out_specs = (
        P("dp", "mp"),
        P("dp", "mp"),
        P(None, "mp", None, "dp"),
        P("mp", None, "dp"),
        P("mp", "dp"),
        P("mp", "dp"),
        P("mp"),
    )
    return jax.shard_map(shards, mesh=mesh, in_specs=in_specs, out_specs=out_specs, check_vma=False)
```

```python
import math

import jax
import jax.numpy as jnp
from jax import lax
from jax.sharding import PartitionSpec as P

D = 6144
HEADS = 24
HS = 128
PATCHES = 128
QB = 8
IMG_DP = 1
ROWS = 128
TQ = 16
ITEMS = 192


epsilon = 1e-06
contract_rows = (((0,), (0,)), ((), ()))
contract_cols = (((1,), (1,)), ((), ()))


def gelu_pair(inputs):
    normal_cdf = 0.5 * (1.0 + jax.scipy.special.erf(inputs * 0.7071067811865476))
    density = jnp.exp(-0.5 * inputs * inputs) * 0.3989422804014327
    return (inputs * normal_cdf, normal_cdf + inputs * density)


def head_norm(values):
    center = values - jnp.mean(values, axis=0, keepdims=True)
    inverse = lax.rsqrt(jnp.mean(center * center, axis=0, keepdims=True) + epsilon)
    return (center * inverse, inverse)


def norm_back(upstream, normed, inverse):
    return inverse * (
        upstream
        - jnp.mean(upstream, axis=0, keepdims=True)
        - normed * jnp.mean(upstream * normed, axis=0, keepdims=True)
    )


def to_items(pair_rows):
    depth = pair_rows.shape[1]
    shaped = pair_rows.reshape(2, depth, HEADS, IMG_DP, 1, PATCHES)
    spread = jnp.broadcast_to(shaped, (2, depth, HEADS, IMG_DP, QB, PATCHES))
    return jnp.transpose(spread, (1, 2, 3, 4, 0, 5)).reshape(depth, HEADS * IMG_DP * QB, 2, PATCHES)


def from_items(pair_items):
    depth = pair_items.shape[0]
    shaped = pair_items.reshape(depth, HEADS, IMG_DP, QB, 2, PATCHES)
    summed = jnp.sum(shaped.astype(jnp.float32), axis=3).astype(jnp.bfloat16)
    return jnp.transpose(summed, (3, 0, 1, 2, 4)).reshape(2, depth, HEADS, IMG_DP * PATCHES)


def attend(queries, keyvals):
    query_hat, query_scale = head_norm(queries.astype(jnp.float32))
    key_hat, key_scale = head_norm(keyvals[:, :, 0].astype(jnp.float32))
    query_norm = query_hat.astype(jnp.bfloat16)
    key_norm = key_hat.astype(jnp.bfloat16)
    factor = 1.0 / math.sqrt(queries.shape[0])
    scores = (
        jnp.einsum("cia,cib->iab", query_norm, key_norm, preferred_element_type=jnp.float32)
        * factor
    )
    raised = jnp.exp(scores)
    shares = raised / jnp.sum(raised, axis=2, keepdims=True)
    rounded = shares.astype(jnp.bfloat16)
    values = keyvals[:, :, 1]
    attended = jnp.einsum(
        "iab,cib->cia", rounded, values, preferred_element_type=jnp.float32
    ).astype(jnp.bfloat16)
    stored = (
        query_hat,
        query_scale,
        key_hat,
        key_scale,
        query_norm,
        key_norm,
        shares,
        rounded,
        values,
    )
    return (attended, stored)


def attend_back(upstream, stored):
    query_hat, query_scale, key_hat, key_scale, query_norm, key_norm, shares, rounded, values = (
        stored
    )
    factor = 1.0 / math.sqrt(upstream.shape[0])
    share_grad = jnp.einsum("cia,cib->iab", upstream, values, preferred_element_type=jnp.float32)
    value_grad = jnp.einsum("iab,cia->cib", rounded, upstream, preferred_element_type=jnp.float32)
    score_grad = (
        shares * (share_grad - jnp.sum(shares * share_grad, axis=2, keepdims=True)) * factor
    ).astype(jnp.bfloat16)
    query_back = jnp.einsum(
        "iab,cib->cia", score_grad, key_norm, preferred_element_type=jnp.float32
    )
    key_back = jnp.einsum(
        "iab,cia->cib", score_grad, query_norm, preferred_element_type=jnp.float32
    )
    query_grad = norm_back(query_back, query_hat, query_scale).astype(jnp.bfloat16)
    key_grad = norm_back(key_back, key_hat, key_scale).astype(jnp.bfloat16)
    pair_grad = jnp.stack([key_grad, value_grad.astype(jnp.bfloat16)], axis=2)
    return (query_grad, pair_grad)


def swap_pairs(n_dp, n_mp):
    ratio = n_mp // n_dp
    pairs = []
    for row in range(n_dp):
        for col in range(n_mp):
            owner, part = divmod(col, ratio)
            pairs.append((row * n_mp + col, owner * n_mp + row * ratio + part))
    return pairs


def swap(block):
    n_dp, n_mp = lax.axis_size("dp"), lax.axis_size("mp")
    return lax.ppermute(block, ("dp", "mp"), swap_pairs(n_dp, n_mp))


def spread_quarter(block):
    n_dp, n_mp = lax.axis_size("dp"), lax.axis_size("mp")
    ratio = n_mp // n_dp
    rows, width = block.shape
    copies = jnp.broadcast_to(swap(block)[None], (n_mp, rows, width))
    pieces = lax.all_to_all(copies, "mp", split_axis=0, concat_axis=0, tiled=True)
    pieces = pieces.reshape(n_dp, ratio, rows, width)
    return jnp.transpose(pieces, (0, 2, 1, 3)).reshape(n_dp * rows, ratio * width)


def spread_quarter_rows(block):
    n_dp, n_mp = lax.axis_size("dp"), lax.axis_size("mp")
    ratio = n_mp // n_dp
    rows, width = block.shape
    copies = jnp.broadcast_to(swap(block)[None], (n_mp, rows, width))
    pieces = lax.all_to_all(copies, "mp", split_axis=0, concat_axis=0, tiled=True)
    pieces = pieces.reshape(n_dp, ratio, rows, width)
    return jnp.transpose(pieces, (0, 2, 1, 3)).reshape(n_dp, rows, ratio * width)


def gather_quarter(partial, rows):
    n_dp, n_mp = lax.axis_size("dp"), lax.axis_size("mp")
    ratio = n_mp // n_dp
    width = partial.shape[1] // ratio
    pieces = partial.reshape(n_dp, rows, ratio, width)
    pieces = jnp.transpose(pieces, (0, 2, 1, 3)).reshape(n_mp, rows, width)
    summed = lax.psum_scatter(pieces, "mp", scatter_dimension=0, tiled=True)
    return swap(summed.reshape(rows, width))


def gather_quarter_exchange(partial, rows):
    n_dp, n_mp = lax.axis_size("dp"), lax.axis_size("mp")
    ratio = n_mp // n_dp
    width = partial.shape[1] // ratio
    pieces = partial.reshape(n_dp, rows, ratio, width)
    pieces = jnp.transpose(pieces, (0, 2, 1, 3)).reshape(n_mp, rows, width)
    received = lax.all_to_all(pieces, "mp", split_axis=0, concat_axis=0, tiled=True)
    return swap(jnp.sum(received, axis=0))


def blockwise_grad(left, right, n_blocks):
    rows = left.shape[1] // n_blocks
    total = None
    for block in range(n_blocks):
        piece = jnp.dot(
            left[:, block * rows:(block + 1) * rows],
            right[block * rows:(block + 1) * rows],
            preferred_element_type=jnp.float32,
        ).astype(jnp.bfloat16).astype(jnp.float32)
        total = piece if total is None else total + piece
    return total.astype(jnp.bfloat16)


def shards(tokens, norm_gain, qkv_weight, head_weight, up_weight, down_weight, cotangent):
    n_dp, n_mp = lax.axis_size("dp"), lax.axis_size("mp")
    head_slice = HS // n_mp
    quarter = qkv_weight.shape[-1]
    rows, width = tokens.shape
    qkv_flat = qkv_weight.reshape(-1, quarter)
    head_flat = head_weight.reshape(-1, quarter)

    widened = tokens.astype(jnp.float32)
    gain_wide = norm_gain.astype(jnp.float32)
    with_gain = jnp.concatenate([tokens, norm_gain.reshape(1, width)], axis=0)
    spread_in = spread_quarter_rows(with_gain)
    tokens_all = spread_in[:, :rows].reshape(-1, quarter).astype(jnp.float32)
    gain_quarter = spread_in[0, rows].astype(jnp.float32)
    part_mean = jnp.mean(tokens_all, axis=1)
    part_center = tokens_all - part_mean[:, None]
    part_m2 = jnp.sum(part_center * part_center, axis=1)
    parts = lax.all_gather(jnp.stack([part_mean, part_m2]), "dp", axis=0, tiled=False)
    mean_all = jnp.mean(parts[:, 0], axis=0)
    spread = parts[:, 0] - mean_all[None, :]
    m2_all = jnp.sum(parts[:, 1], axis=0) + quarter * jnp.sum(spread * spread, axis=0)
    scale_all = lax.rsqrt(m2_all / D + epsilon)
    hidden_all = (
        ((tokens_all - mean_all[:, None]) * scale_all[:, None]) * gain_quarter
    ).astype(jnp.bfloat16)
    me = lax.axis_index("dp")
    row_mean = lax.dynamic_slice_in_dim(mean_all, me * rows, rows)[:, None]
    row_scale = lax.dynamic_slice_in_dim(scale_all, me * rows, rows)[:, None]
    normed = (widened - row_mean) * row_scale
    cot_all = spread_quarter(cotangent)

    n_proj = qkv_flat.shape[0]
    proj_up = jnp.concatenate(
        [
            lax.dot_general(qkv_flat, hidden_all, contract_cols, preferred_element_type=jnp.float32),
            lax.dot_general(up_weight, hidden_all, contract_cols, preferred_element_type=jnp.float32),
        ],
        axis=0,
    )
    proj_up = lax.psum_scatter(proj_up, "dp", scatter_dimension=1, tiled=True)
    cot_later, proj_up = lax.optimization_barrier((cot_all, proj_up))
    projected = proj_up[:n_proj].astype(jnp.bfloat16).reshape(3, head_slice, HEADS, ROWS)
    up_input = proj_up[n_proj:]
    activated, gelu_slope = gelu_pair(up_input)
    up_output = activated.astype(jnp.bfloat16)

    by_head = HEADS % n_mp == 0
    if by_head:
        head_group = HEADS // n_mp
        qkv_heads = lax.all_to_all(projected, "mp", split_axis=2, concat_axis=1, tiled=True)
        query_heads = qkv_heads[0].reshape(HS, head_group * QB, TQ)
        pairs = jnp.stack([qkv_heads[1], qkv_heads[2]], axis=2)
        pair_heads = jnp.broadcast_to(
            pairs[:, :, None], (HS, head_group, QB, 2, PATCHES)
        ).reshape(HS, head_group * QB, 2, PATCHES)
        attended, stored = attend(query_heads, pair_heads)
        head_rows = lax.all_to_all(
            attended.reshape(HS, head_group, ROWS), "mp", split_axis=0, concat_axis=1, tiled=True
        ).reshape(head_slice * HEADS, ROWS)
    else:
        queries = projected[0].reshape(head_slice, ITEMS, TQ)
        keyvals = to_items(projected[1:])
        query_heads, pair_heads = (
            lax.all_to_all(queries, "mp", split_axis=1, concat_axis=0, tiled=True),
            lax.all_to_all(keyvals, "mp", split_axis=1, concat_axis=0, tiled=True),
        )
        attended, stored = attend(query_heads, pair_heads)
        head_rows = lax.all_to_all(attended, "mp", split_axis=0, concat_axis=1, tiled=True).reshape(
            head_slice * HEADS, ROWS
        )
    n_att = head_rows.shape[0]
    both_all = lax.all_gather(
        jnp.concatenate([head_rows, up_output], axis=0), "dp", axis=1, tiled=True
    )
    head_rows_all, up_output_all = both_all[:n_att], both_all[n_att:]
    branch = lax.dot_general(
        head_rows_all, head_flat, contract_rows, preferred_element_type=jnp.float32
    ) + lax.dot_general(up_output_all, down_weight, contract_rows, preferred_element_type=jnp.float32)
    n_dp_ratio = n_mp // n_dp
    branch_pieces = jnp.transpose(
        branch.reshape(n_dp, rows, n_dp_ratio, width), (0, 2, 1, 3)
    ).reshape(n_mp, rows, width)
    branch_summed = lax.psum_scatter(branch_pieces, "mp", scatter_dimension=0, tiled=True)

    down_grad = blockwise_grad(up_output_all, cot_all, n_dp)
    head_grad = blockwise_grad(head_rows_all, cot_all, n_dp)
    back = jnp.concatenate(
        [
            lax.dot_general(head_flat, cot_later, contract_cols, preferred_element_type=jnp.float32),
            lax.dot_general(down_weight, cot_later, contract_cols, preferred_element_type=jnp.float32),
        ],
        axis=0,
    )
    back = lax.psum_scatter(back, "dp", scatter_dimension=1, tiled=True)
    up_upstream = (back[n_att:] * gelu_slope).astype(jnp.bfloat16)
    head_upstream = back[:n_att].astype(jnp.bfloat16).reshape(head_slice, HEADS, ROWS)
    if by_head:
        upstream = lax.all_to_all(
            head_upstream, "mp", split_axis=1, concat_axis=0, tiled=True
        ).reshape(HS, head_group * QB, TQ)
        query_grad, pair_grad = attend_back(upstream, stored)
        pair_sum = jnp.sum(
            pair_grad.reshape(HS, head_group, QB, 2, PATCHES).astype(jnp.float32), axis=2
        ).astype(jnp.bfloat16)
        grads = jnp.stack(
            [query_grad.reshape(HS, head_group, ROWS), pair_sum[:, :, 0], pair_sum[:, :, 1]]
        )
        proj_grad = lax.all_to_all(grads, "mp", split_axis=1, concat_axis=2, tiled=True)
    else:
        upstream = lax.all_to_all(
            head_upstream.reshape(head_slice, ITEMS, TQ), "mp", split_axis=1, concat_axis=0, tiled=True
        )
        query_grad, pair_grad = attend_back(upstream, stored)
        query_local, pair_local = (
            lax.all_to_all(query_grad, "mp", split_axis=0, concat_axis=1, tiled=True),
            lax.all_to_all(pair_grad, "mp", split_axis=0, concat_axis=1, tiled=True),
        )
        proj_grad = jnp.concatenate(
            [query_local.reshape(1, head_slice, HEADS, ROWS), from_items(pair_local)], axis=0
        )
    proj_grad = proj_grad.reshape(3 * head_slice * HEADS, ROWS)
    grads_all = lax.all_gather(
        jnp.concatenate([proj_grad, up_upstream], axis=0), "dp", axis=1, tiled=True
    )
    proj_grad_all, up_upstream_all = grads_all[:n_proj], grads_all[n_proj:]
    qkv_grad = blockwise_grad(proj_grad_all, hidden_all, n_dp)
    up_grad = blockwise_grad(up_upstream_all, hidden_all, n_dp)
    input_partial = lax.dot_general(
        proj_grad_all, qkv_flat, contract_rows, preferred_element_type=jnp.float32
    ) + lax.dot_general(up_upstream_all, up_weight, contract_rows, preferred_element_type=jnp.float32)
    input_local = gather_quarter_exchange(input_partial, rows)

    scaled = input_local * gain_wide
    plain_sum, cross_sum = lax.psum(
        (jnp.sum(scaled, axis=1), jnp.sum(scaled * normed, axis=1)), "mp"
    )
    tokens_grad = row_scale * (
        scaled - plain_sum[:, None] / D - normed * (cross_sum[:, None] / D)
    )
    tokens_grad = tokens_grad + cotangent.astype(jnp.float32)
    branch_summed, tokens_grad = lax.optimization_barrier((branch_summed, tokens_grad))
    branch_local = swap(branch_summed.reshape(rows, width))
    mixed = (widened + branch_local).astype(jnp.bfloat16)
    gain_piece = jnp.sum(input_local * normed, axis=0)
    gain_grad = lax.psum(gain_piece, "dp")
    return (
        mixed,
        tokens_grad,
        qkv_grad.reshape(qkv_weight.shape),
        head_grad.reshape(head_weight.shape),
        up_grad,
        down_grad,
        gain_grad,
    )


def solution(mesh):
    in_specs = (
        P("dp", "mp"),
        P("mp"),
        P(None, "mp", None, "dp"),
        P("mp", None, "dp"),
        P("mp", "dp"),
        P("mp", "dp"),
        P("dp", "mp"),
    )
    out_specs = (
        P("dp", "mp"),
        P("dp", "mp"),
        P(None, "mp", None, "dp"),
        P("mp", None, "dp"),
        P("mp", "dp"),
        P("mp", "dp"),
        P("mp"),
    )
    return jax.shard_map(shards, mesh=mesh, in_specs=in_specs, out_specs=out_specs, check_vma=False)
```

```python
import math

import jax
import jax.numpy as jnp
from jax import lax
from jax.sharding import PartitionSpec as P

D = 6144
HEADS = 24
HS = 128
PATCHES = 128
QB = 8
IMG_DP = 1
ROWS = 128
TQ = 16
ITEMS = 192


epsilon = 1e-06
contract_rows = (((0,), (0,)), ((), ()))
contract_cols = (((1,), (1,)), ((), ()))


def gelu_pair(inputs):
    normal_cdf = 0.5 * (1.0 + jax.scipy.special.erf(inputs * 0.7071067811865476))
    density = jnp.exp(-0.5 * inputs * inputs) * 0.3989422804014327
    return (inputs * normal_cdf, normal_cdf + inputs * density)


def head_norm(values):
    center = values - jnp.mean(values, axis=0, keepdims=True)
    inverse = lax.rsqrt(jnp.mean(center * center, axis=0, keepdims=True) + epsilon)
    return (center * inverse, inverse)


def norm_back(upstream, normed, inverse):
    return inverse * (
        upstream
        - jnp.mean(upstream, axis=0, keepdims=True)
        - normed * jnp.mean(upstream * normed, axis=0, keepdims=True)
    )


def to_items(pair_rows):
    depth = pair_rows.shape[1]
    shaped = pair_rows.reshape(2, depth, HEADS, IMG_DP, 1, PATCHES)
    spread = jnp.broadcast_to(shaped, (2, depth, HEADS, IMG_DP, QB, PATCHES))
    return jnp.transpose(spread, (1, 2, 3, 4, 0, 5)).reshape(depth, HEADS * IMG_DP * QB, 2, PATCHES)


def from_items(pair_items):
    depth = pair_items.shape[0]
    shaped = pair_items.reshape(depth, HEADS, IMG_DP, QB, 2, PATCHES)
    summed = jnp.sum(shaped.astype(jnp.float32), axis=3).astype(jnp.bfloat16)
    return jnp.transpose(summed, (3, 0, 1, 2, 4)).reshape(2, depth, HEADS, IMG_DP * PATCHES)


def attend(queries, keyvals):
    query_hat, query_scale = head_norm(queries.astype(jnp.float32))
    key_hat, key_scale = head_norm(keyvals[:, :, 0].astype(jnp.float32))
    query_norm = query_hat.astype(jnp.bfloat16)
    key_norm = key_hat.astype(jnp.bfloat16)
    factor = 1.0 / math.sqrt(queries.shape[0])
    scores = (
        jnp.einsum("cia,cib->iab", query_norm, key_norm, preferred_element_type=jnp.float32)
        * factor
    )
    raised = jnp.exp(scores)
    shares = raised / jnp.sum(raised, axis=2, keepdims=True)
    rounded = shares.astype(jnp.bfloat16)
    values = keyvals[:, :, 1]
    attended = jnp.einsum(
        "iab,cib->cia", rounded, values, preferred_element_type=jnp.float32
    ).astype(jnp.bfloat16)
    stored = (
        query_hat,
        query_scale,
        key_hat,
        key_scale,
        query_norm,
        key_norm,
        shares,
        rounded,
        values,
    )
    return (attended, stored)


def attend_back(upstream, stored):
    query_hat, query_scale, key_hat, key_scale, query_norm, key_norm, shares, rounded, values = (
        stored
    )
    factor = 1.0 / math.sqrt(upstream.shape[0])
    share_grad = jnp.einsum("cia,cib->iab", upstream, values, preferred_element_type=jnp.float32)
    value_grad = jnp.einsum("iab,cia->cib", rounded, upstream, preferred_element_type=jnp.float32)
    score_grad = (
        shares * (share_grad - jnp.sum(shares * share_grad, axis=2, keepdims=True)) * factor
    ).astype(jnp.bfloat16)
    query_back = jnp.einsum(
        "iab,cib->cia", score_grad, key_norm, preferred_element_type=jnp.float32
    )
    key_back = jnp.einsum(
        "iab,cia->cib", score_grad, query_norm, preferred_element_type=jnp.float32
    )
    query_grad = norm_back(query_back, query_hat, query_scale).astype(jnp.bfloat16)
    key_grad = norm_back(key_back, key_hat, key_scale).astype(jnp.bfloat16)
    pair_grad = jnp.stack([key_grad, value_grad.astype(jnp.bfloat16)], axis=2)
    return (query_grad, pair_grad)


def swap_pairs(n_dp, n_mp):
    ratio = n_mp // n_dp
    pairs = []
    for row in range(n_dp):
        for col in range(n_mp):
            owner, part = divmod(col, ratio)
            pairs.append((row * n_mp + col, owner * n_mp + row * ratio + part))
    return pairs


def swap(block):
    n_dp, n_mp = lax.axis_size("dp"), lax.axis_size("mp")
    return lax.ppermute(block, ("dp", "mp"), swap_pairs(n_dp, n_mp))


def spread_quarter(block):
    n_dp, n_mp = lax.axis_size("dp"), lax.axis_size("mp")
    ratio = n_mp // n_dp
    rows, width = block.shape
    copies = jnp.broadcast_to(swap(block)[None], (n_mp, rows, width))
    pieces = lax.all_to_all(copies, "mp", split_axis=0, concat_axis=0, tiled=True)
    pieces = pieces.reshape(n_dp, ratio, rows, width)
    return jnp.transpose(pieces, (0, 2, 1, 3)).reshape(n_dp * rows, ratio * width)


def spread_quarter_rows(block):
    n_dp, n_mp = lax.axis_size("dp"), lax.axis_size("mp")
    ratio = n_mp // n_dp
    rows, width = block.shape
    copies = jnp.broadcast_to(swap(block)[None], (n_mp, rows, width))
    pieces = lax.all_to_all(copies, "mp", split_axis=0, concat_axis=0, tiled=True)
    pieces = pieces.reshape(n_dp, ratio, rows, width)
    return jnp.transpose(pieces, (0, 2, 1, 3)).reshape(n_dp, rows, ratio * width)


def gather_quarter(partial, rows):
    n_dp, n_mp = lax.axis_size("dp"), lax.axis_size("mp")
    ratio = n_mp // n_dp
    width = partial.shape[1] // ratio
    pieces = partial.reshape(n_dp, rows, ratio, width)
    pieces = jnp.transpose(pieces, (0, 2, 1, 3)).reshape(n_mp, rows, width)
    summed = lax.psum_scatter(pieces, "mp", scatter_dimension=0, tiled=True)
    return swap(summed.reshape(rows, width))


def gather_quarter_exchange(partial, rows):
    n_dp, n_mp = lax.axis_size("dp"), lax.axis_size("mp")
    ratio = n_mp // n_dp
    width = partial.shape[1] // ratio
    pieces = partial.reshape(n_dp, rows, ratio, width)
    pieces = jnp.transpose(pieces, (0, 2, 1, 3)).reshape(n_mp, rows, width)
    received = lax.all_to_all(pieces, "mp", split_axis=0, concat_axis=0, tiled=True)
    return swap(jnp.sum(received, axis=0))


def blockwise_grad(left, right, n_blocks):
    rows = left.shape[1] // n_blocks
    total = None
    for block in range(n_blocks):
        piece = jnp.dot(
            left[:, block * rows:(block + 1) * rows],
            right[block * rows:(block + 1) * rows],
            preferred_element_type=jnp.float32,
        ).astype(jnp.bfloat16).astype(jnp.float32)
        total = piece if total is None else total + piece
    return total.astype(jnp.bfloat16)


def shards(tokens, norm_gain, qkv_weight, head_weight, up_weight, down_weight, cotangent):
    n_dp, n_mp = lax.axis_size("dp"), lax.axis_size("mp")
    head_slice = HS // n_mp
    quarter = qkv_weight.shape[-1]
    rows, width = tokens.shape
    qkv_flat = qkv_weight.reshape(-1, quarter)
    head_flat = head_weight.reshape(-1, quarter)

    widened = tokens.astype(jnp.float32)
    gain_wide = norm_gain.astype(jnp.float32)
    with_gain = jnp.concatenate([tokens, norm_gain.reshape(1, width)], axis=0)
    spread_in = spread_quarter_rows(with_gain)
    tokens_all = spread_in[:, :rows].reshape(-1, quarter).astype(jnp.float32)
    gain_quarter = spread_in[0, rows].astype(jnp.float32)
    part_mean = jnp.mean(tokens_all, axis=1)
    part_center = tokens_all - part_mean[:, None]
    part_m2 = jnp.sum(part_center * part_center, axis=1)
    parts = lax.all_gather(jnp.stack([part_mean, part_m2]), "dp", axis=0, tiled=False)
    mean_all = jnp.mean(parts[:, 0], axis=0)
    spread = parts[:, 0] - mean_all[None, :]
    m2_all = jnp.sum(parts[:, 1], axis=0) + quarter * jnp.sum(spread * spread, axis=0)
    scale_all = lax.rsqrt(m2_all / D + epsilon)
    hidden_all = (
        ((tokens_all - mean_all[:, None]) * scale_all[:, None]) * gain_quarter
    ).astype(jnp.bfloat16)
    me = lax.axis_index("dp")
    row_mean = lax.dynamic_slice_in_dim(mean_all, me * rows, rows)[:, None]
    row_scale = lax.dynamic_slice_in_dim(scale_all, me * rows, rows)[:, None]
    normed = (widened - row_mean) * row_scale
    cot_all = spread_quarter(cotangent)

    n_proj = qkv_flat.shape[0]
    proj_up = jnp.concatenate(
        [
            lax.dot_general(qkv_flat, hidden_all, contract_cols, preferred_element_type=jnp.float32),
            lax.dot_general(up_weight, hidden_all, contract_cols, preferred_element_type=jnp.float32),
        ],
        axis=0,
    )
    proj_up = lax.psum_scatter(proj_up, "dp", scatter_dimension=1, tiled=True)
    cot_later, proj_up = lax.optimization_barrier((cot_all, proj_up))
    projected = proj_up[:n_proj].astype(jnp.bfloat16).reshape(3, head_slice, HEADS, ROWS)
    up_input = proj_up[n_proj:]
    activated, gelu_slope = gelu_pair(up_input)
    up_output = activated.astype(jnp.bfloat16)

    by_head = HEADS % n_mp == 0
    if by_head:
        head_group = HEADS // n_mp
        qkv_heads = lax.all_to_all(projected, "mp", split_axis=2, concat_axis=1, tiled=True)
        query_heads = qkv_heads[0].reshape(HS, head_group * QB, TQ)
        pairs = jnp.stack([qkv_heads[1], qkv_heads[2]], axis=2)
        pair_heads = jnp.broadcast_to(
            pairs[:, :, None], (HS, head_group, QB, 2, PATCHES)
        ).reshape(HS, head_group * QB, 2, PATCHES)
        attended, stored = attend(query_heads, pair_heads)
        head_rows = lax.all_to_all(
            attended.reshape(HS, head_group, ROWS), "mp", split_axis=0, concat_axis=1, tiled=True
        ).reshape(head_slice * HEADS, ROWS)
    else:
        queries = projected[0].reshape(head_slice, ITEMS, TQ)
        keyvals = to_items(projected[1:])
        query_heads, pair_heads = (
            lax.all_to_all(queries, "mp", split_axis=1, concat_axis=0, tiled=True),
            lax.all_to_all(keyvals, "mp", split_axis=1, concat_axis=0, tiled=True),
        )
        attended, stored = attend(query_heads, pair_heads)
        head_rows = lax.all_to_all(attended, "mp", split_axis=0, concat_axis=1, tiled=True).reshape(
            head_slice * HEADS, ROWS
        )
    n_att = head_rows.shape[0]
    both_all = lax.all_gather(
        jnp.concatenate([head_rows, up_output], axis=0), "dp", axis=1, tiled=True
    )
    head_rows_all, up_output_all = both_all[:n_att], both_all[n_att:]
    branch = lax.dot_general(
        head_rows_all, head_flat, contract_rows, preferred_element_type=jnp.float32
    ) + lax.dot_general(up_output_all, down_weight, contract_rows, preferred_element_type=jnp.float32)
    branch_local = gather_quarter(branch, rows)
    mixed = (widened + branch_local).astype(jnp.bfloat16)

    down_grad = blockwise_grad(up_output_all, cot_all, n_dp)
    head_grad = blockwise_grad(head_rows_all, cot_all, n_dp)
    back = jnp.concatenate(
        [
            lax.dot_general(head_flat, cot_later, contract_cols, preferred_element_type=jnp.float32),
            lax.dot_general(down_weight, cot_later, contract_cols, preferred_element_type=jnp.float32),
        ],
        axis=0,
    )
    back = lax.psum_scatter(back, "dp", scatter_dimension=1, tiled=True)
    up_upstream = (back[n_att:] * gelu_slope).astype(jnp.bfloat16)
    up_upstream_all = lax.all_gather(up_upstream, "dp", axis=1, tiled=True)
    head_upstream = back[:n_att].astype(jnp.bfloat16).reshape(head_slice, HEADS, ROWS)
    if by_head:
        upstream = lax.all_to_all(
            head_upstream, "mp", split_axis=1, concat_axis=0, tiled=True
        ).reshape(HS, head_group * QB, TQ)
        query_grad, pair_grad = attend_back(upstream, stored)
        pair_sum = jnp.sum(
            pair_grad.reshape(HS, head_group, QB, 2, PATCHES).astype(jnp.float32), axis=2
        ).astype(jnp.bfloat16)
        grads = jnp.stack(
            [query_grad.reshape(HS, head_group, ROWS), pair_sum[:, :, 0], pair_sum[:, :, 1]]
        )
        proj_grad = lax.all_to_all(grads, "mp", split_axis=1, concat_axis=2, tiled=True)
    else:
        upstream = lax.all_to_all(
            head_upstream.reshape(head_slice, ITEMS, TQ), "mp", split_axis=1, concat_axis=0, tiled=True
        )
        query_grad, pair_grad = attend_back(upstream, stored)
        query_local, pair_local = (
            lax.all_to_all(query_grad, "mp", split_axis=0, concat_axis=1, tiled=True),
            lax.all_to_all(pair_grad, "mp", split_axis=0, concat_axis=1, tiled=True),
        )
        proj_grad = jnp.concatenate(
            [query_local.reshape(1, head_slice, HEADS, ROWS), from_items(pair_local)], axis=0
        )
    proj_grad = proj_grad.reshape(3 * head_slice * HEADS, ROWS)
    proj_grad_all = lax.all_gather(proj_grad, "dp", axis=1, tiled=True)
    qkv_grad = blockwise_grad(proj_grad_all, hidden_all, n_dp)
    up_grad = blockwise_grad(up_upstream_all, hidden_all, n_dp)
    input_partial = lax.dot_general(
        proj_grad_all, qkv_flat, contract_rows, preferred_element_type=jnp.float32
    ) + lax.dot_general(up_upstream_all, up_weight, contract_rows, preferred_element_type=jnp.float32)
    input_local = gather_quarter_exchange(input_partial, rows)

    scaled = input_local * gain_wide
    plain_sum, cross_sum = lax.psum(
        (jnp.sum(scaled, axis=1), jnp.sum(scaled * normed, axis=1)), "mp"
    )
    tokens_grad = row_scale * (
        scaled - plain_sum[:, None] / D - normed * (cross_sum[:, None] / D)
    )
    tokens_grad = tokens_grad + cotangent.astype(jnp.float32)
    gain_piece = jnp.sum(input_local * normed, axis=0)
    gain_grad = lax.psum(gain_piece, "dp")
    return (
        mixed,
        tokens_grad,
        qkv_grad.reshape(qkv_weight.shape),
        head_grad.reshape(head_weight.shape),
        up_grad,
        down_grad,
        gain_grad,
    )


def solution(mesh):
    in_specs = (
        P("dp", "mp"),
        P("mp"),
        P(None, "mp", None, "dp"),
        P("mp", None, "dp"),
        P("mp", "dp"),
        P("mp", "dp"),
        P("dp", "mp"),
    )
    out_specs = (
        P("dp", "mp"),
        P("dp", "mp"),
        P(None, "mp", None, "dp"),
        P("mp", None, "dp"),
        P("mp", "dp"),
        P("mp", "dp"),
        P("mp"),
    )
    return jax.shard_map(shards, mesh=mesh, in_specs=in_specs, out_specs=out_specs, check_vma=False)
```

```python
import math

import jax
import jax.numpy as jnp
from jax import lax
from jax.sharding import PartitionSpec as P

D = 6144
HEADS = 24
HS = 128
PATCHES = 128
QB = 8
IMG_DP = 1
ROWS = 128
TQ = 16
ITEMS = 192


epsilon = 1e-06
contract_rows = (((0,), (0,)), ((), ()))
contract_cols = (((1,), (1,)), ((), ()))


def gelu_pair(inputs):
    normal_cdf = 0.5 * (1.0 + jax.scipy.special.erf(inputs * 0.7071067811865476))
    density = jnp.exp(-0.5 * inputs * inputs) * 0.3989422804014327
    return (inputs * normal_cdf, normal_cdf + inputs * density)


def head_norm(values):
    center = values - jnp.mean(values, axis=0, keepdims=True)
    inverse = lax.rsqrt(jnp.mean(center * center, axis=0, keepdims=True) + epsilon)
    return (center * inverse, inverse)


def norm_back(upstream, normed, inverse):
    return inverse * (
        upstream
        - jnp.mean(upstream, axis=0, keepdims=True)
        - normed * jnp.mean(upstream * normed, axis=0, keepdims=True)
    )


def to_items(pair_rows):
    depth = pair_rows.shape[1]
    shaped = pair_rows.reshape(2, depth, HEADS, IMG_DP, 1, PATCHES)
    spread = jnp.broadcast_to(shaped, (2, depth, HEADS, IMG_DP, QB, PATCHES))
    return jnp.transpose(spread, (1, 2, 3, 4, 0, 5)).reshape(depth, HEADS * IMG_DP * QB, 2, PATCHES)


def from_items(pair_items):
    depth = pair_items.shape[0]
    shaped = pair_items.reshape(depth, HEADS, IMG_DP, QB, 2, PATCHES)
    summed = jnp.sum(shaped.astype(jnp.float32), axis=3).astype(jnp.bfloat16)
    return jnp.transpose(summed, (3, 0, 1, 2, 4)).reshape(2, depth, HEADS, IMG_DP * PATCHES)


def attend(queries, keyvals):
    query_hat, query_scale = head_norm(queries.astype(jnp.float32))
    key_hat, key_scale = head_norm(keyvals[:, :, 0].astype(jnp.float32))
    query_norm = query_hat.astype(jnp.bfloat16)
    key_norm = key_hat.astype(jnp.bfloat16)
    factor = 1.0 / math.sqrt(queries.shape[0])
    scores = (
        jnp.einsum("cia,cib->iab", query_norm, key_norm, preferred_element_type=jnp.float32)
        * factor
    )
    raised = jnp.exp(scores)
    shares = raised / jnp.sum(raised, axis=2, keepdims=True)
    rounded = shares.astype(jnp.bfloat16)
    values = keyvals[:, :, 1]
    attended = jnp.einsum(
        "iab,cib->cia", rounded, values, preferred_element_type=jnp.float32
    ).astype(jnp.bfloat16)
    stored = (
        query_hat,
        query_scale,
        key_hat,
        key_scale,
        query_norm,
        key_norm,
        shares,
        rounded,
        values,
    )
    return (attended, stored)


def attend_back(upstream, stored):
    query_hat, query_scale, key_hat, key_scale, query_norm, key_norm, shares, rounded, values = (
        stored
    )
    factor = 1.0 / math.sqrt(upstream.shape[0])
    share_grad = jnp.einsum("cia,cib->iab", upstream, values, preferred_element_type=jnp.float32)
    value_grad = jnp.einsum("iab,cia->cib", rounded, upstream, preferred_element_type=jnp.float32)
    score_grad = (
        shares * (share_grad - jnp.sum(shares * share_grad, axis=2, keepdims=True)) * factor
    ).astype(jnp.bfloat16)
    query_back = jnp.einsum(
        "iab,cib->cia", score_grad, key_norm, preferred_element_type=jnp.float32
    )
    key_back = jnp.einsum(
        "iab,cia->cib", score_grad, query_norm, preferred_element_type=jnp.float32
    )
    query_grad = norm_back(query_back, query_hat, query_scale).astype(jnp.bfloat16)
    key_grad = norm_back(key_back, key_hat, key_scale).astype(jnp.bfloat16)
    pair_grad = jnp.stack([key_grad, value_grad.astype(jnp.bfloat16)], axis=2)
    return (query_grad, pair_grad)


def swap_pairs(n_dp, n_mp):
    ratio = n_mp // n_dp
    pairs = []
    for row in range(n_dp):
        for col in range(n_mp):
            owner, part = divmod(col, ratio)
            pairs.append((row * n_mp + col, owner * n_mp + row * ratio + part))
    return pairs


def swap_by_part_pairs(n_dp, n_mp):
    ratio = n_mp // n_dp
    pairs = []
    for row in range(n_dp):
        for col in range(n_mp):
            part, owner = divmod(col, n_dp)
            pairs.append((row * n_mp + col, owner * n_mp + row * ratio + part))
    return pairs


def swap(block):
    n_dp, n_mp = lax.axis_size("dp"), lax.axis_size("mp")
    return lax.ppermute(block, ("dp", "mp"), swap_pairs(n_dp, n_mp))


def spread_quarter(block):
    n_dp, n_mp = lax.axis_size("dp"), lax.axis_size("mp")
    ratio = n_mp // n_dp
    rows, width = block.shape
    copies = jnp.broadcast_to(swap(block)[None], (n_mp, rows, width))
    pieces = lax.all_to_all(copies, "mp", split_axis=0, concat_axis=0, tiled=True)
    pieces = pieces.reshape(n_dp, ratio, rows, width)
    return jnp.transpose(pieces, (0, 2, 1, 3)).reshape(n_dp * rows, ratio * width)


def spread_quarter_rows(block):
    n_dp, n_mp = lax.axis_size("dp"), lax.axis_size("mp")
    ratio = n_mp // n_dp
    rows, width = block.shape
    copies = jnp.broadcast_to(swap(block)[None], (n_mp, rows, width))
    pieces = lax.all_to_all(copies, "mp", split_axis=0, concat_axis=0, tiled=True)
    pieces = pieces.reshape(n_dp, ratio, rows, width)
    return jnp.transpose(pieces, (0, 2, 1, 3)).reshape(n_dp, rows, ratio * width)


def gather_quarter(partial, rows):
    n_dp, n_mp = lax.axis_size("dp"), lax.axis_size("mp")
    ratio = n_mp // n_dp
    width = partial.shape[1] // ratio
    pieces = partial.reshape(n_dp, rows, ratio, width)
    pieces = jnp.transpose(pieces, (0, 2, 1, 3)).reshape(n_mp, rows, width)
    summed = lax.psum_scatter(pieces, "mp", scatter_dimension=0, tiled=True)
    return swap(summed.reshape(rows, width))


def gather_quarter_exchange(partial, rows):
    n_dp, n_mp = lax.axis_size("dp"), lax.axis_size("mp")
    ratio = n_mp // n_dp
    width = partial.shape[1] // ratio
    pieces = partial.reshape(n_dp, rows, ratio, width)
    pieces = jnp.transpose(pieces, (0, 2, 1, 3)).reshape(n_mp, rows, width)
    received = lax.all_to_all(pieces, "mp", split_axis=0, concat_axis=0, tiled=True)
    return swap(jnp.sum(received, axis=0))


def blockwise_grad(left, right, n_blocks):
    rows = left.shape[1] // n_blocks
    total = None
    for block in range(n_blocks):
        piece = jnp.dot(
            left[:, block * rows:(block + 1) * rows],
            right[block * rows:(block + 1) * rows],
            preferred_element_type=jnp.float32,
        ).astype(jnp.bfloat16).astype(jnp.float32)
        total = piece if total is None else total + piece
    return total.astype(jnp.bfloat16)


def shards(tokens, norm_gain, qkv_weight, head_weight, up_weight, down_weight, cotangent):
    n_dp, n_mp = lax.axis_size("dp"), lax.axis_size("mp")
    head_slice = HS // n_mp
    quarter = qkv_weight.shape[-1]
    rows, width = tokens.shape
    qkv_flat = qkv_weight.reshape(-1, quarter)
    head_flat = head_weight.reshape(-1, quarter)

    widened = tokens.astype(jnp.float32)
    gain_wide = norm_gain.astype(jnp.float32)
    with_gain = jnp.concatenate([tokens, norm_gain.reshape(1, width)], axis=0)
    spread_in = spread_quarter_rows(with_gain)
    tokens_all = spread_in[:, :rows].reshape(-1, quarter).astype(jnp.float32)
    gain_quarter = spread_in[0, rows].astype(jnp.float32)
    part_mean = jnp.mean(tokens_all, axis=1)
    part_center = tokens_all - part_mean[:, None]
    part_m2 = jnp.sum(part_center * part_center, axis=1)
    parts = lax.all_gather(jnp.stack([part_mean, part_m2]), "dp", axis=0, tiled=False)
    mean_all = jnp.mean(parts[:, 0], axis=0)
    spread = parts[:, 0] - mean_all[None, :]
    m2_all = jnp.sum(parts[:, 1], axis=0) + quarter * jnp.sum(spread * spread, axis=0)
    scale_all = lax.rsqrt(m2_all / D + epsilon)
    hidden_all = (
        ((tokens_all - mean_all[:, None]) * scale_all[:, None]) * gain_quarter
    ).astype(jnp.bfloat16)
    me = lax.axis_index("dp")
    row_mean = lax.dynamic_slice_in_dim(mean_all, me * rows, rows)[:, None]
    row_scale = lax.dynamic_slice_in_dim(scale_all, me * rows, rows)[:, None]
    normed = (widened - row_mean) * row_scale
    cot_all = spread_quarter(cotangent)

    n_proj = qkv_flat.shape[0]
    proj_up = jnp.concatenate(
        [
            lax.dot_general(qkv_flat, hidden_all, contract_cols, preferred_element_type=jnp.float32),
            lax.dot_general(up_weight, hidden_all, contract_cols, preferred_element_type=jnp.float32),
        ],
        axis=0,
    )
    proj_up = lax.psum_scatter(proj_up, "dp", scatter_dimension=1, tiled=True)
    cot_later, proj_up = lax.optimization_barrier((cot_all, proj_up))
    projected = proj_up[:n_proj].astype(jnp.bfloat16).reshape(3, head_slice, HEADS, ROWS)
    up_input = proj_up[n_proj:]
    activated, gelu_slope = gelu_pair(up_input)
    up_output = activated.astype(jnp.bfloat16)

    by_head = HEADS % n_mp == 0
    if by_head:
        head_group = HEADS // n_mp
        qkv_heads = lax.all_to_all(projected, "mp", split_axis=2, concat_axis=1, tiled=True)
        query_heads = qkv_heads[0].reshape(HS, head_group * QB, TQ)
        pairs = jnp.stack([qkv_heads[1], qkv_heads[2]], axis=2)
        pair_heads = jnp.broadcast_to(
            pairs[:, :, None], (HS, head_group, QB, 2, PATCHES)
        ).reshape(HS, head_group * QB, 2, PATCHES)
        attended, stored = attend(query_heads, pair_heads)
        head_rows = lax.all_to_all(
            attended.reshape(HS, head_group, ROWS), "mp", split_axis=0, concat_axis=1, tiled=True
        ).reshape(head_slice * HEADS, ROWS)
    else:
        queries = projected[0].reshape(head_slice, ITEMS, TQ)
        keyvals = to_items(projected[1:])
        query_heads, pair_heads = (
            lax.all_to_all(queries, "mp", split_axis=1, concat_axis=0, tiled=True),
            lax.all_to_all(keyvals, "mp", split_axis=1, concat_axis=0, tiled=True),
        )
        attended, stored = attend(query_heads, pair_heads)
        head_rows = lax.all_to_all(attended, "mp", split_axis=0, concat_axis=1, tiled=True).reshape(
            head_slice * HEADS, ROWS
        )
    n_att = head_rows.shape[0]
    both_all = lax.all_gather(
        jnp.concatenate([head_rows, up_output], axis=0), "dp", axis=1, tiled=True
    )
    head_rows_all, up_output_all = both_all[:n_att], both_all[n_att:]
    branch = lax.dot_general(
        head_rows_all, head_flat, contract_rows, preferred_element_type=jnp.float32
    ) + lax.dot_general(up_output_all, down_weight, contract_rows, preferred_element_type=jnp.float32)
    branch_local = gather_quarter(branch, rows)
    mixed = (widened + branch_local).astype(jnp.bfloat16)

    down_grad = blockwise_grad(up_output_all, cot_all, n_dp)
    head_grad = blockwise_grad(head_rows_all, cot_all, n_dp)
    back = jnp.concatenate(
        [
            lax.dot_general(head_flat, cot_later, contract_cols, preferred_element_type=jnp.float32),
            lax.dot_general(down_weight, cot_later, contract_cols, preferred_element_type=jnp.float32),
        ],
        axis=0,
    )
    back = lax.psum_scatter(back, "dp", scatter_dimension=1, tiled=True)
    up_upstream = (back[n_att:] * gelu_slope).astype(jnp.bfloat16)
    head_upstream = back[:n_att].astype(jnp.bfloat16).reshape(head_slice, HEADS, ROWS)
    if by_head:
        upstream = lax.all_to_all(
            head_upstream, "mp", split_axis=1, concat_axis=0, tiled=True
        ).reshape(HS, head_group * QB, TQ)
        query_grad, pair_grad = attend_back(upstream, stored)
        pair_sum = jnp.sum(
            pair_grad.reshape(HS, head_group, QB, 2, PATCHES).astype(jnp.float32), axis=2
        ).astype(jnp.bfloat16)
        grads = jnp.stack(
            [query_grad.reshape(HS, head_group, ROWS), pair_sum[:, :, 0], pair_sum[:, :, 1]]
        )
        proj_grad = lax.all_to_all(grads, "mp", split_axis=1, concat_axis=2, tiled=True)
    else:
        upstream = lax.all_to_all(
            head_upstream.reshape(head_slice, ITEMS, TQ), "mp", split_axis=1, concat_axis=0, tiled=True
        )
        query_grad, pair_grad = attend_back(upstream, stored)
        query_local, pair_local = (
            lax.all_to_all(query_grad, "mp", split_axis=0, concat_axis=1, tiled=True),
            lax.all_to_all(pair_grad, "mp", split_axis=0, concat_axis=1, tiled=True),
        )
        proj_grad = jnp.concatenate(
            [query_local.reshape(1, head_slice, HEADS, ROWS), from_items(pair_local)], axis=0
        )
    proj_grad = proj_grad.reshape(3 * head_slice * HEADS, ROWS)
    grads_all = lax.all_gather(
        jnp.concatenate([proj_grad, up_upstream], axis=0), "dp", axis=1, tiled=True
    )
    proj_grad_all, up_upstream_all = grads_all[:n_proj], grads_all[n_proj:]
    qkv_grad = blockwise_grad(proj_grad_all, hidden_all, n_dp)
    up_grad = blockwise_grad(up_upstream_all, hidden_all, n_dp)
    ratio = n_mp // n_dp
    input_pieces = jnp.concatenate(
        [
            (
                lax.dot_general(
                    proj_grad_all, qkv_flat[:, part * width:(part + 1) * width],
                    contract_rows, preferred_element_type=jnp.float32,
                )
                + lax.dot_general(
                    up_upstream_all, up_weight[:, part * width:(part + 1) * width],
                    contract_rows, preferred_element_type=jnp.float32,
                )
            ).reshape(n_dp, rows, width)
            for part in range(ratio)
        ],
        axis=0,
    )
    received = lax.all_to_all(input_pieces, "mp", split_axis=0, concat_axis=0, tiled=True)
    input_local = lax.ppermute(
        jnp.sum(received, axis=0), ("dp", "mp"), swap_by_part_pairs(n_dp, n_mp)
    )

    scaled = input_local * gain_wide
    plain_sum, cross_sum = lax.psum(
        (jnp.sum(scaled, axis=1), jnp.sum(scaled * normed, axis=1)), "mp"
    )
    tokens_grad = row_scale * (
        scaled - plain_sum[:, None] / D - normed * (cross_sum[:, None] / D)
    )
    tokens_grad = tokens_grad + cotangent.astype(jnp.float32)
    gain_piece = jnp.sum(input_local * normed, axis=0)
    gain_grad = lax.psum(gain_piece, "dp")
    return (
        mixed,
        tokens_grad,
        qkv_grad.reshape(qkv_weight.shape),
        head_grad.reshape(head_weight.shape),
        up_grad,
        down_grad,
        gain_grad,
    )


def solution(mesh):
    in_specs = (
        P("dp", "mp"),
        P("mp"),
        P(None, "mp", None, "dp"),
        P("mp", None, "dp"),
        P("mp", "dp"),
        P("mp", "dp"),
        P("dp", "mp"),
    )
    out_specs = (
        P("dp", "mp"),
        P("dp", "mp"),
        P(None, "mp", None, "dp"),
        P("mp", None, "dp"),
        P("mp", "dp"),
        P("mp", "dp"),
        P("mp"),
    )
    return jax.shard_map(shards, mesh=mesh, in_specs=in_specs, out_specs=out_specs, check_vma=False)
```

```python
import math

import jax
import jax.numpy as jnp
from jax import lax
from jax.sharding import PartitionSpec as P

D = 6144
HEADS = 24
HS = 128
PATCHES = 128
QB = 8
IMG_DP = 1
ROWS = 128
TQ = 16
ITEMS = 192


epsilon = 1e-06
contract_rows = (((0,), (0,)), ((), ()))
contract_cols = (((1,), (1,)), ((), ()))


def gelu_pair(inputs):
    normal_cdf = 0.5 * (1.0 + jax.scipy.special.erf(inputs * 0.7071067811865476))
    density = jnp.exp(-0.5 * inputs * inputs) * 0.3989422804014327
    return (inputs * normal_cdf, normal_cdf + inputs * density)


def head_norm(values):
    center = values - jnp.mean(values, axis=0, keepdims=True)
    inverse = lax.rsqrt(jnp.mean(center * center, axis=0, keepdims=True) + epsilon)
    return (center * inverse, inverse)


def norm_back(upstream, normed, inverse):
    return inverse * (
        upstream
        - jnp.mean(upstream, axis=0, keepdims=True)
        - normed * jnp.mean(upstream * normed, axis=0, keepdims=True)
    )


def to_items(pair_rows):
    depth = pair_rows.shape[1]
    shaped = pair_rows.reshape(2, depth, HEADS, IMG_DP, 1, PATCHES)
    spread = jnp.broadcast_to(shaped, (2, depth, HEADS, IMG_DP, QB, PATCHES))
    return jnp.transpose(spread, (1, 2, 3, 4, 0, 5)).reshape(depth, HEADS * IMG_DP * QB, 2, PATCHES)


def from_items(pair_items):
    depth = pair_items.shape[0]
    shaped = pair_items.reshape(depth, HEADS, IMG_DP, QB, 2, PATCHES)
    summed = jnp.sum(shaped.astype(jnp.float32), axis=3).astype(jnp.bfloat16)
    return jnp.transpose(summed, (3, 0, 1, 2, 4)).reshape(2, depth, HEADS, IMG_DP * PATCHES)


def attend(queries, keyvals):
    query_hat, query_scale = head_norm(queries.astype(jnp.float32))
    key_hat, key_scale = head_norm(keyvals[:, :, 0].astype(jnp.float32))
    query_norm = query_hat.astype(jnp.bfloat16)
    key_norm = key_hat.astype(jnp.bfloat16)
    factor = 1.0 / math.sqrt(queries.shape[0])
    scores = (
        jnp.einsum("cia,cib->iab", query_norm, key_norm, preferred_element_type=jnp.float32)
        * factor
    )
    raised = jnp.exp(scores)
    shares = raised / jnp.sum(raised, axis=2, keepdims=True)
    rounded = shares.astype(jnp.bfloat16)
    values = keyvals[:, :, 1]
    attended = jnp.einsum(
        "iab,cib->cia", rounded, values, preferred_element_type=jnp.float32
    ).astype(jnp.bfloat16)
    stored = (
        query_hat,
        query_scale,
        key_hat,
        key_scale,
        query_norm,
        key_norm,
        shares,
        rounded,
        values,
    )
    return (attended, stored)


def attend_back(upstream, stored):
    query_hat, query_scale, key_hat, key_scale, query_norm, key_norm, shares, rounded, values = (
        stored
    )
    factor = 1.0 / math.sqrt(upstream.shape[0])
    share_grad = jnp.einsum("cia,cib->iab", upstream, values, preferred_element_type=jnp.float32)
    value_grad = jnp.einsum("iab,cia->cib", rounded, upstream, preferred_element_type=jnp.float32)
    score_grad = (
        shares * (share_grad - jnp.sum(shares * share_grad, axis=2, keepdims=True)) * factor
    ).astype(jnp.bfloat16)
    query_back = jnp.einsum(
        "iab,cib->cia", score_grad, key_norm, preferred_element_type=jnp.float32
    )
    key_back = jnp.einsum(
        "iab,cia->cib", score_grad, query_norm, preferred_element_type=jnp.float32
    )
    query_grad = norm_back(query_back, query_hat, query_scale).astype(jnp.bfloat16)
    key_grad = norm_back(key_back, key_hat, key_scale).astype(jnp.bfloat16)
    pair_grad = jnp.stack([key_grad, value_grad.astype(jnp.bfloat16)], axis=2)
    return (query_grad, pair_grad)


def swap_pairs(n_dp, n_mp):
    ratio = n_mp // n_dp
    pairs = []
    for row in range(n_dp):
        for col in range(n_mp):
            owner, part = divmod(col, ratio)
            pairs.append((row * n_mp + col, owner * n_mp + row * ratio + part))
    return pairs


def swap_by_part_pairs(n_dp, n_mp):
    ratio = n_mp // n_dp
    pairs = []
    for row in range(n_dp):
        for col in range(n_mp):
            part, owner = divmod(col, n_dp)
            pairs.append((row * n_mp + col, owner * n_mp + row * ratio + part))
    return pairs


def swap(block):
    n_dp, n_mp = lax.axis_size("dp"), lax.axis_size("mp")
    return lax.ppermute(block, ("dp", "mp"), swap_pairs(n_dp, n_mp))


def spread_quarter(block):
    n_dp, n_mp = lax.axis_size("dp"), lax.axis_size("mp")
    ratio = n_mp // n_dp
    rows, width = block.shape
    copies = jnp.broadcast_to(swap(block)[None], (n_mp, rows, width))
    pieces = lax.all_to_all(copies, "mp", split_axis=0, concat_axis=0, tiled=True)
    pieces = pieces.reshape(n_dp, ratio, rows, width)
    return jnp.transpose(pieces, (0, 2, 1, 3)).reshape(n_dp * rows, ratio * width)


def spread_quarter_rows(block):
    n_dp, n_mp = lax.axis_size("dp"), lax.axis_size("mp")
    ratio = n_mp // n_dp
    rows, width = block.shape
    copies = jnp.broadcast_to(swap(block)[None], (n_mp, rows, width))
    pieces = lax.all_to_all(copies, "mp", split_axis=0, concat_axis=0, tiled=True)
    pieces = pieces.reshape(n_dp, ratio, rows, width)
    return jnp.transpose(pieces, (0, 2, 1, 3)).reshape(n_dp, rows, ratio * width)


def gather_quarter(partial, rows):
    n_dp, n_mp = lax.axis_size("dp"), lax.axis_size("mp")
    ratio = n_mp // n_dp
    width = partial.shape[1] // ratio
    pieces = partial.reshape(n_dp, rows, ratio, width)
    pieces = jnp.transpose(pieces, (0, 2, 1, 3)).reshape(n_mp, rows, width)
    summed = lax.psum_scatter(pieces, "mp", scatter_dimension=0, tiled=True)
    return swap(summed.reshape(rows, width))


def gather_quarter_exchange(partial, rows):
    n_dp, n_mp = lax.axis_size("dp"), lax.axis_size("mp")
    ratio = n_mp // n_dp
    width = partial.shape[1] // ratio
    pieces = partial.reshape(n_dp, rows, ratio, width)
    pieces = jnp.transpose(pieces, (0, 2, 1, 3)).reshape(n_mp, rows, width)
    received = lax.all_to_all(pieces, "mp", split_axis=0, concat_axis=0, tiled=True)
    return swap(jnp.sum(received, axis=0))


def blockwise_grad(left, right, n_blocks):
    rows = left.shape[1] // n_blocks
    total = None
    for block in range(n_blocks):
        piece = jnp.dot(
            left[:, block * rows:(block + 1) * rows],
            right[block * rows:(block + 1) * rows],
            preferred_element_type=jnp.float32,
        ).astype(jnp.bfloat16).astype(jnp.float32)
        total = piece if total is None else total + piece
    return total.astype(jnp.bfloat16)


def shards(tokens, norm_gain, qkv_weight, head_weight, up_weight, down_weight, cotangent):
    n_dp, n_mp = lax.axis_size("dp"), lax.axis_size("mp")
    head_slice = HS // n_mp
    quarter = qkv_weight.shape[-1]
    rows, width = tokens.shape
    qkv_flat = qkv_weight.reshape(-1, quarter)
    head_flat = head_weight.reshape(-1, quarter)

    widened = tokens.astype(jnp.float32)
    gain_wide = norm_gain.astype(jnp.float32)
    with_gain = jnp.concatenate([tokens, norm_gain.reshape(1, width)], axis=0)
    spread_in = spread_quarter_rows(with_gain)
    tokens_all = spread_in[:, :rows].reshape(-1, quarter).astype(jnp.float32)
    gain_quarter = spread_in[0, rows].astype(jnp.float32)
    part_mean = jnp.mean(tokens_all, axis=1)
    part_center = tokens_all - part_mean[:, None]
    part_m2 = jnp.sum(part_center * part_center, axis=1)
    parts = lax.all_gather(jnp.stack([part_mean, part_m2]), "dp", axis=0, tiled=False)
    mean_all = jnp.mean(parts[:, 0], axis=0)
    spread = parts[:, 0] - mean_all[None, :]
    m2_all = jnp.sum(parts[:, 1], axis=0) + quarter * jnp.sum(spread * spread, axis=0)
    scale_all = lax.rsqrt(m2_all / D + epsilon)
    hidden_all = (
        ((tokens_all - mean_all[:, None]) * scale_all[:, None]) * gain_quarter
    ).astype(jnp.bfloat16)
    me = lax.axis_index("dp")
    row_mean = lax.dynamic_slice_in_dim(mean_all, me * rows, rows)[:, None]
    row_scale = lax.dynamic_slice_in_dim(scale_all, me * rows, rows)[:, None]
    normed = (widened - row_mean) * row_scale
    cot_all = spread_quarter(cotangent)

    n_proj = qkv_flat.shape[0]
    proj_up = jnp.concatenate(
        [
            lax.dot_general(qkv_flat, hidden_all, contract_cols, preferred_element_type=jnp.float32),
            lax.dot_general(up_weight, hidden_all, contract_cols, preferred_element_type=jnp.float32),
        ],
        axis=0,
    )
    proj_up = lax.psum_scatter(proj_up, "dp", scatter_dimension=1, tiled=True)
    cot_later, proj_up = lax.optimization_barrier((cot_all, proj_up))
    projected = proj_up[:n_proj].astype(jnp.bfloat16).reshape(3, head_slice, HEADS, ROWS)
    up_input = proj_up[n_proj:]
    activated, gelu_slope = gelu_pair(up_input)
    up_output = activated.astype(jnp.bfloat16)

    by_head = HEADS % n_mp == 0
    if by_head:
        head_group = HEADS // n_mp
        qkv_heads = lax.all_to_all(projected, "mp", split_axis=2, concat_axis=1, tiled=True)
        query_heads = qkv_heads[0].reshape(HS, head_group * QB, TQ)
        pairs = jnp.stack([qkv_heads[1], qkv_heads[2]], axis=2)
        pair_heads = jnp.broadcast_to(
            pairs[:, :, None], (HS, head_group, QB, 2, PATCHES)
        ).reshape(HS, head_group * QB, 2, PATCHES)
        attended, stored = attend(query_heads, pair_heads)
        head_rows = lax.all_to_all(
            attended.reshape(HS, head_group, ROWS), "mp", split_axis=0, concat_axis=1, tiled=True
        ).reshape(head_slice * HEADS, ROWS)
    else:
        queries = projected[0].reshape(head_slice, ITEMS, TQ)
        keyvals = to_items(projected[1:])
        query_heads, pair_heads = (
            lax.all_to_all(queries, "mp", split_axis=1, concat_axis=0, tiled=True),
            lax.all_to_all(keyvals, "mp", split_axis=1, concat_axis=0, tiled=True),
        )
        attended, stored = attend(query_heads, pair_heads)
        head_rows = lax.all_to_all(attended, "mp", split_axis=0, concat_axis=1, tiled=True).reshape(
            head_slice * HEADS, ROWS
        )
    n_att = head_rows.shape[0]
    both_all = lax.all_gather(
        jnp.concatenate([head_rows, up_output], axis=0), "dp", axis=1, tiled=True
    )
    head_rows_all, up_output_all = both_all[:n_att], both_all[n_att:]
    branch_pieces = jnp.concatenate(
        [
            (
                lax.dot_general(
                    head_rows_all, head_flat[:, part * width:(part + 1) * width],
                    contract_rows, preferred_element_type=jnp.float32,
                )
                + lax.dot_general(
                    up_output_all, down_weight[:, part * width:(part + 1) * width],
                    contract_rows, preferred_element_type=jnp.float32,
                )
            ).reshape(n_dp, rows, width)
            for part in range(n_mp // n_dp)
        ],
        axis=0,
    )
    branch_summed = lax.psum_scatter(branch_pieces, "mp", scatter_dimension=0, tiled=True)
    branch_local = lax.ppermute(
        branch_summed.reshape(rows, width), ("dp", "mp"), swap_by_part_pairs(n_dp, n_mp)
    )
    mixed = (widened + branch_local).astype(jnp.bfloat16)

    down_grad = blockwise_grad(up_output_all, cot_all, n_dp)
    head_grad = blockwise_grad(head_rows_all, cot_all, n_dp)
    back = jnp.concatenate(
        [
            lax.dot_general(head_flat, cot_later, contract_cols, preferred_element_type=jnp.float32),
            lax.dot_general(down_weight, cot_later, contract_cols, preferred_element_type=jnp.float32),
        ],
        axis=0,
    )
    back = lax.psum_scatter(back, "dp", scatter_dimension=1, tiled=True)
    up_upstream = (back[n_att:] * gelu_slope).astype(jnp.bfloat16)
    head_upstream = back[:n_att].astype(jnp.bfloat16).reshape(head_slice, HEADS, ROWS)
    if by_head:
        upstream = lax.all_to_all(
            head_upstream, "mp", split_axis=1, concat_axis=0, tiled=True
        ).reshape(HS, head_group * QB, TQ)
        query_grad, pair_grad = attend_back(upstream, stored)
        pair_sum = jnp.sum(
            pair_grad.reshape(HS, head_group, QB, 2, PATCHES).astype(jnp.float32), axis=2
        ).astype(jnp.bfloat16)
        grads = jnp.stack(
            [query_grad.reshape(HS, head_group, ROWS), pair_sum[:, :, 0], pair_sum[:, :, 1]]
        )
        proj_grad = lax.all_to_all(grads, "mp", split_axis=1, concat_axis=2, tiled=True)
    else:
        upstream = lax.all_to_all(
            head_upstream.reshape(head_slice, ITEMS, TQ), "mp", split_axis=1, concat_axis=0, tiled=True
        )
        query_grad, pair_grad = attend_back(upstream, stored)
        query_local, pair_local = (
            lax.all_to_all(query_grad, "mp", split_axis=0, concat_axis=1, tiled=True),
            lax.all_to_all(pair_grad, "mp", split_axis=0, concat_axis=1, tiled=True),
        )
        proj_grad = jnp.concatenate(
            [query_local.reshape(1, head_slice, HEADS, ROWS), from_items(pair_local)], axis=0
        )
    proj_grad = proj_grad.reshape(3 * head_slice * HEADS, ROWS)
    grads_all = lax.all_gather(
        jnp.concatenate([proj_grad, up_upstream], axis=0), "dp", axis=1, tiled=True
    )
    proj_grad_all, up_upstream_all = grads_all[:n_proj], grads_all[n_proj:]
    qkv_grad = blockwise_grad(proj_grad_all, hidden_all, n_dp)
    up_grad = blockwise_grad(up_upstream_all, hidden_all, n_dp)
    ratio = n_mp // n_dp
    input_pieces = jnp.concatenate(
        [
            (
                lax.dot_general(
                    proj_grad_all, qkv_flat[:, part * width:(part + 1) * width],
                    contract_rows, preferred_element_type=jnp.float32,
                )
                + lax.dot_general(
                    up_upstream_all, up_weight[:, part * width:(part + 1) * width],
                    contract_rows, preferred_element_type=jnp.float32,
                )
            ).reshape(n_dp, rows, width)
            for part in range(ratio)
        ],
        axis=0,
    )
    received = lax.all_to_all(input_pieces, "mp", split_axis=0, concat_axis=0, tiled=True)
    input_local = lax.ppermute(
        jnp.sum(received, axis=0), ("dp", "mp"), swap_by_part_pairs(n_dp, n_mp)
    )

    scaled = input_local * gain_wide
    plain_sum, cross_sum = lax.psum(
        (jnp.sum(scaled, axis=1), jnp.sum(scaled * normed, axis=1)), "mp"
    )
    tokens_grad = row_scale * (
        scaled - plain_sum[:, None] / D - normed * (cross_sum[:, None] / D)
    )
    tokens_grad = tokens_grad + cotangent.astype(jnp.float32)
    gain_piece = jnp.sum(input_local * normed, axis=0)
    gain_grad = lax.psum(gain_piece, "dp")
    return (
        mixed,
        tokens_grad,
        qkv_grad.reshape(qkv_weight.shape),
        head_grad.reshape(head_weight.shape),
        up_grad,
        down_grad,
        gain_grad,
    )


def solution(mesh):
    in_specs = (
        P("dp", "mp"),
        P("mp"),
        P(None, "mp", None, "dp"),
        P("mp", None, "dp"),
        P("mp", "dp"),
        P("mp", "dp"),
        P("dp", "mp"),
    )
    out_specs = (
        P("dp", "mp"),
        P("dp", "mp"),
        P(None, "mp", None, "dp"),
        P("mp", None, "dp"),
        P("mp", "dp"),
        P("mp", "dp"),
        P("mp"),
    )
    return jax.shard_map(shards, mesh=mesh, in_specs=in_specs, out_specs=out_specs, check_vma=False)
```
